256 devices in a mesh: blk: 16 (over x_lo, y, core), exp: 16 (over z, x_hi).
Axes of the slice: x: 4 (x_hi: 2, x_lo: 2; x = x_hi * 2 + x_lo), y: 4, z: 8, core: 2. Of those that a mesh axis runs over, the one named last changes fastest.
Arguments:
- hidden: bfloat16 [4096, 2560], P('exp', 'blk'), may hold values from -6 to 6
- attn_gain: float32 [2560], replicated, may hold values from 0.25 to 1.75
- qkv_weight: bfloat16 [2560, 3584], P(None, 'blk'), may hold values from -0.125 to 0.125
- out_weight: bfloat16 [2560, 2560], P(None, 'blk'), may hold values from -0.125 to 0.125
- kv_pool: bfloat16 [16, 64, 128, 1024], P('exp', 'blk'), may hold values from -64 to 64
- page_table: int32 [16, 64], P('exp'), may hold values from 0 to 63, each once within a row
- cache_lens: int32 [16], P('exp'), may hold values from 1 to 7936, as said below
- ffn_gain: float32 [2560], replicated, may hold values from 0.25 to 1.75
- route_ids: int32 [4096, 6], P('exp'), may hold values from 0 to 63, all different within a row; in each aligned block of 256 rows (0 to 255, 256 to 511, ...) at most 32 rows name the same one
- route_weights: float32 [4096, 6], P('exp'), may hold values from 0.05 to 2
- shared_gate_up: bfloat16 [2560, 2, 3072], P(None, None, 'blk'), may hold values from -0.125 to 0.125
- shared_down: bfloat16 [3072, 2560], P('blk'), may hold values from -0.109375 to 0.109375
- expert_gate_up: bfloat16 [256, 2560, 768], P(('blk', 'exp')), may hold values from -0.125 to 0.125
- expert_down: bfloat16 [256, 384, 2560], P(('blk', 'exp')), may hold values from -0.3125 to 0.3125
Outputs:
- hidden_out: bfloat16 [4096, 2560], P('exp', 'blk')
- kv_pool_out: bfloat16 [16, 64, 128, 1024], P('exp', 'blk')
The draws below stay inside these ranges and needn't reach their ends.
Inputs may be any that keep to these rules, and one draw needn't show every extreme that they name: `route_ids`: among the 256 tokens of one request at most 32 choose any one expert, and some expert is chosen by exactly 32 of them; a token's 6 experts differ. `page_table`: each row names every page of the request's pool once. `cache_lens`: some request has exactly 7936 cached tokens.
All inputs are finite; a program needn't handle non-finite values.
Results may differ from the reference program's by a relative error of at most 0.02.
The reference program's roundings to bfloat16 on the way count: a program that leaves them out, or rounds other values in their place, can miss the bound.
Values may be sent and summed in bfloat16 or wider, within the bound.
No kernel may reach another device: no remote copies, remote signals or barrier semaphores. Data moves between devices by JAX's collectives and lax.ppermute only.
A program may use at most 256 MiB of HBM per device.

```python
import math
import jax
import jax.numpy as jnp
import numpy as np
from jax import lax

D = 2560
HEADS = 20
KV_HEADS = 4
HEAD_DIM = 128
TOPK = 6
FF_SHARED = 3072
SPLIT = 4
PAGE = 128
NEW = 256
EXPERTS = 64
REQUESTS = 16
TOKENS = 4096
POOL = 64
CMAX = 7936
CAP = 32
QKV_W = 3584
FF_PART = 384
N_EXP = 16


def draw_cache_lens(key, part):
    first_key, second_key = jax.random.split(key)
    lengths = jax.random.randint(first_key, (REQUESTS,), 1, CMAX + 1)
    longest = jax.random.randint(second_key, (), 0, REQUESTS)
    return jnp.where(jnp.arange(REQUESTS) == longest, CMAX, lengths).astype(jnp.int32)


def draw_kv_pool(key, part):
    shape = (REQUESTS, POOL, PAGE, 2 * KV_HEADS * HEAD_DIM)
    first_key = jax.random.fold_in(jax.random.fold_in(key, 11), 0)
    values = jax.random.normal(first_key, shape, jnp.float32)
    return jnp.clip(values, -64.0, 64.0).astype(jnp.bfloat16)


def level_of(rng, dims, pieces, least, high):
    gain = 1.0
    for dim, parts in pieces:
        draws = jax.random.uniform(jax.random.fold_in(jax.random.fold_in(rng, 6), dim), (parts,), jnp.float32, least / len(pieces), high / len(pieces))
        gain = gain * jnp.repeat(jnp.exp(draws), dims[dim] // parts).reshape((-1,) + (1,) * (len(dims) - 1 - dim))
    return gain


def assign_block(key, own, number, rows, count, top, bound, lean):
    order = jax.random.permutation(key, count)
    heavy_load, usual = portions_of(count, rows * top, bound, lean, True), portions_of(count, rows * top, bound, lean, False)
    places = jnp.arange(count)

    def named(tallies, offset_by):
        used = int((tallies > 0).sum())
        fixed = max(1, used // 4)
        passed = fixed + (places - fixed + offset_by * (used - fixed)) % max(1, count - fixed)
        return jnp.zeros((count,), jnp.int32).at[order[jnp.where(places < fixed, places, passed)]].set(jnp.asarray(tallies, jnp.int32))

    tallies = jnp.where(number % 4 == 0, named(heavy_load, number // 4), named(usual, number - number // 4 - 1))
    mixed = jax.random.permutation(jax.random.fold_in(own, 3), count)
    giver, sink = mixed[0:count // 2 * 2:2], mixed[1:count // 2 * 2:2]
    slack = jnp.minimum(tallies[giver] - 1, bound - tallies[sink]) // 2
    slack = jnp.where((giver == order[0]) | (sink == order[0]) | (tallies[sink] == 0), 0, jnp.maximum(slack, 0))
    passed = jax.random.randint(jax.random.fold_in(own, 4), (count // 2,), 0, 1 << 20) % (slack + 1)
    tallies = tallies.at[giver].add(-passed).at[sink].add(passed)
    labels = jnp.searchsorted(jnp.cumsum(tallies), jnp.arange(rows * top), side="right").astype(jnp.int32)
    grid = labels.reshape(top, rows).T
    grid = grid[jax.random.permutation(jax.random.fold_in(own, 1), rows)]
    offset_by = jax.random.randint(jax.random.fold_in(own, 2), (rows, 1), 0, top)
    return jnp.take_along_axis(grid, (jnp.arange(top)[None, :] + offset_by) % top, axis=1)


def portions_of(number_of, total, reach, slope, full):
    portions = [(1 << 20) // math.isqrt(rank ** slope) + 1 for rank in range(1, number_of + 1)]
    largest = reach if full else min(reach, max(-(-total // number_of), total * portions[0] // sum(portions)))
    least = 1 if total - largest >= number_of - 1 else 0
    counts, surplus = [largest] + [least] * (number_of - 1), total - largest - least * (number_of - 1)
    while surplus > 0:
        free = [i for i in range(1, number_of) if counts[i] < largest] or [i for i in range(1, number_of) if counts[i] < reach]
        whole, budget = sum([portions[i] for i in free]), surplus
        for i in free:
            addition = min(reach - counts[i], max(1, budget * portions[i] // whole), surplus)
            counts[i] = counts[i] + addition
            surplus = surplus - addition
    return np.array(counts)


def centred(rng, extent, spread, reach, cuts=(), dtype=jnp.bfloat16):
    values = spread * jax.random.normal(rng, extent, jnp.float32)
    if cuts:
        values = values * level_of(rng, extent, cuts, -0.22, 0.18)
    return jnp.clip(values, -reach, reach).astype(dtype)


def setup_inputs(seed: int = 0) -> dict:
    splits = jax.random.split(jax.random.key(seed), 15)
    hidden = centred(splits[0], (TOKENS, D), 1.0, 6.0, ((0, 16), (1, 16)))
    attn_gain = jnp.clip(1.0 + 0.15 * jax.random.normal(splits[1], (D,), jnp.float32), 0.25, 1.75)
    qkv_weight = centred(splits[2], (D, QKV_W), D ** -0.5, 0.125, ((1, 16),))
    out_weight = centred(splits[3], (D, D), D ** -0.5, 0.125, ((1, 16),))
    kv_pool = draw_kv_pool(jax.random.fold_in(splits[14], 71), 0)
    page_table = jax.vmap(lambda own: jax.random.permutation(own, POOL))(jax.random.split(splits[5], REQUESTS)).reshape((REQUESTS, POOL)).astype(jnp.int32)
    cache_lens = draw_cache_lens(jax.random.fold_in(splits[14], 71), 0)
    ffn_gain = jnp.clip(1.0 + 0.15 * jax.random.normal(splits[7], (D,), jnp.float32), 0.25, 1.75)
    route_ids_keys = jax.random.split(jax.random.fold_in(splits[8], 1), TOKENS // NEW)
    route_ids_turns = jax.random.permutation(jax.random.fold_in(splits[8], 3), TOKENS // NEW)
    route_ids = jax.vmap(lambda own, number: assign_block(jax.random.fold_in(splits[8], 2), own, number, NEW, EXPERTS, TOPK, CAP, 1))(route_ids_keys, route_ids_turns).reshape((TOKENS, TOPK))
    route_weights = jnp.clip(jnp.exp(math.log(2.0) - 3.6888794 * jax.random.uniform(splits[9], (TOKENS, TOPK), jnp.float32) ** level_of(splits[9], (TOKENS, TOPK), ((0, 16),), -0.2, 0.2)), 0.05, 2.0)
    shared_gate_up = centred(splits[10], (D, 2, FF_SHARED), D ** -0.5, 0.125, ((2, 16),))
    shared_down = centred(splits[11], (FF_SHARED, D), FF_SHARED ** -0.5, 0.109375, ((0, 16),))
    expert_gate_up = centred(splits[12], (EXPERTS * SPLIT, D, 2 * FF_PART), D ** -0.5, 0.125, ((0, 256),))
    expert_down = centred(splits[13], (EXPERTS * SPLIT, FF_PART, D), FF_PART ** -0.5, 0.3125, ((0, 256),))
    return dict(hidden=hidden, attn_gain=attn_gain, qkv_weight=qkv_weight, out_weight=out_weight, kv_pool=kv_pool, page_table=page_table, cache_lens=cache_lens, ffn_gain=ffn_gain, route_ids=route_ids, route_weights=route_weights, shared_gate_up=shared_gate_up, shared_down=shared_down, expert_gate_up=expert_gate_up, expert_down=expert_down)


rope_base = 500000.0
norm_eps = 1e-05

def normalize(inputs, gain_vec):
    values = inputs.astype(jnp.float32)
    inv_rms = lax.rsqrt(lax.optimization_barrier(jnp.mean(values * values, axis=-1, keepdims=True)) + norm_eps)
    return (values * inv_rms * gain_vec).astype(jnp.bfloat16)

def rotate(inputs, positions):
    half_dim = HEAD_DIM // 2
    frequency = rope_base ** (-(jnp.arange(half_dim).astype(jnp.float32) * 2.0 / HEAD_DIM))
    angles = positions.astype(jnp.float32)[:, None] * frequency[None, :]
    cosine = jnp.cos(angles)[:, None, :]
    sine_vals = jnp.sin(angles)[:, None, :]
    lower_half = inputs[..., :half_dim]
    upper_half = inputs[..., half_dim:]
    return jnp.concatenate([lower_half * cosine - upper_half * sine_vals, upper_half * cosine + lower_half * sine_vals], axis=-1)

def attend_request(request_item, attn_gain, qkv_weight):
    row_block, page_pool, page_map, length = request_item
    query_width = HEADS * HEAD_DIM
    key_width = KV_HEADS * HEAD_DIM
    group_size = HEADS // KV_HEADS
    attn_in = normalize(row_block, attn_gain)
    projected_all = jnp.dot(attn_in, qkv_weight, preferred_element_type=jnp.float32).astype(jnp.bfloat16)
    positions = length + jnp.arange(NEW).astype(jnp.int32)
    queries = rotate(projected_all[:, :query_width].astype(jnp.float32).reshape(NEW, HEADS, HEAD_DIM), positions).astype(jnp.bfloat16)
    new_keys = rotate(projected_all[:, query_width:query_width + key_width].astype(jnp.float32).reshape(NEW, KV_HEADS, HEAD_DIM), positions).astype(jnp.bfloat16)
    appended = jnp.concatenate([new_keys.reshape(NEW, key_width), projected_all[:, query_width + key_width:]], axis=1)
    page_total = page_map.shape[0]
    page_index = jnp.arange(page_total).astype(jnp.int32)
    logical = lax.optimization_barrier(jnp.sum(jnp.where(page_map[None, :] == page_index[:, None], page_index[None, :], 0), axis=1)).astype(jnp.int32)
    slot_pos = logical[:, None] * PAGE + jnp.arange(PAGE).astype(jnp.int32)[None, :]
    offset = slot_pos - length
    written = (offset >= 0) & (offset < NEW)
    picked = appended[jnp.clip(offset, 0, NEW - 1)]
    pool_out = jnp.where(written[:, :, None], picked, page_pool)
    slot_rows = pool_out.reshape(page_total * PAGE, 2 * key_width)
    key_all = slot_rows[:, :key_width].reshape(-1, KV_HEADS, HEAD_DIM).astype(jnp.float32)
    val_all = slot_rows[:, key_width:].reshape(-1, KV_HEADS, HEAD_DIM).astype(jnp.float32)
    grouped = queries.reshape(NEW, KV_HEADS, group_size, HEAD_DIM).astype(jnp.float32)
    scores = jnp.einsum('tkgd,skd->tkgs', grouped, key_all) * (1.0 / math.sqrt(HEAD_DIM))
    allowed = (slot_pos.reshape(-1)[None, :] <= positions[:, None])[:, None, None, :]
    maxima = lax.optimization_barrier(jnp.max(jnp.where(allowed, scores, -1e+30), axis=-1, keepdims=True))
    weights = jnp.where(allowed, jnp.exp(scores - maxima), 0.0)
    totals = lax.optimization_barrier(jnp.sum(weights, axis=-1))
    probs_low = lax.optimization_barrier(weights.astype(jnp.bfloat16))
    weighted = jnp.einsum('tkgs,skd->tkgd', probs_low.astype(jnp.float32), val_all, precision=lax.Precision.HIGHEST)
    attention = (weighted / totals[..., None]).reshape(NEW, query_width).astype(jnp.bfloat16)
    return (attention, pool_out)

def reference(hidden, attn_gain, qkv_weight, out_weight, kv_pool, page_table, cache_lens, ffn_gain, route_ids, route_weights, shared_gate_up, shared_down, expert_gate_up, expert_down):
    row_blocks = hidden.reshape(REQUESTS, NEW, D)
    attention, pool_out = lax.map(lambda request_item: attend_request(request_item, attn_gain, qkv_weight), (row_blocks, kv_pool, page_table, cache_lens))
    attention = attention.reshape(TOKENS, D)
    mixed_rows = (hidden.astype(jnp.float32) + jnp.dot(attention, out_weight, preferred_element_type=jnp.float32)).astype(jnp.bfloat16)
    ffn_in = normalize(mixed_rows, ffn_gain)
    gate_up = jnp.dot(ffn_in, shared_gate_up.reshape(D, 2 * FF_SHARED), preferred_element_type=jnp.float32)
    shared_act = (jax.nn.silu(gate_up[:, :FF_SHARED]) * gate_up[:, FF_SHARED:]).astype(jnp.bfloat16)
    running_sum = mixed_rows.astype(jnp.float32) + jnp.dot(shared_act, shared_down, preferred_element_type=jnp.float32)
    row_limit = N_EXP * CAP
    token_index = jnp.arange(TOKENS).astype(jnp.int32)

    def one_expert(running, expert):
        route_hits = route_ids == expert
        chosen = jnp.any(route_hits, axis=1)
        weight = lax.optimization_barrier(jnp.sum(jnp.where(route_hits, route_weights, 0.0), axis=1))
        sort_keys = jnp.where(chosen, token_index, TOKENS + token_index).astype(jnp.int32)
        picked_rows = jnp.argsort(sort_keys)[:row_limit].astype(jnp.int32)
        rows_in = ffn_in[picked_rows]
        is_valid = chosen[picked_rows]
        part_weights = lax.dynamic_slice_in_dim(expert_gate_up, expert * SPLIT, SPLIT, 0)
        part_downs = lax.dynamic_slice_in_dim(expert_down, expert * SPLIT, SPLIT, 0)
        summed = jnp.zeros((row_limit, D), jnp.float32)
        for part_index in range(SPLIT):
            expert_gu = jnp.dot(rows_in, part_weights[part_index], preferred_element_type=jnp.float32)
            expert_act = (jax.nn.silu(expert_gu[:, :FF_PART]) * expert_gu[:, FF_PART:]).astype(jnp.bfloat16)
            expert_part = jnp.dot(expert_act, part_downs[part_index], preferred_element_type=jnp.float32).astype(jnp.bfloat16)
            summed = summed + expert_part.astype(jnp.float32)
        contrib = summed * jnp.where(is_valid, weight[picked_rows], 0.0)[:, None]
        return (running.at[picked_rows].add(contrib), None)
    routed, _ = lax.scan(one_expert, jnp.zeros((TOKENS, D), jnp.float32), jnp.arange(EXPERTS).astype(jnp.int32))
    hidden_out = (running_sum + routed).astype(jnp.bfloat16)
    return (hidden_out, pool_out)
```

```python
import math

import jax
import jax.numpy as jnp
from jax import lax
from jax.sharding import PartitionSpec as P

HEADS = 20
KV_HEADS = 4
HEAD_DIM = 128
TOPK = 6
SPLIT = 4
PAGE = 128
NEW = 256
FF_PART = 384


rope_base = 500000.0
norm_eps = 1e-05


def normalize(inputs, gain_vec):
    values = inputs.astype(jnp.float32)
    inv_rms = lax.rsqrt(jnp.mean(values * values, axis=-1, keepdims=True) + norm_eps)
    return (values * inv_rms * gain_vec).astype(jnp.bfloat16)


def rotate(inputs, positions):
    half_dim = HEAD_DIM // 2
    frequency = rope_base ** (-(jnp.arange(half_dim).astype(jnp.float32) * 2.0 / HEAD_DIM))
    angles = positions.astype(jnp.float32)[:, None] * frequency[None, :]
    cosine = jnp.cos(angles)[:, None, :]
    sine_vals = jnp.sin(angles)[:, None, :]
    lower_half = inputs[..., :half_dim]
    upper_half = inputs[..., half_dim:]
    return jnp.concatenate(
        [
            lower_half * cosine - upper_half * sine_vals,
            upper_half * cosine + lower_half * sine_vals,
        ],
        axis=-1,
    )


def partial_softmax(queries, query_pos, block_rows, key_pos):
    key_width = KV_HEADS * HEAD_DIM
    key_rows = block_rows[:, :key_width].reshape(-1, KV_HEADS, HEAD_DIM)
    value_rows = block_rows[:, key_width:].reshape(-1, KV_HEADS, HEAD_DIM)
    scores = jnp.einsum("tkgd,skd->tkgs", queries, key_rows, preferred_element_type=jnp.float32) * (
        1.0 / math.sqrt(HEAD_DIM)
    )
    allowed = (key_pos[None, :] <= query_pos[:, None])[:, None, None, :]
    maxima = jnp.max(jnp.where(allowed, scores, -1e30), axis=-1)
    weights = jnp.where(allowed, jnp.exp(scores - maxima[..., None]), 0.0)
    totals = jnp.sum(weights, axis=-1)
    weighted = jnp.einsum(
        "tkgs,skd->tkgd",
        weights.astype(jnp.bfloat16),
        value_rows,
        preferred_element_type=jnp.float32,
    )
    return (maxima, totals, weighted)


def per_device(
    hidden,
    attn_gain,
    qkv_weight,
    out_weight,
    kv_pool,
    page_table,
    cache_lens,
    ffn_gain,
    route_ids,
    route_weights,
    shared_gate_up,
    shared_down,
    expert_gate_up,
    expert_down,
):
    blocks = lax.axis_size("blk")
    groups = lax.axis_size("exp")
    block_index = lax.axis_index("blk")
    model_width = hidden.shape[1] * blocks
    query_width = HEADS * HEAD_DIM
    key_width = KV_HEADS * HEAD_DIM
    group_size = HEADS // KV_HEADS
    own_rows = NEW // blocks
    full_rows = lax.all_gather(hidden, "blk", axis=1, tiled=True)
    attn_in = normalize(full_rows, attn_gain)
    projected = jnp.dot(attn_in, qkv_weight, preferred_element_type=jnp.float32).astype(
        jnp.bfloat16
    )
    projected_all = lax.all_gather(projected, "blk", axis=1, tiled=True)
    length = cache_lens[0]
    positions = length + jnp.arange(NEW, dtype=jnp.int32)
    queries = rotate(
        projected_all[:, :query_width].astype(jnp.float32).reshape(NEW, HEADS, HEAD_DIM), positions
    ).astype(jnp.bfloat16)
    fresh_keys = rotate(
        projected_all[:, query_width : query_width + key_width]
        .astype(jnp.float32)
        .reshape(NEW, KV_HEADS, HEAD_DIM),
        positions,
    ).astype(jnp.bfloat16)
    appended = jnp.concatenate(
        [fresh_keys.reshape(NEW, key_width), projected_all[:, query_width + key_width :]], axis=1
    )
    page_map = page_table[0]
    pool_pages = page_map.shape[0]
    page_index = jnp.arange(pool_pages, dtype=jnp.int32)
    logical = jnp.sum(
        jnp.where(page_map[None, :] == page_index[:, None], page_index[None, :], 0), axis=1
    )
    local_pages = kv_pool.shape[1]
    local_logical = lax.dynamic_slice_in_dim(logical, block_index * local_pages, local_pages)
    slot_offsets = jnp.arange(PAGE, dtype=jnp.int32)
    local_pos = local_logical[:, None] * PAGE + slot_offsets[None, :]
    offset = local_pos - length
    written = (offset >= 0) & (offset < NEW)
    picked = appended[jnp.clip(offset, 0, NEW - 1)]
    pool_out = jnp.where(written[:, :, None], picked, kv_pool[0])
    grouped = queries.reshape(NEW, KV_HEADS, group_size, HEAD_DIM)
    slot_rows = pool_out.reshape(local_pages * PAGE, 2 * key_width)
    maxima, totals, weighted = partial_softmax(grouped, positions, slot_rows, local_pos.reshape(-1))
    payload = jnp.concatenate(
        [
            weighted.reshape(NEW, query_width),
            maxima.reshape(NEW, HEADS),
            totals.reshape(NEW, HEADS),
        ],
        axis=1,
    ).reshape(blocks, own_rows, query_width + 2 * HEADS)
    gathered = lax.all_to_all(payload, "blk", split_axis=0, concat_axis=0, tiled=True)
    part_acc = gathered[:, :, :query_width].reshape(blocks, own_rows, HEADS, HEAD_DIM)
    part_max = gathered[:, :, query_width : query_width + HEADS]
    part_sum = gathered[:, :, query_width + HEADS :]
    overall = jnp.max(part_max, axis=0)
    factors = jnp.exp(part_max - overall[None])
    total_sum = jnp.sum(part_sum * factors, axis=0)
    total_acc = jnp.sum(part_acc * factors[..., None], axis=0)
    own_attention = (
        (total_acc / total_sum[..., None]).reshape(own_rows, query_width).astype(jnp.bfloat16)
    )
    attended = jnp.dot(
        lax.all_gather(own_attention, "blk", axis=0, tiled=True),
        out_weight,
        preferred_element_type=jnp.float32,
    )
    mixed_cols = (hidden.astype(jnp.float32) + attended).astype(jnp.bfloat16)
    mixed_rows = lax.all_gather(mixed_cols, "blk", axis=1, tiled=True)
    ffn_in = normalize(mixed_rows, ffn_gain)
    shared_cols = shared_gate_up.shape[2]
    gate_up = jnp.dot(
        ffn_in,
        shared_gate_up.reshape(model_width, 2 * shared_cols),
        preferred_element_type=jnp.float32,
    )
    shared_act = (jax.nn.silu(gate_up[:, :shared_cols]) * gate_up[:, shared_cols:]).astype(
        jnp.bfloat16
    )
    shared_term = jnp.dot(shared_act, shared_down, preferred_element_type=jnp.float32)
    row_experts = groups // SPLIT
    expert_count = row_experts * blocks
    capacity = NEW * TOPK * 4 // (expert_count * 3)
    row_expert_ids = block_index * row_experts + jnp.arange(row_experts, dtype=jnp.int32)
    route_hits = route_ids[:, :, None] == row_expert_ids[None, None, :]
    chosen = jnp.any(route_hits, axis=1)
    route_share = jnp.sum(jnp.where(route_hits, route_weights[:, :, None], 0.0), axis=1)
    slot_rank = jnp.cumsum(chosen.astype(jnp.int32), axis=0) - 1
    slot_ids = jnp.arange(capacity, dtype=jnp.int32)
    placed = chosen.T[:, None, :] & (slot_rank.T[:, None, :] == slot_ids[None, :, None])
    selector = placed.astype(jnp.bfloat16)
    outgoing = jnp.einsum(
        "ect,td->ecd", selector, ffn_in, preferred_element_type=jnp.float32
    ).astype(jnp.bfloat16)
    outgoing = jnp.repeat(outgoing, SPLIT, axis=0)
    received = lax.all_to_all(outgoing, "exp", split_axis=0, concat_axis=0, tiled=True)
    flat_rows = received.reshape(-1, model_width)
    expert_gu = jnp.dot(flat_rows, expert_gate_up[0], preferred_element_type=jnp.float32)
    activated = (jax.nn.silu(expert_gu[:, :FF_PART]) * expert_gu[:, FF_PART:]).astype(jnp.bfloat16)
    result = jnp.dot(activated, expert_down[0], preferred_element_type=jnp.float32).astype(
        jnp.bfloat16
    )
    returned = lax.all_to_all(
        result.reshape(received.shape), "exp", split_axis=0, concat_axis=0, tiled=True
    )
    summed = jnp.sum(
        returned.reshape(row_experts, SPLIT, capacity, model_width).astype(jnp.float32), axis=1
    )
    slot_weight = jnp.sum(placed.astype(jnp.float32) * route_share.T[:, None, :], axis=2)
    slot_values = summed * slot_weight[:, :, None]
    upper_part = slot_values.astype(jnp.bfloat16)
    lower_part = (slot_values - upper_part.astype(jnp.float32)).astype(jnp.bfloat16)
    routed = jnp.einsum(
        "ect,ecd->td", selector, upper_part, preferred_element_type=jnp.float32
    ) + jnp.einsum("ect,ecd->td", selector, lower_part, preferred_element_type=jnp.float32)
    layer_term = shared_term + routed
    summed_cols = lax.psum_scatter(layer_term, "blk", scatter_dimension=1, tiled=True)
    hidden_out = (mixed_cols.astype(jnp.float32) + summed_cols).astype(jnp.bfloat16)
    return (hidden_out, pool_out[None])


def solution(mesh):
    placed = (
        P("exp", "blk"),
        P(),
        P(None, "blk"),
        P(None, "blk"),
        P("exp", "blk", None, None),
        P("exp", None),
        P("exp"),
        P(),
        P("exp", None),
        P("exp", None),
        P(None, None, "blk"),
        P("blk", None),
        P(("blk", "exp"), None, None),
        P(("blk", "exp"), None, None),
    )
    return jax.shard_map(
        per_device,
        mesh=mesh,
        in_specs=placed,
        out_specs=(P("exp", "blk"), P("exp", "blk", None, None)),
        check_vma=False,
    )
```

```python
import math

import jax
import jax.numpy as jnp
from jax import lax
from jax.experimental import pallas as pl
from jax.experimental.pallas import tpu as pltpu
from jax.sharding import PartitionSpec as P

HEADS = 20
KV_HEADS = 4
HEAD_DIM = 128
TOPK = 6
SPLIT = 4
PAGE = 128
NEW = 256
FF_PART = 384


rope_base = 500000.0
norm_eps = 1e-05


def normalize(inputs, gain_vec):
    values = inputs.astype(jnp.float32)
    inv_rms = lax.rsqrt(jnp.mean(values * values, axis=-1, keepdims=True) + norm_eps)
    return (values * inv_rms * gain_vec).astype(jnp.bfloat16)


def rotate(inputs, positions):
    half_dim = HEAD_DIM // 2
    frequency = rope_base ** (-(jnp.arange(half_dim).astype(jnp.float32) * 2.0 / HEAD_DIM))
    angles = positions.astype(jnp.float32)[:, None] * frequency[None, :]
    cosine = jnp.cos(angles)[:, None, :]
    sine_vals = jnp.sin(angles)[:, None, :]
    lower_half = inputs[..., :half_dim]
    upper_half = inputs[..., half_dim:]
    return jnp.concatenate(
        [
            lower_half * cosine - upper_half * sine_vals,
            upper_half * cosine + lower_half * sine_vals,
        ],
        axis=-1,
    )


def attention_kernel(proj_ref, cos_ref, sin_ref, slot_ref, qpos_ref, kpos_ref, out_ref):
    key_width = KV_HEADS * HEAD_DIM
    group_size = HEADS // KV_HEADS
    allowed = kpos_ref[...] <= qpos_ref[...]
    cosine = cos_ref[...]
    sine_signed = sin_ref[...]
    lane = lax.broadcasted_iota(jnp.int32, (NEW, 128), 1)
    stats = jnp.zeros((NEW, 128), jnp.float32)
    for head in range(HEADS):
        kv = head // group_size
        raw = proj_ref[:, head * HEAD_DIM : (head + 1) * HEAD_DIM].astype(jnp.float32)
        swapped = pltpu.roll(raw, HEAD_DIM // 2, 1)
        query = (raw * cosine + swapped * sine_signed).astype(jnp.bfloat16)
        keys = slot_ref[:, kv * HEAD_DIM : (kv + 1) * HEAD_DIM]
        values = slot_ref[:, key_width + kv * HEAD_DIM : key_width + (kv + 1) * HEAD_DIM]
        scores = lax.dot_general(
            query, keys, (((1,), (1,)), ((), ())), preferred_element_type=jnp.float32
        ) * (1.0 / math.sqrt(HEAD_DIM))
        scores = jnp.where(allowed, scores, -1e30)
        peak = jnp.max(scores, axis=1, keepdims=True)
        probs = jnp.where(allowed, jnp.exp(scores - peak), 0.0)
        total = jnp.sum(probs, axis=1, keepdims=True)
        out_ref[:, head * HEAD_DIM : (head + 1) * HEAD_DIM] = jnp.dot(
            probs.astype(jnp.bfloat16), values, preferred_element_type=jnp.float32
        )
        stats = jnp.where(lane == head, peak, stats)
        stats = jnp.where(lane == HEADS + head, total, stats)
    out_ref[:, HEADS * HEAD_DIM :] = stats


def local_attention(projected_all, cosine, sine_signed, slot_rows, positions, key_pos):
    width = HEADS * HEAD_DIM + 128
    return pl.pallas_call(
        attention_kernel,
        out_shape=jax.ShapeDtypeStruct((NEW, width), jnp.float32),
        in_specs=[pl.BlockSpec(memory_space=pltpu.VMEM)] * 6,
        out_specs=pl.BlockSpec(memory_space=pltpu.VMEM),
        cost_estimate=pl.CostEstimate(
            flops=4 * NEW * slot_rows.shape[0] * HEAD_DIM * HEADS,
            transcendentals=NEW * slot_rows.shape[0] * HEADS,
            bytes_accessed=NEW * width * 4 + slot_rows.size * 2 + projected_all.size * 2,
        ),
    )(projected_all, cosine, sine_signed, slot_rows, positions[:, None], key_pos[None, :])


def combine_kernel(part_ref, out_ref):
    stats = part_ref[:, :, HEADS * HEAD_DIM :]
    overall = jnp.max(stats, axis=0, keepdims=True)
    factors = jnp.exp(stats - overall)
    lane = lax.broadcasted_iota(jnp.int32, stats.shape, 2)
    for head in range(HEADS):
        factor = jnp.sum(jnp.where(lane == head, factors, 0.0), axis=2, keepdims=True)
        total = jnp.sum(jnp.where(lane == HEADS + head, stats, 0.0), axis=2, keepdims=True)
        denominator = jnp.sum(factor * total, axis=0)
        numerator = jnp.sum(
            part_ref[:, :, head * HEAD_DIM : (head + 1) * HEAD_DIM] * factor, axis=0
        )
        out_ref[:, head * HEAD_DIM : (head + 1) * HEAD_DIM] = (
            numerator / denominator
        ).astype(out_ref.dtype)


def combine_attention(parts):
    sources, rows, width = parts.shape
    return pl.pallas_call(
        combine_kernel,
        out_shape=jax.ShapeDtypeStruct((rows, HEADS * HEAD_DIM), jnp.bfloat16),
        in_specs=[pl.BlockSpec(memory_space=pltpu.VMEM)],
        out_specs=pl.BlockSpec(memory_space=pltpu.VMEM),
        cost_estimate=pl.CostEstimate(
            flops=3 * parts.size, transcendentals=sources * rows * 128,
            bytes_accessed=parts.size * 4 + rows * HEADS * HEAD_DIM * 2,
        ),
    )(parts)


def per_device(
    hidden,
    attn_gain,
    qkv_weight,
    out_weight,
    kv_pool,
    page_table,
    cache_lens,
    ffn_gain,
    route_ids,
    route_weights,
    shared_gate_up,
    shared_down,
    expert_gate_up,
    expert_down,
):
    blocks = lax.axis_size("blk")
    groups = lax.axis_size("exp")
    block_index = lax.axis_index("blk")
    model_width = hidden.shape[1] * blocks
    query_width = HEADS * HEAD_DIM
    key_width = KV_HEADS * HEAD_DIM
    group_size = HEADS // KV_HEADS
    own_rows = NEW // blocks
    full_rows = lax.all_gather(hidden, "blk", axis=1, tiled=True)
    attn_in = normalize(full_rows, attn_gain)
    projected = jnp.dot(attn_in, qkv_weight, preferred_element_type=jnp.float32).astype(
        jnp.bfloat16
    )
    projected_all = lax.all_gather(projected, "blk", axis=1, tiled=True)
    length = cache_lens[0]
    positions = length + jnp.arange(NEW, dtype=jnp.int32)
    fresh_keys = rotate(
        projected_all[:, query_width : query_width + key_width]
        .astype(jnp.float32)
        .reshape(NEW, KV_HEADS, HEAD_DIM),
        positions,
    ).astype(jnp.bfloat16)
    appended = jnp.concatenate(
        [fresh_keys.reshape(NEW, key_width), projected_all[:, query_width + key_width :]], axis=1
    )
    page_map = page_table[0]
    pool_pages = page_map.shape[0]
    page_index = jnp.arange(pool_pages, dtype=jnp.int32)
    logical = jnp.sum(
        jnp.where(page_map[None, :] == page_index[:, None], page_index[None, :], 0), axis=1
    )
    local_pages = kv_pool.shape[1]
    local_logical = lax.dynamic_slice_in_dim(logical, block_index * local_pages, local_pages)
    slot_offsets = jnp.arange(PAGE, dtype=jnp.int32)
    local_pos = local_logical[:, None] * PAGE + slot_offsets[None, :]
    offset = local_pos - length
    written = (offset >= 0) & (offset < NEW)
    picked = appended[jnp.clip(offset, 0, NEW - 1)]
    pool_out = jnp.where(written[:, :, None], picked, kv_pool[0])
    half_dim = HEAD_DIM // 2
    frequency = rope_base ** (-(jnp.arange(half_dim).astype(jnp.float32) * 2.0 / HEAD_DIM))
    angles = positions.astype(jnp.float32)[:, None] * frequency[None, :]
    cosine = jnp.cos(angles)
    sine_vals = jnp.sin(angles)
    cosine_full = jnp.concatenate([cosine, cosine], axis=1)
    sine_signed = jnp.concatenate([-sine_vals, sine_vals], axis=1)
    slot_rows = pool_out.reshape(local_pages * PAGE, 2 * key_width)
    payload = local_attention(
        projected_all, cosine_full, sine_signed, slot_rows, positions, local_pos.reshape(-1)
    ).reshape(blocks, own_rows, query_width + 128)
    gathered = lax.all_to_all(payload, "blk", split_axis=0, concat_axis=0, tiled=True)
    own_attention = combine_attention(gathered)
    attended = jnp.dot(
        lax.all_gather(own_attention, "blk", axis=0, tiled=True),
        out_weight,
        preferred_element_type=jnp.float32,
    )
    mixed_cols = (hidden.astype(jnp.float32) + attended).astype(jnp.bfloat16)
    mixed_rows = lax.all_gather(mixed_cols, "blk", axis=1, tiled=True)
    ffn_in = normalize(mixed_rows, ffn_gain)
    shared_cols = shared_gate_up.shape[2]
    gate_up = jnp.dot(
        ffn_in,
        shared_gate_up.reshape(model_width, 2 * shared_cols),
        preferred_element_type=jnp.float32,
    )
    shared_act = (jax.nn.silu(gate_up[:, :shared_cols]) * gate_up[:, shared_cols:]).astype(
        jnp.bfloat16
    )
    shared_term = jnp.dot(shared_act, shared_down, preferred_element_type=jnp.float32)
    row_experts = groups // SPLIT
    expert_count = row_experts * blocks
    capacity = NEW * TOPK * 4 // (expert_count * 3)
    row_expert_ids = block_index * row_experts + jnp.arange(row_experts, dtype=jnp.int32)
    route_hits = route_ids[:, :, None] == row_expert_ids[None, None, :]
    chosen = jnp.any(route_hits, axis=1)
    route_share = jnp.sum(jnp.where(route_hits, route_weights[:, :, None], 0.0), axis=1)
    slot_rank = jnp.cumsum(chosen.astype(jnp.int32), axis=0) - 1
    slot_ids = jnp.arange(capacity, dtype=jnp.int32)
    placed = chosen.T[:, None, :] & (slot_rank.T[:, None, :] == slot_ids[None, :, None])
    selector = placed.astype(jnp.bfloat16)
    outgoing = jnp.einsum(
        "ect,td->ecd", selector, ffn_in, preferred_element_type=jnp.float32
    ).astype(jnp.bfloat16)
    outgoing = jnp.repeat(outgoing, SPLIT, axis=0)
    received = lax.all_to_all(outgoing, "exp", split_axis=0, concat_axis=0, tiled=True)
    flat_rows = received.reshape(-1, model_width)
    expert_gu = jnp.dot(flat_rows, expert_gate_up[0], preferred_element_type=jnp.float32)
    activated = (jax.nn.silu(expert_gu[:, :FF_PART]) * expert_gu[:, FF_PART:]).astype(jnp.bfloat16)
    result = jnp.dot(activated, expert_down[0], preferred_element_type=jnp.float32).astype(
        jnp.bfloat16
    )
    returned = lax.all_to_all(
        result.reshape(received.shape), "exp", split_axis=0, concat_axis=0, tiled=True
    )
    summed = jnp.sum(
        returned.reshape(row_experts, SPLIT, capacity, model_width).astype(jnp.float32), axis=1
    )
    slot_weight = jnp.sum(placed.astype(jnp.float32) * route_share.T[:, None, :], axis=2)
    slot_values = summed * slot_weight[:, :, None]
    upper_part = slot_values.astype(jnp.bfloat16)
    lower_part = (slot_values - upper_part.astype(jnp.float32)).astype(jnp.bfloat16)
    routed = jnp.einsum(
        "ect,ecd->td", selector, upper_part, preferred_element_type=jnp.float32
    ) + jnp.einsum("ect,ecd->td", selector, lower_part, preferred_element_type=jnp.float32)
    layer_term = shared_term + routed
    summed_cols = lax.psum_scatter(layer_term, "blk", scatter_dimension=1, tiled=True)
    hidden_out = (mixed_cols.astype(jnp.float32) + summed_cols).astype(jnp.bfloat16)
    return (hidden_out, pool_out[None])


def solution(mesh):
    placed = (
        P("exp", "blk"),
        P(),
        P(None, "blk"),
        P(None, "blk"),
        P("exp", "blk", None, None),
        P("exp", None),
        P("exp"),
        P(),
        P("exp", None),
        P("exp", None),
        P(None, None, "blk"),
        P("blk", None),
        P(("blk", "exp"), None, None),
        P(("blk", "exp"), None, None),
    )
    return jax.shard_map(
        per_device,
        mesh=mesh,
        in_specs=placed,
        out_specs=(P("exp", "blk"), P("exp", "blk", None, None)),
        check_vma=False,
    )
```

```python
import math

import jax
import jax.numpy as jnp
from jax import lax
from jax.experimental import pallas as pl
from jax.experimental.pallas import tpu as pltpu
from jax.sharding import PartitionSpec as P

HEADS = 20
KV_HEADS = 4
HEAD_DIM = 128
TOPK = 6
SPLIT = 4
PAGE = 128
NEW = 256
FF_PART = 384


rope_base = 500000.0
norm_eps = 1e-05


def normalize(inputs, gain_vec):
    values = inputs.astype(jnp.float32)
    inv_rms = lax.rsqrt(jnp.mean(values * values, axis=-1, keepdims=True) + norm_eps)
    return (values * inv_rms * gain_vec).astype(jnp.bfloat16)


def rotate(inputs, positions):
    half_dim = HEAD_DIM // 2
    frequency = rope_base ** (-(jnp.arange(half_dim).astype(jnp.float32) * 2.0 / HEAD_DIM))
    angles = positions.astype(jnp.float32)[:, None] * frequency[None, :]
    cosine = jnp.cos(angles)[:, None, :]
    sine_vals = jnp.sin(angles)[:, None, :]
    lower_half = inputs[..., :half_dim]
    upper_half = inputs[..., half_dim:]
    return jnp.concatenate(
        [
            lower_half * cosine - upper_half * sine_vals,
            upper_half * cosine + lower_half * sine_vals,
        ],
        axis=-1,
    )


def attention_kernel(proj_ref, cos_ref, sin_ref, slot_ref, qpos_ref, kpos_ref, out_ref):
    key_width = KV_HEADS * HEAD_DIM
    group_size = HEADS // KV_HEADS
    allowed = kpos_ref[...] <= qpos_ref[...]
    cosine = cos_ref[...]
    sine_signed = sin_ref[...]
    lane = lax.broadcasted_iota(jnp.int32, (NEW, 128), 1)
    stats = jnp.zeros((NEW, 128), jnp.float32)
    for head in range(HEADS):
        kv = head // group_size
        raw = proj_ref[:, head * HEAD_DIM : (head + 1) * HEAD_DIM].astype(jnp.float32)
        swapped = pltpu.roll(raw, HEAD_DIM // 2, 1)
        query = (raw * cosine + swapped * sine_signed).astype(jnp.bfloat16)
        keys = slot_ref[:, kv * HEAD_DIM : (kv + 1) * HEAD_DIM]
        values = slot_ref[:, key_width + kv * HEAD_DIM : key_width + (kv + 1) * HEAD_DIM]
        scores = lax.dot_general(
            query, keys, (((1,), (1,)), ((), ())), preferred_element_type=jnp.float32
        ) * (1.0 / math.sqrt(HEAD_DIM))
        scores = jnp.where(allowed, scores, -1e30)
        peak = jnp.max(scores, axis=1, keepdims=True)
        probs = jnp.where(allowed, jnp.exp(scores - peak), 0.0)
        total = jnp.sum(probs, axis=1, keepdims=True)
        out_ref[:, head * HEAD_DIM : (head + 1) * HEAD_DIM] = jnp.dot(
            probs.astype(jnp.bfloat16), values, preferred_element_type=jnp.float32
        )
        stats = jnp.where(lane == head, peak, stats)
        stats = jnp.where(lane == HEADS + head, total, stats)
    out_ref[:, HEADS * HEAD_DIM :] = stats


def local_attention(projected_all, cosine, sine_signed, slot_rows, positions, key_pos):
    width = HEADS * HEAD_DIM + 128
    return pl.pallas_call(
        attention_kernel,
        out_shape=jax.ShapeDtypeStruct((NEW, width), jnp.float32),
        in_specs=[pl.BlockSpec(memory_space=pltpu.VMEM)] * 6,
        out_specs=pl.BlockSpec(memory_space=pltpu.VMEM),
        cost_estimate=pl.CostEstimate(
            flops=4 * NEW * slot_rows.shape[0] * HEAD_DIM * HEADS,
            transcendentals=NEW * slot_rows.shape[0] * HEADS,
            bytes_accessed=NEW * width * 4 + slot_rows.size * 2 + projected_all.size * 2,
        ),
    )(projected_all, cosine, sine_signed, slot_rows, positions[:, None], key_pos[None, :])


def combine_kernel(part_ref, out_ref):
    stats = part_ref[:, :, HEADS * HEAD_DIM :]
    overall = jnp.max(stats, axis=0, keepdims=True)
    factors = jnp.exp(stats - overall)
    lane = lax.broadcasted_iota(jnp.int32, stats.shape, 2)
    for head in range(HEADS):
        factor = jnp.sum(jnp.where(lane == head, factors, 0.0), axis=2, keepdims=True)
        total = jnp.sum(jnp.where(lane == HEADS + head, stats, 0.0), axis=2, keepdims=True)
        denominator = jnp.sum(factor * total, axis=0)
        numerator = jnp.sum(
            part_ref[:, :, head * HEAD_DIM : (head + 1) * HEAD_DIM] * factor, axis=0
        )
        out_ref[:, head * HEAD_DIM : (head + 1) * HEAD_DIM] = (
            numerator / denominator
        ).astype(out_ref.dtype)


def combine_attention(parts):
    sources, rows, width = parts.shape
    return pl.pallas_call(
        combine_kernel,
        out_shape=jax.ShapeDtypeStruct((rows, HEADS * HEAD_DIM), jnp.bfloat16),
        in_specs=[pl.BlockSpec(memory_space=pltpu.VMEM)],
        out_specs=pl.BlockSpec(memory_space=pltpu.VMEM),
        cost_estimate=pl.CostEstimate(
            flops=3 * parts.size, transcendentals=sources * rows * 128,
            bytes_accessed=parts.size * 4 + rows * HEADS * HEAD_DIM * 2,
        ),
    )(parts)


def gather_blocks(values, axis):
    count = lax.axis_size("blk")
    stacked = jnp.broadcast_to(values[None], (count,) + values.shape)
    received = lax.all_to_all(stacked, "blk", split_axis=0, concat_axis=0, tiled=True)
    return jnp.concatenate([received[i] for i in range(count)], axis=axis)


def scatter_sum_blocks(values):
    count = lax.axis_size("blk")
    rows, width = values.shape
    pieces = values.reshape(rows, count, width // count).transpose(1, 0, 2)
    received = lax.all_to_all(pieces, "blk", split_axis=0, concat_axis=0, tiled=True)
    return jnp.sum(received, axis=0)


def per_device(
    hidden,
    attn_gain,
    qkv_weight,
    out_weight,
    kv_pool,
    page_table,
    cache_lens,
    ffn_gain,
    route_ids,
    route_weights,
    shared_gate_up,
    shared_down,
    expert_gate_up,
    expert_down,
):
    blocks = lax.axis_size("blk")
    groups = lax.axis_size("exp")
    block_index = lax.axis_index("blk")
    model_width = hidden.shape[1] * blocks
    query_width = HEADS * HEAD_DIM
    key_width = KV_HEADS * HEAD_DIM
    group_size = HEADS // KV_HEADS
    own_rows = NEW // blocks
    full_rows = gather_blocks(hidden, 1)
    attn_in = normalize(full_rows, attn_gain)
    projected = jnp.dot(attn_in, qkv_weight, preferred_element_type=jnp.float32).astype(
        jnp.bfloat16
    )
    projected_all = gather_blocks(projected, 1)
    length = cache_lens[0]
    positions = length + jnp.arange(NEW, dtype=jnp.int32)
    fresh_keys = rotate(
        projected_all[:, query_width : query_width + key_width]
        .astype(jnp.float32)
        .reshape(NEW, KV_HEADS, HEAD_DIM),
        positions,
    ).astype(jnp.bfloat16)
    appended = jnp.concatenate(
        [fresh_keys.reshape(NEW, key_width), projected_all[:, query_width + key_width :]], axis=1
    )
    page_map = page_table[0]
    pool_pages = page_map.shape[0]
    page_index = jnp.arange(pool_pages, dtype=jnp.int32)
    logical = jnp.sum(
        jnp.where(page_map[None, :] == page_index[:, None], page_index[None, :], 0), axis=1
    )
    local_pages = kv_pool.shape[1]
    local_logical = lax.dynamic_slice_in_dim(logical, block_index * local_pages, local_pages)
    slot_offsets = jnp.arange(PAGE, dtype=jnp.int32)
    local_pos = local_logical[:, None] * PAGE + slot_offsets[None, :]
    offset = local_pos - length
    written = (offset >= 0) & (offset < NEW)
    picked = appended[jnp.clip(offset, 0, NEW - 1)]
    pool_out = jnp.where(written[:, :, None], picked, kv_pool[0])
    half_dim = HEAD_DIM // 2
    frequency = rope_base ** (-(jnp.arange(half_dim).astype(jnp.float32) * 2.0 / HEAD_DIM))
    angles = positions.astype(jnp.float32)[:, None] * frequency[None, :]
    cosine = jnp.cos(angles)
    sine_vals = jnp.sin(angles)
    cosine_full = jnp.concatenate([cosine, cosine], axis=1)
    sine_signed = jnp.concatenate([-sine_vals, sine_vals], axis=1)
    slot_rows = pool_out.reshape(local_pages * PAGE, 2 * key_width)
    payload = local_attention(
        projected_all, cosine_full, sine_signed, slot_rows, positions, local_pos.reshape(-1)
    ).reshape(blocks, own_rows, query_width + 128)
    gathered = lax.all_to_all(payload, "blk", split_axis=0, concat_axis=0, tiled=True)
    own_attention = combine_attention(gathered)
    attended = jnp.dot(
        gather_blocks(own_attention, 0),
        out_weight,
        preferred_element_type=jnp.float32,
    )
    mixed_cols = (hidden.astype(jnp.float32) + attended).astype(jnp.bfloat16)
    mixed_rows = gather_blocks(mixed_cols, 1)
    ffn_in = normalize(mixed_rows, ffn_gain)
    shared_cols = shared_gate_up.shape[2]
    gate_up = jnp.dot(
        ffn_in,
        shared_gate_up.reshape(model_width, 2 * shared_cols),
        preferred_element_type=jnp.float32,
    )
    shared_act = (jax.nn.silu(gate_up[:, :shared_cols]) * gate_up[:, shared_cols:]).astype(
        jnp.bfloat16
    )
    shared_term = jnp.dot(shared_act, shared_down, preferred_element_type=jnp.float32)
    row_experts = groups // SPLIT
    expert_count = row_experts * blocks
    capacity = NEW * TOPK * 4 // (expert_count * 3)
    row_expert_ids = block_index * row_experts + jnp.arange(row_experts, dtype=jnp.int32)
    route_hits = route_ids[:, :, None] == row_expert_ids[None, None, :]
    chosen = jnp.any(route_hits, axis=1)
    route_share = jnp.sum(jnp.where(route_hits, route_weights[:, :, None], 0.0), axis=1)
    slot_rank = jnp.cumsum(chosen.astype(jnp.int32), axis=0) - 1
    slot_ids = jnp.arange(capacity, dtype=jnp.int32)
    placed = chosen.T[:, None, :] & (slot_rank.T[:, None, :] == slot_ids[None, :, None])
    selector = placed.astype(jnp.bfloat16)
    outgoing = jnp.einsum(
        "ect,td->ecd", selector, ffn_in, preferred_element_type=jnp.float32
    ).astype(jnp.bfloat16)
    outgoing = jnp.repeat(outgoing, SPLIT, axis=0)
    received = lax.all_to_all(outgoing, "exp", split_axis=0, concat_axis=0, tiled=True)
    flat_rows = received.reshape(-1, model_width)
    expert_gu = jnp.dot(flat_rows, expert_gate_up[0], preferred_element_type=jnp.float32)
    activated = (jax.nn.silu(expert_gu[:, :FF_PART]) * expert_gu[:, FF_PART:]).astype(jnp.bfloat16)
    result = jnp.dot(activated, expert_down[0], preferred_element_type=jnp.float32).astype(
        jnp.bfloat16
    )
    returned = lax.all_to_all(
        result.reshape(received.shape), "exp", split_axis=0, concat_axis=0, tiled=True
    )
    summed = jnp.sum(
        returned.reshape(row_experts, SPLIT, capacity, model_width).astype(jnp.float32), axis=1
    )
    slot_weight = jnp.sum(placed.astype(jnp.float32) * route_share.T[:, None, :], axis=2)
    slot_values = summed * slot_weight[:, :, None]
    upper_part = slot_values.astype(jnp.bfloat16)
    lower_part = (slot_values - upper_part.astype(jnp.float32)).astype(jnp.bfloat16)
    routed = jnp.einsum(
        "ect,ecd->td", selector, upper_part, preferred_element_type=jnp.float32
    ) + jnp.einsum("ect,ecd->td", selector, lower_part, preferred_element_type=jnp.float32)
    layer_term = shared_term + routed
    summed_cols = scatter_sum_blocks(layer_term)
    hidden_out = (mixed_cols.astype(jnp.float32) + summed_cols).astype(jnp.bfloat16)
    return (hidden_out, pool_out[None])


def solution(mesh):
    placed = (
        P("exp", "blk"),
        P(),
        P(None, "blk"),
        P(None, "blk"),
        P("exp", "blk", None, None),
        P("exp", None),
        P("exp"),
        P(),
        P("exp", None),
        P("exp", None),
        P(None, None, "blk"),
        P("blk", None),
        P(("blk", "exp"), None, None),
        P(("blk", "exp"), None, None),
    )
    return jax.shard_map(
        per_device,
        mesh=mesh,
        in_specs=placed,
        out_specs=(P("exp", "blk"), P("exp", "blk", None, None)),
        check_vma=False,
    )
```

```python
import math

import jax
import jax.numpy as jnp
from jax import lax
from jax.experimental import pallas as pl
from jax.experimental.pallas import tpu as pltpu
from jax.sharding import PartitionSpec as P

HEADS = 20
KV_HEADS = 4
HEAD_DIM = 128
TOPK = 6
SPLIT = 4
PAGE = 128
NEW = 256
FF_PART = 384


rope_base = 500000.0
norm_eps = 1e-05


def normalize(inputs, gain_vec):
    values = inputs.astype(jnp.float32)
    inv_rms = lax.rsqrt(jnp.mean(values * values, axis=-1, keepdims=True) + norm_eps)
    return (values * inv_rms * gain_vec).astype(jnp.bfloat16)


def rotate(inputs, positions):
    half_dim = HEAD_DIM // 2
    frequency = rope_base ** (-(jnp.arange(half_dim).astype(jnp.float32) * 2.0 / HEAD_DIM))
    angles = positions.astype(jnp.float32)[:, None] * frequency[None, :]
    cosine = jnp.cos(angles)[:, None, :]
    sine_vals = jnp.sin(angles)[:, None, :]
    lower_half = inputs[..., :half_dim]
    upper_half = inputs[..., half_dim:]
    return jnp.concatenate(
        [
            lower_half * cosine - upper_half * sine_vals,
            upper_half * cosine + lower_half * sine_vals,
        ],
        axis=-1,
    )


def attention_kernel(proj_ref, cos_ref, sin_ref, slot_ref, qpos_ref, kpos_ref, out_ref):
    key_width = KV_HEADS * HEAD_DIM
    group_size = HEADS // KV_HEADS
    allowed = kpos_ref[...] <= qpos_ref[...]
    cosine = cos_ref[...]
    sine_signed = sin_ref[...]
    lane = lax.broadcasted_iota(jnp.int32, (NEW, 128), 1)
    stats = jnp.zeros((NEW, 128), jnp.float32)
    for head in range(HEADS):
        kv = head // group_size
        raw = proj_ref[:, head * HEAD_DIM : (head + 1) * HEAD_DIM].astype(jnp.float32)
        swapped = pltpu.roll(raw, HEAD_DIM // 2, 1)
        query = (raw * cosine + swapped * sine_signed).astype(jnp.bfloat16)
        keys = slot_ref[:, kv * HEAD_DIM : (kv + 1) * HEAD_DIM]
        values = slot_ref[:, key_width + kv * HEAD_DIM : key_width + (kv + 1) * HEAD_DIM]
        scores = lax.dot_general(
            query, keys, (((1,), (1,)), ((), ())), preferred_element_type=jnp.float32
        ) * (1.0 / math.sqrt(HEAD_DIM))
        scores = jnp.where(allowed, scores, -1e30)
        peak = jnp.max(scores, axis=1, keepdims=True)
        probs = jnp.where(allowed, jnp.exp(scores - peak), 0.0)
        total = jnp.sum(probs, axis=1, keepdims=True)
        out_ref[:, head * HEAD_DIM : (head + 1) * HEAD_DIM] = jnp.dot(
            probs.astype(jnp.bfloat16), values, preferred_element_type=jnp.float32
        )
        stats = jnp.where(lane == head, peak, stats)
        stats = jnp.where(lane == HEADS + head, total, stats)
    out_ref[:, HEADS * HEAD_DIM :] = stats


def local_attention(projected_all, cosine, sine_signed, slot_rows, positions, key_pos):
    width = HEADS * HEAD_DIM + 128
    return pl.pallas_call(
        attention_kernel,
        out_shape=jax.ShapeDtypeStruct((NEW, width), jnp.float32),
        in_specs=[pl.BlockSpec(memory_space=pltpu.VMEM)] * 6,
        out_specs=pl.BlockSpec(memory_space=pltpu.VMEM),
        cost_estimate=pl.CostEstimate(
            flops=4 * NEW * slot_rows.shape[0] * HEAD_DIM * HEADS,
            transcendentals=NEW * slot_rows.shape[0] * HEADS,
            bytes_accessed=NEW * width * 4 + slot_rows.size * 2 + projected_all.size * 2,
        ),
    )(projected_all, cosine, sine_signed, slot_rows, positions[:, None], key_pos[None, :])


def combine_kernel(part_ref, out_ref):
    stats = part_ref[:, :, HEADS * HEAD_DIM :]
    overall = jnp.max(stats, axis=0, keepdims=True)
    factors = jnp.exp(stats - overall)
    lane = lax.broadcasted_iota(jnp.int32, stats.shape, 2)
    for head in range(HEADS):
        factor = jnp.sum(jnp.where(lane == head, factors, 0.0), axis=2, keepdims=True)
        total = jnp.sum(jnp.where(lane == HEADS + head, stats, 0.0), axis=2, keepdims=True)
        denominator = jnp.sum(factor * total, axis=0)
        numerator = jnp.sum(
            part_ref[:, :, head * HEAD_DIM : (head + 1) * HEAD_DIM] * factor, axis=0
        )
        out_ref[:, head * HEAD_DIM : (head + 1) * HEAD_DIM] = (
            numerator / denominator
        ).astype(out_ref.dtype)


def combine_attention(parts):
    sources, rows, width = parts.shape
    return pl.pallas_call(
        combine_kernel,
        out_shape=jax.ShapeDtypeStruct((rows, HEADS * HEAD_DIM), jnp.bfloat16),
        in_specs=[pl.BlockSpec(memory_space=pltpu.VMEM)],
        out_specs=pl.BlockSpec(memory_space=pltpu.VMEM),
        cost_estimate=pl.CostEstimate(
            flops=3 * parts.size, transcendentals=sources * rows * 128,
            bytes_accessed=parts.size * 4 + rows * HEADS * HEAD_DIM * 2,
        ),
    )(parts)


def gather_blocks(values, axis):
    count = lax.axis_size("blk")
    stacked = jnp.broadcast_to(values[None], (count,) + values.shape)
    received = lax.all_to_all(stacked, "blk", split_axis=0, concat_axis=0, tiled=True)
    if axis == 0:
        return received.reshape((count * values.shape[0],) + values.shape[1:])
    return received.transpose(1, 0, 2).reshape(values.shape[0], count * values.shape[1])


def scatter_sum_blocks(values):
    count = lax.axis_size("blk")
    rows, width = values.shape
    pieces = values.reshape(rows, count, width // count).transpose(1, 0, 2)
    received = lax.all_to_all(pieces, "blk", split_axis=0, concat_axis=0, tiled=True)
    return jnp.sum(received, axis=0)


def per_device(
    hidden,
    attn_gain,
    qkv_weight,
    out_weight,
    kv_pool,
    page_table,
    cache_lens,
    ffn_gain,
    route_ids,
    route_weights,
    shared_gate_up,
    shared_down,
    expert_gate_up,
    expert_down,
):
    blocks = lax.axis_size("blk")
    groups = lax.axis_size("exp")
    block_index = lax.axis_index("blk")
    model_width = hidden.shape[1] * blocks
    query_width = HEADS * HEAD_DIM
    key_width = KV_HEADS * HEAD_DIM
    group_size = HEADS // KV_HEADS
    own_rows = NEW // blocks
    full_rows = gather_blocks(hidden, 1)
    attn_in = normalize(full_rows, attn_gain)
    projected = jnp.dot(attn_in, qkv_weight, preferred_element_type=jnp.float32).astype(
        jnp.bfloat16
    )
    projected_all = gather_blocks(projected, 1)
    length = cache_lens[0]
    positions = length + jnp.arange(NEW, dtype=jnp.int32)
    fresh_keys = rotate(
        projected_all[:, query_width : query_width + key_width]
        .astype(jnp.float32)
        .reshape(NEW, KV_HEADS, HEAD_DIM),
        positions,
    ).astype(jnp.bfloat16)
    appended = jnp.concatenate(
        [fresh_keys.reshape(NEW, key_width), projected_all[:, query_width + key_width :]], axis=1
    )
    page_map = page_table[0]
    pool_pages = page_map.shape[0]
    page_index = jnp.arange(pool_pages, dtype=jnp.int32)
    logical = jnp.sum(
        jnp.where(page_map[None, :] == page_index[:, None], page_index[None, :], 0), axis=1
    )
    local_pages = kv_pool.shape[1]
    local_logical = lax.dynamic_slice_in_dim(logical, block_index * local_pages, local_pages)
    slot_offsets = jnp.arange(PAGE, dtype=jnp.int32)
    local_pos = local_logical[:, None] * PAGE + slot_offsets[None, :]
    offset = local_pos - length
    written = (offset >= 0) & (offset < NEW)
    picked = appended[jnp.clip(offset, 0, NEW - 1)]
    pool_out = jnp.where(written[:, :, None], picked, kv_pool[0])
    half_dim = HEAD_DIM // 2
    frequency = rope_base ** (-(jnp.arange(half_dim).astype(jnp.float32) * 2.0 / HEAD_DIM))
    angles = positions.astype(jnp.float32)[:, None] * frequency[None, :]
    cosine = jnp.cos(angles)
    sine_vals = jnp.sin(angles)
    cosine_full = jnp.concatenate([cosine, cosine], axis=1)
    sine_signed = jnp.concatenate([-sine_vals, sine_vals], axis=1)
    slot_rows = pool_out.reshape(local_pages * PAGE, 2 * key_width)
    payload = local_attention(
        projected_all, cosine_full, sine_signed, slot_rows, positions, local_pos.reshape(-1)
    ).reshape(blocks, own_rows, query_width + 128)
    gathered = lax.all_to_all(payload, "blk", split_axis=0, concat_axis=0, tiled=True)
    own_attention = combine_attention(gathered)
    attended = jnp.dot(
        gather_blocks(own_attention, 0),
        out_weight,
        preferred_element_type=jnp.float32,
    )
    mixed_cols = (hidden.astype(jnp.float32) + attended).astype(jnp.bfloat16)
    mixed_rows = gather_blocks(mixed_cols, 1)
    ffn_in = normalize(mixed_rows, ffn_gain)
    shared_cols = shared_gate_up.shape[2]
    gate_up = jnp.dot(
        ffn_in,
        shared_gate_up.reshape(model_width, 2 * shared_cols),
        preferred_element_type=jnp.float32,
    )
    shared_act = (jax.nn.silu(gate_up[:, :shared_cols]) * gate_up[:, shared_cols:]).astype(
        jnp.bfloat16
    )
    shared_term = jnp.dot(shared_act, shared_down, preferred_element_type=jnp.float32)
    row_experts = groups // SPLIT
    expert_count = row_experts * blocks
    capacity = NEW * TOPK * 4 // (expert_count * 3)
    row_expert_ids = block_index * row_experts + jnp.arange(row_experts, dtype=jnp.int32)
    route_hits = route_ids[:, :, None] == row_expert_ids[None, None, :]
    chosen = jnp.any(route_hits, axis=1)
    route_share = jnp.sum(jnp.where(route_hits, route_weights[:, :, None], 0.0), axis=1)
    slot_rank = jnp.cumsum(chosen.astype(jnp.int32), axis=0) - 1
    slot_ids = jnp.arange(capacity, dtype=jnp.int32)
    placed = chosen.T[:, None, :] & (slot_rank.T[:, None, :] == slot_ids[None, :, None])
    selector = placed.astype(jnp.bfloat16)
    outgoing = jnp.einsum(
        "ect,td->ecd", selector, ffn_in, preferred_element_type=jnp.float32
    ).astype(jnp.bfloat16)
    outgoing = jnp.repeat(outgoing, SPLIT, axis=0)
    received = lax.all_to_all(outgoing, "exp", split_axis=0, concat_axis=0, tiled=True)
    flat_rows = received.reshape(-1, model_width)
    expert_gu = jnp.dot(flat_rows, expert_gate_up[0], preferred_element_type=jnp.float32)
    activated = (jax.nn.silu(expert_gu[:, :FF_PART]) * expert_gu[:, FF_PART:]).astype(jnp.bfloat16)
    result = jnp.dot(activated, expert_down[0], preferred_element_type=jnp.float32).astype(
        jnp.bfloat16
    )
    returned = lax.all_to_all(
        result.reshape(received.shape), "exp", split_axis=0, concat_axis=0, tiled=True
    )
    summed = jnp.sum(
        returned.reshape(row_experts, SPLIT, capacity, model_width).astype(jnp.float32), axis=1
    )
    slot_weight = jnp.sum(placed.astype(jnp.float32) * route_share.T[:, None, :], axis=2)
    slot_values = summed * slot_weight[:, :, None]
    upper_part = slot_values.astype(jnp.bfloat16)
    lower_part = (slot_values - upper_part.astype(jnp.float32)).astype(jnp.bfloat16)
    routed = jnp.einsum(
        "ect,ecd->td", selector, upper_part, preferred_element_type=jnp.float32
    ) + jnp.einsum("ect,ecd->td", selector, lower_part, preferred_element_type=jnp.float32)
    layer_term = shared_term + routed
    summed_cols = scatter_sum_blocks(layer_term)
    hidden_out = (mixed_cols.astype(jnp.float32) + summed_cols).astype(jnp.bfloat16)
    return (hidden_out, pool_out[None])


def solution(mesh):
    placed = (
        P("exp", "blk"),
        P(),
        P(None, "blk"),
        P(None, "blk"),
        P("exp", "blk", None, None),
        P("exp", None),
        P("exp"),
        P(),
        P("exp", None),
        P("exp", None),
        P(None, None, "blk"),
        P("blk", None),
        P(("blk", "exp"), None, None),
        P(("blk", "exp"), None, None),
    )
    return jax.shard_map(
        per_device,
        mesh=mesh,
        in_specs=placed,
        out_specs=(P("exp", "blk"), P("exp", "blk", None, None)),
        check_vma=False,
    )
```

```python
import math

import jax
import jax.numpy as jnp
from jax import lax
from jax.experimental import pallas as pl
from jax.experimental.pallas import tpu as pltpu
from jax.sharding import PartitionSpec as P

HEADS = 20
KV_HEADS = 4
HEAD_DIM = 128
TOPK = 6
SPLIT = 4
PAGE = 128
NEW = 256
FF_PART = 384


rope_base = 500000.0
norm_eps = 1e-05


def normalize(inputs, gain_vec):
    values = inputs.astype(jnp.float32)
    inv_rms = lax.rsqrt(jnp.mean(values * values, axis=-1, keepdims=True) + norm_eps)
    return (values * inv_rms * gain_vec).astype(jnp.bfloat16)


def rotate(inputs, positions):
    half_dim = HEAD_DIM // 2
    frequency = rope_base ** (-(jnp.arange(half_dim).astype(jnp.float32) * 2.0 / HEAD_DIM))
    angles = positions.astype(jnp.float32)[:, None] * frequency[None, :]
    cosine = jnp.cos(angles)[:, None, :]
    sine_vals = jnp.sin(angles)[:, None, :]
    lower_half = inputs[..., :half_dim]
    upper_half = inputs[..., half_dim:]
    return jnp.concatenate(
        [
            lower_half * cosine - upper_half * sine_vals,
            upper_half * cosine + lower_half * sine_vals,
        ],
        axis=-1,
    )


def split_three(value):
    high = value.astype(jnp.bfloat16).astype(jnp.float32)
    rest = value - high
    middle = rest.astype(jnp.bfloat16).astype(jnp.float32)
    low = (rest - middle).astype(jnp.bfloat16).astype(jnp.float32)
    return [high, middle, low]


def attention_kernel(proj_ref, cos_ref, sin_ref, slot_ref, qpos_ref, kpos_ref, out_ref):
    key_width = KV_HEADS * HEAD_DIM
    group_size = HEADS // KV_HEADS
    allowed = kpos_ref[...] <= qpos_ref[...]
    cosine = cos_ref[...]
    sine_signed = sin_ref[...]
    lane = lax.broadcasted_iota(jnp.int32, (NEW, 128), 1)
    stats = jnp.zeros((NEW, 128), jnp.float32)
    for head in range(HEADS):
        kv = head // group_size
        raw = proj_ref[:, head * HEAD_DIM : (head + 1) * HEAD_DIM].astype(jnp.float32)
        swapped = pltpu.roll(raw, HEAD_DIM // 2, 1)
        query = (raw * cosine + swapped * sine_signed).astype(jnp.bfloat16)
        keys = slot_ref[:, kv * HEAD_DIM : (kv + 1) * HEAD_DIM]
        values = slot_ref[:, key_width + kv * HEAD_DIM : key_width + (kv + 1) * HEAD_DIM]
        scores = lax.dot_general(
            query, keys, (((1,), (1,)), ((), ())), preferred_element_type=jnp.float32
        ) * (1.0 / math.sqrt(HEAD_DIM))
        scores = jnp.where(allowed, scores, -1e30)
        peak = jnp.max(scores, axis=1, keepdims=True)
        probs = jnp.where(allowed, jnp.exp(scores - peak), 0.0)
        total = jnp.sum(probs, axis=1, keepdims=True)
        out_ref[:, head * HEAD_DIM : (head + 1) * HEAD_DIM] = jnp.dot(
            probs.astype(jnp.bfloat16), values, preferred_element_type=jnp.float32
        ).astype(out_ref.dtype)
        for slot, value in enumerate(split_three(peak) + split_three(total)):
            stats = jnp.where(lane == slot * HEADS + head, value, stats)
    out_ref[:, HEADS * HEAD_DIM :] = stats.astype(out_ref.dtype)


def local_attention(projected_all, cosine, sine_signed, slot_rows, positions, key_pos):
    width = HEADS * HEAD_DIM + 128
    return pl.pallas_call(
        attention_kernel,
        out_shape=jax.ShapeDtypeStruct((NEW, width), jnp.bfloat16),
        in_specs=[pl.BlockSpec(memory_space=pltpu.VMEM)] * 6,
        out_specs=pl.BlockSpec(memory_space=pltpu.VMEM),
        cost_estimate=pl.CostEstimate(
            flops=4 * NEW * slot_rows.shape[0] * HEAD_DIM * HEADS,
            transcendentals=NEW * slot_rows.shape[0] * HEADS,
            bytes_accessed=NEW * width * 2 + slot_rows.size * 2 + projected_all.size * 2,
        ),
    )(projected_all, cosine, sine_signed, slot_rows, positions[:, None], key_pos[None, :])


def combine_kernel(part_ref, out_ref):
    coded = part_ref[:, :, HEADS * HEAD_DIM :].astype(jnp.float32)
    lane = lax.broadcasted_iota(jnp.int32, coded.shape, 2)

    def pick(slot):
        return jnp.sum(jnp.where(lane == slot, coded, 0.0), axis=2, keepdims=True)

    for head in range(HEADS):
        peak = (pick(head) + pick(HEADS + head)) + pick(2 * HEADS + head)
        total = (pick(3 * HEADS + head) + pick(4 * HEADS + head)) + pick(5 * HEADS + head)
        factor = jnp.exp(peak - jnp.max(peak, axis=0, keepdims=True))
        denominator = jnp.sum(factor * total, axis=0)
        numerator = jnp.sum(
            part_ref[:, :, head * HEAD_DIM : (head + 1) * HEAD_DIM].astype(jnp.float32) * factor,
            axis=0,
        )
        out_ref[:, head * HEAD_DIM : (head + 1) * HEAD_DIM] = (
            numerator / denominator
        ).astype(out_ref.dtype)


def combine_attention(parts):
    sources, rows, width = parts.shape
    return pl.pallas_call(
        combine_kernel,
        out_shape=jax.ShapeDtypeStruct((rows, HEADS * HEAD_DIM), jnp.bfloat16),
        in_specs=[pl.BlockSpec(memory_space=pltpu.VMEM)],
        out_specs=pl.BlockSpec(memory_space=pltpu.VMEM),
        cost_estimate=pl.CostEstimate(
            flops=3 * parts.size, transcendentals=sources * rows * 128,
            bytes_accessed=parts.size * 2 + rows * HEADS * HEAD_DIM * 2,
        ),
    )(parts)


def gather_blocks(values, axis):
    count = lax.axis_size("blk")
    stacked = jnp.broadcast_to(values[None], (count,) + values.shape)
    received = lax.all_to_all(stacked, "blk", split_axis=0, concat_axis=0, tiled=True)
    if axis == 0:
        return received.reshape((count * values.shape[0],) + values.shape[1:])
    return received.transpose(1, 0, 2).reshape(values.shape[0], count * values.shape[1])


def scatter_sum_blocks(values):
    count = lax.axis_size("blk")
    rows, width = values.shape
    pieces = values.reshape(rows, count, width // count).transpose(1, 0, 2)
    received = lax.all_to_all(pieces, "blk", split_axis=0, concat_axis=0, tiled=True)
    return jnp.sum(received, axis=0)


def per_device(
    hidden,
    attn_gain,
    qkv_weight,
    out_weight,
    kv_pool,
    page_table,
    cache_lens,
    ffn_gain,
    route_ids,
    route_weights,
    shared_gate_up,
    shared_down,
    expert_gate_up,
    expert_down,
):
    blocks = lax.axis_size("blk")
    groups = lax.axis_size("exp")
    block_index = lax.axis_index("blk")
    model_width = hidden.shape[1] * blocks
    query_width = HEADS * HEAD_DIM
    key_width = KV_HEADS * HEAD_DIM
    group_size = HEADS // KV_HEADS
    own_rows = NEW // blocks
    full_rows = gather_blocks(hidden, 1)
    attn_in = normalize(full_rows, attn_gain)
    projected = jnp.dot(attn_in, qkv_weight, preferred_element_type=jnp.float32).astype(
        jnp.bfloat16
    )
    projected_all = gather_blocks(projected, 1)
    length = cache_lens[0]
    positions = length + jnp.arange(NEW, dtype=jnp.int32)
    fresh_keys = rotate(
        projected_all[:, query_width : query_width + key_width]
        .astype(jnp.float32)
        .reshape(NEW, KV_HEADS, HEAD_DIM),
        positions,
    ).astype(jnp.bfloat16)
    appended = jnp.concatenate(
        [fresh_keys.reshape(NEW, key_width), projected_all[:, query_width + key_width :]], axis=1
    )
    page_map = page_table[0]
    pool_pages = page_map.shape[0]
    page_index = jnp.arange(pool_pages, dtype=jnp.int32)
    logical = jnp.sum(
        jnp.where(page_map[None, :] == page_index[:, None], page_index[None, :], 0), axis=1
    )
    local_pages = kv_pool.shape[1]
    local_logical = lax.dynamic_slice_in_dim(logical, block_index * local_pages, local_pages)
    slot_offsets = jnp.arange(PAGE, dtype=jnp.int32)
    local_pos = local_logical[:, None] * PAGE + slot_offsets[None, :]
    offset = local_pos - length
    written = (offset >= 0) & (offset < NEW)
    picked = appended[jnp.clip(offset, 0, NEW - 1)]
    pool_out = jnp.where(written[:, :, None], picked, kv_pool[0])
    half_dim = HEAD_DIM // 2
    frequency = rope_base ** (-(jnp.arange(half_dim).astype(jnp.float32) * 2.0 / HEAD_DIM))
    angles = positions.astype(jnp.float32)[:, None] * frequency[None, :]
    cosine = jnp.cos(angles)
    sine_vals = jnp.sin(angles)
    cosine_full = jnp.concatenate([cosine, cosine], axis=1)
    sine_signed = jnp.concatenate([-sine_vals, sine_vals], axis=1)
    slot_rows = pool_out.reshape(local_pages * PAGE, 2 * key_width)
    payload = local_attention(
        projected_all, cosine_full, sine_signed, slot_rows, positions, local_pos.reshape(-1)
    ).reshape(blocks, own_rows, query_width + 128)
    gathered = lax.all_to_all(payload, "blk", split_axis=0, concat_axis=0, tiled=True)
    own_attention = combine_attention(gathered)
    attended = jnp.dot(
        gather_blocks(own_attention, 0),
        out_weight,
        preferred_element_type=jnp.float32,
    )
    mixed_cols = (hidden.astype(jnp.float32) + attended).astype(jnp.bfloat16)
    mixed_rows = gather_blocks(mixed_cols, 1)
    ffn_in = normalize(mixed_rows, ffn_gain)
    shared_cols = shared_gate_up.shape[2]
    gate_up = jnp.dot(
        ffn_in,
        shared_gate_up.reshape(model_width, 2 * shared_cols),
        preferred_element_type=jnp.float32,
    )
    shared_act = (jax.nn.silu(gate_up[:, :shared_cols]) * gate_up[:, shared_cols:]).astype(
        jnp.bfloat16
    )
    shared_term = jnp.dot(shared_act, shared_down, preferred_element_type=jnp.float32)
    row_experts = groups // SPLIT
    expert_count = row_experts * blocks
    capacity = NEW * TOPK * 4 // (expert_count * 3)
    row_expert_ids = block_index * row_experts + jnp.arange(row_experts, dtype=jnp.int32)
    route_hits = route_ids[:, :, None] == row_expert_ids[None, None, :]
    chosen = jnp.any(route_hits, axis=1)
    route_share = jnp.sum(jnp.where(route_hits, route_weights[:, :, None], 0.0), axis=1)
    slot_rank = jnp.cumsum(chosen.astype(jnp.int32), axis=0) - 1
    slot_ids = jnp.arange(capacity, dtype=jnp.int32)
    placed = chosen.T[:, None, :] & (slot_rank.T[:, None, :] == slot_ids[None, :, None])
    selector = placed.astype(jnp.bfloat16)
    outgoing = jnp.einsum(
        "ect,td->ecd", selector, ffn_in, preferred_element_type=jnp.float32
    ).astype(jnp.bfloat16)
    outgoing = jnp.repeat(outgoing, SPLIT, axis=0)
    received = lax.all_to_all(outgoing, "exp", split_axis=0, concat_axis=0, tiled=True)
    flat_rows = received.reshape(-1, model_width)
    expert_gu = jnp.dot(flat_rows, expert_gate_up[0], preferred_element_type=jnp.float32)
    activated = (jax.nn.silu(expert_gu[:, :FF_PART]) * expert_gu[:, FF_PART:]).astype(jnp.bfloat16)
    result = jnp.dot(activated, expert_down[0], preferred_element_type=jnp.float32).astype(
        jnp.bfloat16
    )
    returned = lax.all_to_all(
        result.reshape(received.shape), "exp", split_axis=0, concat_axis=0, tiled=True
    )
    summed = jnp.sum(
        returned.reshape(row_experts, SPLIT, capacity, model_width).astype(jnp.float32), axis=1
    )
    slot_weight = jnp.sum(placed.astype(jnp.float32) * route_share.T[:, None, :], axis=2)
    slot_values = summed * slot_weight[:, :, None]
    upper_part = slot_values.astype(jnp.bfloat16)
    lower_part = (slot_values - upper_part.astype(jnp.float32)).astype(jnp.bfloat16)
    routed = jnp.einsum(
        "ect,ecd->td", selector, upper_part, preferred_element_type=jnp.float32
    ) + jnp.einsum("ect,ecd->td", selector, lower_part, preferred_element_type=jnp.float32)
    layer_term = shared_term + routed
    summed_cols = scatter_sum_blocks(layer_term)
    hidden_out = (mixed_cols.astype(jnp.float32) + summed_cols).astype(jnp.bfloat16)
    return (hidden_out, pool_out[None])


def solution(mesh):
    placed = (
        P("exp", "blk"),
        P(),
        P(None, "blk"),
        P(None, "blk"),
        P("exp", "blk", None, None),
        P("exp", None),
        P("exp"),
        P(),
        P("exp", None),
        P("exp", None),
        P(None, None, "blk"),
        P("blk", None),
        P(("blk", "exp"), None, None),
        P(("blk", "exp"), None, None),
    )
    return jax.shard_map(
        per_device,
        mesh=mesh,
        in_specs=placed,
        out_specs=(P("exp", "blk"), P("exp", "blk", None, None)),
        check_vma=False,
    )
```

```python
import math

import jax
import jax.numpy as jnp
from jax import lax
from jax.experimental import pallas as pl
from jax.experimental.pallas import tpu as pltpu
from jax.sharding import PartitionSpec as P

HEADS = 20
KV_HEADS = 4
HEAD_DIM = 128
TOPK = 6
SPLIT = 4
PAGE = 128
NEW = 256
FF_PART = 384


rope_base = 500000.0
norm_eps = 1e-05


def normalize(inputs, gain_vec):
    values = inputs.astype(jnp.float32)
    inv_rms = lax.rsqrt(jnp.mean(values * values, axis=-1, keepdims=True) + norm_eps)
    return (values * inv_rms * gain_vec).astype(jnp.bfloat16)


def rotate(inputs, positions):
    half_dim = HEAD_DIM // 2
    frequency = rope_base ** (-(jnp.arange(half_dim).astype(jnp.float32) * 2.0 / HEAD_DIM))
    angles = positions.astype(jnp.float32)[:, None] * frequency[None, :]
    cosine = jnp.cos(angles)[:, None, :]
    sine_vals = jnp.sin(angles)[:, None, :]
    lower_half = inputs[..., :half_dim]
    upper_half = inputs[..., half_dim:]
    return jnp.concatenate(
        [
            lower_half * cosine - upper_half * sine_vals,
            upper_half * cosine + lower_half * sine_vals,
        ],
        axis=-1,
    )


def split_three(value):
    high = value.astype(jnp.bfloat16).astype(jnp.float32)
    rest = value - high
    middle = rest.astype(jnp.bfloat16).astype(jnp.float32)
    low = (rest - middle).astype(jnp.bfloat16).astype(jnp.float32)
    return [high, middle, low]


def attention_kernel(proj_ref, cos_ref, sin_ref, slot_ref, qpos_ref, kpos_ref, out_ref):
    key_width = KV_HEADS * HEAD_DIM
    group_size = HEADS // KV_HEADS
    allowed = kpos_ref[...] <= qpos_ref[...]
    cosine = cos_ref[...]
    sine_signed = sin_ref[...]
    lane = lax.broadcasted_iota(jnp.int32, (NEW, 128), 1)
    stats = jnp.zeros((NEW, 128), jnp.float32)
    for head in range(HEADS):
        kv = head // group_size
        raw = proj_ref[:, head * HEAD_DIM : (head + 1) * HEAD_DIM].astype(jnp.float32)
        swapped = pltpu.roll(raw, HEAD_DIM // 2, 1)
        query = (raw * cosine + swapped * sine_signed).astype(jnp.bfloat16)
        keys = slot_ref[:, kv * HEAD_DIM : (kv + 1) * HEAD_DIM]
        values = slot_ref[:, key_width + kv * HEAD_DIM : key_width + (kv + 1) * HEAD_DIM]
        scores = lax.dot_general(
            query, keys, (((1,), (1,)), ((), ())), preferred_element_type=jnp.float32
        ) * (1.0 / math.sqrt(HEAD_DIM))
        scores = jnp.where(allowed, scores, -1e30)
        peak = jnp.max(scores, axis=1, keepdims=True)
        probs = jnp.where(allowed, jnp.exp(scores - peak), 0.0)
        total = jnp.sum(probs, axis=1, keepdims=True)
        out_ref[:, head * HEAD_DIM : (head + 1) * HEAD_DIM] = jnp.dot(
            probs.astype(jnp.bfloat16), values, preferred_element_type=jnp.float32
        ).astype(out_ref.dtype)
        for slot, value in enumerate(split_three(peak) + split_three(total)):
            stats = jnp.where(lane == slot * HEADS + head, value, stats)
    out_ref[:, HEADS * HEAD_DIM :] = stats.astype(out_ref.dtype)


def local_attention(projected_all, cosine, sine_signed, slot_rows, positions, key_pos):
    width = HEADS * HEAD_DIM + 128
    return pl.pallas_call(
        attention_kernel,
        out_shape=jax.ShapeDtypeStruct((NEW, width), jnp.bfloat16),
        in_specs=[pl.BlockSpec(memory_space=pltpu.VMEM)] * 6,
        out_specs=pl.BlockSpec(memory_space=pltpu.VMEM),
        cost_estimate=pl.CostEstimate(
            flops=4 * NEW * slot_rows.shape[0] * HEAD_DIM * HEADS,
            transcendentals=NEW * slot_rows.shape[0] * HEADS,
            bytes_accessed=NEW * width * 2 + slot_rows.size * 2 + projected_all.size * 2,
        ),
    )(projected_all, cosine, sine_signed, slot_rows, positions[:, None], key_pos[None, :])


def combine_kernel(part_ref, out_ref):
    coded = part_ref[:, :, HEADS * HEAD_DIM :].astype(jnp.float32)
    lane = lax.broadcasted_iota(jnp.int32, coded.shape, 2)

    def pick(slot):
        return jnp.sum(jnp.where(lane == slot, coded, 0.0), axis=2, keepdims=True)

    for head in range(HEADS):
        peak = (pick(head) + pick(HEADS + head)) + pick(2 * HEADS + head)
        total = (pick(3 * HEADS + head) + pick(4 * HEADS + head)) + pick(5 * HEADS + head)
        factor = jnp.exp(peak - jnp.max(peak, axis=0, keepdims=True))
        denominator = jnp.sum(factor * total, axis=0)
        numerator = jnp.sum(
            part_ref[:, :, head * HEAD_DIM : (head + 1) * HEAD_DIM].astype(jnp.float32) * factor,
            axis=0,
        )
        out_ref[:, head * HEAD_DIM : (head + 1) * HEAD_DIM] = (
            numerator / denominator
        ).astype(out_ref.dtype)


def combine_attention(parts):
    sources, rows, width = parts.shape
    return pl.pallas_call(
        combine_kernel,
        out_shape=jax.ShapeDtypeStruct((rows, HEADS * HEAD_DIM), jnp.bfloat16),
        in_specs=[pl.BlockSpec(memory_space=pltpu.VMEM)],
        out_specs=pl.BlockSpec(memory_space=pltpu.VMEM),
        cost_estimate=pl.CostEstimate(
            flops=3 * parts.size, transcendentals=sources * rows * 128,
            bytes_accessed=parts.size * 2 + rows * HEADS * HEAD_DIM * 2,
        ),
    )(parts)


def gather_blocks(values, axis):
    count = lax.axis_size("blk")
    stacked = jnp.broadcast_to(values[None], (count,) + values.shape)
    received = lax.all_to_all(stacked, "blk", split_axis=0, concat_axis=0, tiled=True)
    if axis == 0:
        return received.reshape((count * values.shape[0],) + values.shape[1:])
    return received.transpose(1, 0, 2).reshape(values.shape[0], count * values.shape[1])


def scatter_sum_blocks(values):
    count = lax.axis_size("blk")
    rows, width = values.shape
    pieces = values.reshape(rows, count, width // count).transpose(1, 0, 2)
    received = lax.all_to_all(
        pieces.astype(jnp.bfloat16), "blk", split_axis=0, concat_axis=0, tiled=True
    )
    return jnp.sum(received.astype(jnp.float32), axis=0)


def per_device(
    hidden,
    attn_gain,
    qkv_weight,
    out_weight,
    kv_pool,
    page_table,
    cache_lens,
    ffn_gain,
    route_ids,
    route_weights,
    shared_gate_up,
    shared_down,
    expert_gate_up,
    expert_down,
):
    blocks = lax.axis_size("blk")
    groups = lax.axis_size("exp")
    block_index = lax.axis_index("blk")
    model_width = hidden.shape[1] * blocks
    query_width = HEADS * HEAD_DIM
    key_width = KV_HEADS * HEAD_DIM
    group_size = HEADS // KV_HEADS
    own_rows = NEW // blocks
    full_rows = gather_blocks(hidden, 1)
    attn_in = normalize(full_rows, attn_gain)
    projected = jnp.dot(attn_in, qkv_weight, preferred_element_type=jnp.float32).astype(
        jnp.bfloat16
    )
    projected_all = gather_blocks(projected, 1)
    length = cache_lens[0]
    positions = length + jnp.arange(NEW, dtype=jnp.int32)
    fresh_keys = rotate(
        projected_all[:, query_width : query_width + key_width]
        .astype(jnp.float32)
        .reshape(NEW, KV_HEADS, HEAD_DIM),
        positions,
    ).astype(jnp.bfloat16)
    appended = jnp.concatenate(
        [fresh_keys.reshape(NEW, key_width), projected_all[:, query_width + key_width :]], axis=1
    )
    page_map = page_table[0]
    pool_pages = page_map.shape[0]
    page_index = jnp.arange(pool_pages, dtype=jnp.int32)
    logical = jnp.sum(
        jnp.where(page_map[None, :] == page_index[:, None], page_index[None, :], 0), axis=1
    )
    local_pages = kv_pool.shape[1]
    local_logical = lax.dynamic_slice_in_dim(logical, block_index * local_pages, local_pages)
    slot_offsets = jnp.arange(PAGE, dtype=jnp.int32)
    local_pos = local_logical[:, None] * PAGE + slot_offsets[None, :]
    offset = local_pos - length
    written = (offset >= 0) & (offset < NEW)
    picked = appended[jnp.clip(offset, 0, NEW - 1)]
    pool_out = jnp.where(written[:, :, None], picked, kv_pool[0])
    half_dim = HEAD_DIM // 2
    frequency = rope_base ** (-(jnp.arange(half_dim).astype(jnp.float32) * 2.0 / HEAD_DIM))
    angles = positions.astype(jnp.float32)[:, None] * frequency[None, :]
    cosine = jnp.cos(angles)
    sine_vals = jnp.sin(angles)
    cosine_full = jnp.concatenate([cosine, cosine], axis=1)
    sine_signed = jnp.concatenate([-sine_vals, sine_vals], axis=1)
    slot_rows = pool_out.reshape(local_pages * PAGE, 2 * key_width)
    payload = local_attention(
        projected_all, cosine_full, sine_signed, slot_rows, positions, local_pos.reshape(-1)
    ).reshape(blocks, own_rows, query_width + 128)
    gathered = lax.all_to_all(payload, "blk", split_axis=0, concat_axis=0, tiled=True)
    own_attention = combine_attention(gathered)
    attended = jnp.dot(
        gather_blocks(own_attention, 0),
        out_weight,
        preferred_element_type=jnp.float32,
    )
    mixed_cols = (hidden.astype(jnp.float32) + attended).astype(jnp.bfloat16)
    mixed_rows = gather_blocks(mixed_cols, 1)
    ffn_in = normalize(mixed_rows, ffn_gain)
    shared_cols = shared_gate_up.shape[2]
    gate_up = jnp.dot(
        ffn_in,
        shared_gate_up.reshape(model_width, 2 * shared_cols),
        preferred_element_type=jnp.float32,
    )
    shared_act = (jax.nn.silu(gate_up[:, :shared_cols]) * gate_up[:, shared_cols:]).astype(
        jnp.bfloat16
    )
    shared_term = jnp.dot(shared_act, shared_down, preferred_element_type=jnp.float32)
    row_experts = groups // SPLIT
    expert_count = row_experts * blocks
    capacity = NEW * TOPK * 4 // (expert_count * 3)
    row_expert_ids = block_index * row_experts + jnp.arange(row_experts, dtype=jnp.int32)
    route_hits = route_ids[:, :, None] == row_expert_ids[None, None, :]
    chosen = jnp.any(route_hits, axis=1)
    route_share = jnp.sum(jnp.where(route_hits, route_weights[:, :, None], 0.0), axis=1)
    slot_rank = jnp.cumsum(chosen.astype(jnp.int32), axis=0) - 1
    slot_ids = jnp.arange(capacity, dtype=jnp.int32)
    placed = chosen.T[:, None, :] & (slot_rank.T[:, None, :] == slot_ids[None, :, None])
    selector = placed.astype(jnp.bfloat16)
    outgoing = jnp.einsum(
        "ect,td->ecd", selector, ffn_in, preferred_element_type=jnp.float32
    ).astype(jnp.bfloat16)
    outgoing = jnp.repeat(outgoing, SPLIT, axis=0)
    received = lax.all_to_all(outgoing, "exp", split_axis=0, concat_axis=0, tiled=True)
    flat_rows = received.reshape(-1, model_width)
    expert_gu = jnp.dot(flat_rows, expert_gate_up[0], preferred_element_type=jnp.float32)
    activated = (jax.nn.silu(expert_gu[:, :FF_PART]) * expert_gu[:, FF_PART:]).astype(jnp.bfloat16)
    result = jnp.dot(activated, expert_down[0], preferred_element_type=jnp.float32).astype(
        jnp.bfloat16
    )
    returned = lax.all_to_all(
        result.reshape(received.shape), "exp", split_axis=0, concat_axis=0, tiled=True
    )
    summed = jnp.sum(
        returned.reshape(row_experts, SPLIT, capacity, model_width).astype(jnp.float32), axis=1
    )
    slot_weight = jnp.sum(placed.astype(jnp.float32) * route_share.T[:, None, :], axis=2)
    slot_values = summed * slot_weight[:, :, None]
    upper_part = slot_values.astype(jnp.bfloat16)
    lower_part = (slot_values - upper_part.astype(jnp.float32)).astype(jnp.bfloat16)
    routed = jnp.einsum(
        "ect,ecd->td", selector, upper_part, preferred_element_type=jnp.float32
    ) + jnp.einsum("ect,ecd->td", selector, lower_part, preferred_element_type=jnp.float32)
    layer_term = shared_term + routed
    summed_cols = scatter_sum_blocks(layer_term)
    hidden_out = (mixed_cols.astype(jnp.float32) + summed_cols).astype(jnp.bfloat16)
    return (hidden_out, pool_out[None])


def solution(mesh):
    placed = (
        P("exp", "blk"),
        P(),
        P(None, "blk"),
        P(None, "blk"),
        P("exp", "blk", None, None),
        P("exp", None),
        P("exp"),
        P(),
        P("exp", None),
        P("exp", None),
        P(None, None, "blk"),
        P("blk", None),
        P(("blk", "exp"), None, None),
        P(("blk", "exp"), None, None),
    )
    return jax.shard_map(
        per_device,
        mesh=mesh,
        in_specs=placed,
        out_specs=(P("exp", "blk"), P("exp", "blk", None, None)),
        check_vma=False,
    )
```

```python
import math

import jax
import jax.numpy as jnp
from jax import lax
from jax.experimental import pallas as pl
from jax.experimental.pallas import tpu as pltpu
from jax.sharding import PartitionSpec as P

HEADS = 20
KV_HEADS = 4
HEAD_DIM = 128
TOPK = 6
SPLIT = 4
PAGE = 128
NEW = 256
FF_PART = 384


rope_base = 500000.0
norm_eps = 1e-05


def normalize(inputs, gain_vec):
    values = inputs.astype(jnp.float32)
    inv_rms = lax.rsqrt(jnp.mean(values * values, axis=-1, keepdims=True) + norm_eps)
    return (values * inv_rms * gain_vec).astype(jnp.bfloat16)


def rotate(inputs, positions):
    half_dim = HEAD_DIM // 2
    frequency = rope_base ** (-(jnp.arange(half_dim).astype(jnp.float32) * 2.0 / HEAD_DIM))
    angles = positions.astype(jnp.float32)[:, None] * frequency[None, :]
    cosine = jnp.cos(angles)[:, None, :]
    sine_vals = jnp.sin(angles)[:, None, :]
    lower_half = inputs[..., :half_dim]
    upper_half = inputs[..., half_dim:]
    return jnp.concatenate(
        [
            lower_half * cosine - upper_half * sine_vals,
            upper_half * cosine + lower_half * sine_vals,
        ],
        axis=-1,
    )


def split_three(value):
    high = value.astype(jnp.bfloat16).astype(jnp.float32)
    rest = value - high
    middle = rest.astype(jnp.bfloat16).astype(jnp.float32)
    low = (rest - middle).astype(jnp.bfloat16).astype(jnp.float32)
    return [high, middle, low]


def attention_kernel(proj_ref, cos_ref, sin_ref, slot_ref, qpos_ref, kpos_ref, out_ref):
    key_width = KV_HEADS * HEAD_DIM
    group_size = HEADS // KV_HEADS
    allowed = kpos_ref[...] <= qpos_ref[...]
    cosine = cos_ref[...]
    sine_signed = sin_ref[...]
    lane = lax.broadcasted_iota(jnp.int32, (NEW, 128), 1)
    stats = jnp.zeros((NEW, 128), jnp.float32)
    for head in range(HEADS):
        kv = head // group_size
        raw = proj_ref[:, head * HEAD_DIM : (head + 1) * HEAD_DIM].astype(jnp.float32)
        swapped = pltpu.roll(raw, HEAD_DIM // 2, 1)
        query = (raw * cosine + swapped * sine_signed).astype(jnp.bfloat16)
        keys = slot_ref[:, kv * HEAD_DIM : (kv + 1) * HEAD_DIM]
        values = slot_ref[:, key_width + kv * HEAD_DIM : key_width + (kv + 1) * HEAD_DIM]
        scores = lax.dot_general(
            query, keys, (((1,), (1,)), ((), ())), preferred_element_type=jnp.float32
        ) * (1.0 / math.sqrt(HEAD_DIM))
        scores = jnp.where(allowed, scores, -1e30)
        peak = jnp.max(scores, axis=1, keepdims=True)
        probs = jnp.where(allowed, jnp.exp(scores - peak), 0.0)
        total = jnp.sum(probs, axis=1, keepdims=True)
        out_ref[:, head * HEAD_DIM : (head + 1) * HEAD_DIM] = jnp.dot(
            probs.astype(jnp.bfloat16), values, preferred_element_type=jnp.float32
        ).astype(out_ref.dtype)
        for slot, value in enumerate(split_three(peak) + split_three(total)):
            stats = jnp.where(lane == slot * HEADS + head, value, stats)
    out_ref[:, HEADS * HEAD_DIM :] = stats.astype(out_ref.dtype)


def local_attention(projected_all, cosine, sine_signed, slot_rows, positions, key_pos):
    width = HEADS * HEAD_DIM + 128
    return pl.pallas_call(
        attention_kernel,
        out_shape=jax.ShapeDtypeStruct((NEW, width), jnp.bfloat16),
        in_specs=[pl.BlockSpec(memory_space=pltpu.VMEM)] * 6,
        out_specs=pl.BlockSpec(memory_space=pltpu.VMEM),
        cost_estimate=pl.CostEstimate(
            flops=4 * NEW * slot_rows.shape[0] * HEAD_DIM * HEADS,
            transcendentals=NEW * slot_rows.shape[0] * HEADS,
            bytes_accessed=NEW * width * 2 + slot_rows.size * 2 + projected_all.size * 2,
        ),
    )(projected_all, cosine, sine_signed, slot_rows, positions[:, None], key_pos[None, :])


def combine_kernel(part_ref, out_ref):
    coded = part_ref[:, :, HEADS * HEAD_DIM :].astype(jnp.float32)
    lane = lax.broadcasted_iota(jnp.int32, coded.shape, 2)

    def pick(slot):
        return jnp.sum(jnp.where(lane == slot, coded, 0.0), axis=2, keepdims=True)

    for head in range(HEADS):
        peak = (pick(head) + pick(HEADS + head)) + pick(2 * HEADS + head)
        total = (pick(3 * HEADS + head) + pick(4 * HEADS + head)) + pick(5 * HEADS + head)
        factor = jnp.exp(peak - jnp.max(peak, axis=0, keepdims=True))
        denominator = jnp.sum(factor * total, axis=0)
        numerator = jnp.sum(
            part_ref[:, :, head * HEAD_DIM : (head + 1) * HEAD_DIM].astype(jnp.float32) * factor,
            axis=0,
        )
        out_ref[:, head * HEAD_DIM : (head + 1) * HEAD_DIM] = (
            numerator / denominator
        ).astype(out_ref.dtype)


def combine_attention(parts):
    sources, rows, width = parts.shape
    return pl.pallas_call(
        combine_kernel,
        out_shape=jax.ShapeDtypeStruct((rows, HEADS * HEAD_DIM), jnp.bfloat16),
        in_specs=[pl.BlockSpec(memory_space=pltpu.VMEM)],
        out_specs=pl.BlockSpec(memory_space=pltpu.VMEM),
        cost_estimate=pl.CostEstimate(
            flops=3 * parts.size, transcendentals=sources * rows * 128,
            bytes_accessed=parts.size * 2 + rows * HEADS * HEAD_DIM * 2,
        ),
    )(parts)


def gather_blocks(values, axis):
    count = lax.axis_size("blk")
    stacked = jnp.broadcast_to(values[None], (count,) + values.shape)
    received = lax.all_to_all(stacked, "blk", split_axis=0, concat_axis=0, tiled=True)
    if axis == 0:
        return received.reshape((count * values.shape[0],) + values.shape[1:])
    return received.transpose(1, 0, 2).reshape(values.shape[0], count * values.shape[1])


def scatter_sum_blocks(values):
    count = lax.axis_size("blk")
    rows, width = values.shape
    pieces = values.reshape(rows, count, width // count).transpose(1, 0, 2)
    received = lax.all_to_all(
        pieces.astype(jnp.bfloat16), "blk", split_axis=0, concat_axis=0, tiled=True
    )
    return jnp.sum(received.astype(jnp.float32), axis=0)


def per_device(
    hidden,
    attn_gain,
    qkv_weight,
    out_weight,
    kv_pool,
    page_table,
    cache_lens,
    ffn_gain,
    route_ids,
    route_weights,
    shared_gate_up,
    shared_down,
    expert_gate_up,
    expert_down,
):
    blocks = lax.axis_size("blk")
    groups = lax.axis_size("exp")
    block_index = lax.axis_index("blk")
    model_width = hidden.shape[1] * blocks
    query_width = HEADS * HEAD_DIM
    key_width = KV_HEADS * HEAD_DIM
    group_size = HEADS // KV_HEADS
    own_rows = NEW // blocks
    full_rows = gather_blocks(hidden, 1)
    attn_in = normalize(full_rows, attn_gain)
    projected = jnp.dot(attn_in, qkv_weight, preferred_element_type=jnp.float32).astype(
        jnp.bfloat16
    )
    projected_all = gather_blocks(projected, 1)
    length = cache_lens[0]
    positions = length + jnp.arange(NEW, dtype=jnp.int32)
    fresh_keys = rotate(
        projected_all[:, query_width : query_width + key_width]
        .astype(jnp.float32)
        .reshape(NEW, KV_HEADS, HEAD_DIM),
        positions,
    ).astype(jnp.bfloat16)
    appended = jnp.concatenate(
        [fresh_keys.reshape(NEW, key_width), projected_all[:, query_width + key_width :]], axis=1
    )
    page_map = page_table[0]
    pool_pages = page_map.shape[0]
    page_index = jnp.arange(pool_pages, dtype=jnp.int32)
    logical = jnp.sum(
        jnp.where(page_map[None, :] == page_index[:, None], page_index[None, :], 0), axis=1
    )
    local_pages = kv_pool.shape[1]
    local_logical = lax.dynamic_slice_in_dim(logical, block_index * local_pages, local_pages)
    slot_offsets = jnp.arange(PAGE, dtype=jnp.int32)
    local_pos = local_logical[:, None] * PAGE + slot_offsets[None, :]
    offset = local_pos - length
    written = (offset >= 0) & (offset < NEW)
    picked = appended[jnp.clip(offset, 0, NEW - 1)]
    pool_out = jnp.where(written[:, :, None], picked, kv_pool[0])
    half_dim = HEAD_DIM // 2
    frequency = rope_base ** (-(jnp.arange(half_dim).astype(jnp.float32) * 2.0 / HEAD_DIM))
    angles = positions.astype(jnp.float32)[:, None] * frequency[None, :]
    cosine = jnp.cos(angles)
    sine_vals = jnp.sin(angles)
    cosine_full = jnp.concatenate([cosine, cosine], axis=1)
    sine_signed = jnp.concatenate([-sine_vals, sine_vals], axis=1)
    slot_rows = pool_out.reshape(local_pages * PAGE, 2 * key_width)
    payload = local_attention(
        projected_all, cosine_full, sine_signed, slot_rows, positions, local_pos.reshape(-1)
    ).reshape(blocks, own_rows, query_width + 128)
    gathered = lax.all_to_all(payload, "blk", split_axis=0, concat_axis=0, tiled=True)
    own_attention = combine_attention(gathered)
    attended = jnp.dot(
        gather_blocks(own_attention, 0),
        out_weight,
        preferred_element_type=jnp.float32,
    )
    mixed_cols = (hidden.astype(jnp.float32) + attended).astype(jnp.bfloat16)
    mixed_rows = gather_blocks(mixed_cols, 1)
    ffn_in = normalize(mixed_rows, ffn_gain)
    shared_cols = shared_gate_up.shape[2]
    gate_up = jnp.dot(
        ffn_in,
        shared_gate_up.reshape(model_width, 2 * shared_cols),
        preferred_element_type=jnp.float32,
    )
    shared_act = (jax.nn.silu(gate_up[:, :shared_cols]) * gate_up[:, shared_cols:]).astype(
        jnp.bfloat16
    )
    shared_term = jnp.dot(shared_act, shared_down, preferred_element_type=jnp.float32)
    row_experts = groups // SPLIT
    expert_count = row_experts * blocks
    capacity = NEW * TOPK * 4 // (expert_count * 3)
    row_expert_ids = block_index * row_experts + jnp.arange(row_experts, dtype=jnp.int32)
    route_hits = route_ids[:, :, None] == row_expert_ids[None, None, :]
    chosen = jnp.any(route_hits, axis=1)
    route_share = jnp.sum(jnp.where(route_hits, route_weights[:, :, None], 0.0), axis=1)
    slot_rank = jnp.cumsum(chosen.astype(jnp.int32), axis=0) - 1
    slot_ids = jnp.arange(capacity, dtype=jnp.int32)
    placed = chosen.T[:, None, :] & (slot_rank.T[:, None, :] == slot_ids[None, :, None])
    selector = placed.astype(jnp.bfloat16)
    outgoing = jnp.einsum(
        "ect,td->ecd", selector, ffn_in, preferred_element_type=jnp.float32
    ).astype(jnp.bfloat16)
    outgoing = jnp.repeat(outgoing, SPLIT, axis=0)
    received = lax.all_to_all(outgoing, "exp", split_axis=0, concat_axis=0, tiled=True)
    received, shared_term = lax.optimization_barrier((received, shared_term))
    flat_rows = received.reshape(-1, model_width)
    expert_gu = jnp.dot(flat_rows, expert_gate_up[0], preferred_element_type=jnp.float32)
    activated = (jax.nn.silu(expert_gu[:, :FF_PART]) * expert_gu[:, FF_PART:]).astype(jnp.bfloat16)
    result = jnp.dot(activated, expert_down[0], preferred_element_type=jnp.float32).astype(
        jnp.bfloat16
    )
    returned = lax.all_to_all(
        result.reshape(received.shape), "exp", split_axis=0, concat_axis=0, tiled=True
    )
    summed = jnp.sum(
        returned.reshape(row_experts, SPLIT, capacity, model_width).astype(jnp.float32), axis=1
    )
    slot_weight = jnp.sum(placed.astype(jnp.float32) * route_share.T[:, None, :], axis=2)
    slot_values = summed * slot_weight[:, :, None]
    upper_part = slot_values.astype(jnp.bfloat16)
    lower_part = (slot_values - upper_part.astype(jnp.float32)).astype(jnp.bfloat16)
    routed = jnp.einsum(
        "ect,ecd->td", selector, upper_part, preferred_element_type=jnp.float32
    ) + jnp.einsum("ect,ecd->td", selector, lower_part, preferred_element_type=jnp.float32)
    layer_term = shared_term + routed
    summed_cols = scatter_sum_blocks(layer_term)
    hidden_out = (mixed_cols.astype(jnp.float32) + summed_cols).astype(jnp.bfloat16)
    return (hidden_out, pool_out[None])


def solution(mesh):
    placed = (
        P("exp", "blk"),
        P(),
        P(None, "blk"),
        P(None, "blk"),
        P("exp", "blk", None, None),
        P("exp", None),
        P("exp"),
        P(),
        P("exp", None),
        P("exp", None),
        P(None, None, "blk"),
        P("blk", None),
        P(("blk", "exp"), None, None),
        P(("blk", "exp"), None, None),
    )
    return jax.shard_map(
        per_device,
        mesh=mesh,
        in_specs=placed,
        out_specs=(P("exp", "blk"), P("exp", "blk", None, None)),
        check_vma=False,
    )
```

```python
import math

import jax
import jax.numpy as jnp
from jax import lax
from jax.experimental import pallas as pl
from jax.experimental.pallas import tpu as pltpu
from jax.sharding import PartitionSpec as P

HEADS = 20
KV_HEADS = 4
HEAD_DIM = 128
TOPK = 6
SPLIT = 4
PAGE = 128
NEW = 256
FF_PART = 384


rope_base = 500000.0
norm_eps = 1e-05


def normalize(inputs, gain_vec):
    values = inputs.astype(jnp.float32)
    inv_rms = lax.rsqrt(jnp.mean(values * values, axis=-1, keepdims=True) + norm_eps)
    return (values * inv_rms * gain_vec).astype(jnp.bfloat16)


def rotate(inputs, positions):
    half_dim = HEAD_DIM // 2
    frequency = rope_base ** (-(jnp.arange(half_dim).astype(jnp.float32) * 2.0 / HEAD_DIM))
    angles = positions.astype(jnp.float32)[:, None] * frequency[None, :]
    cosine = jnp.cos(angles)[:, None, :]
    sine_vals = jnp.sin(angles)[:, None, :]
    lower_half = inputs[..., :half_dim]
    upper_half = inputs[..., half_dim:]
    return jnp.concatenate(
        [
            lower_half * cosine - upper_half * sine_vals,
            upper_half * cosine + lower_half * sine_vals,
        ],
        axis=-1,
    )


def split_three(value):
    high = value.astype(jnp.bfloat16).astype(jnp.float32)
    rest = value - high
    middle = rest.astype(jnp.bfloat16).astype(jnp.float32)
    low = (rest - middle).astype(jnp.bfloat16).astype(jnp.float32)
    return [high, middle, low]


def attention_kernel(proj_ref, cos_ref, sin_ref, slot_ref, qpos_ref, kpos_ref, out_ref):
    key_width = KV_HEADS * HEAD_DIM
    group_size = HEADS // KV_HEADS
    allowed = kpos_ref[...] <= qpos_ref[...]
    cosine = cos_ref[...]
    sine_signed = sin_ref[...]
    lane = lax.broadcasted_iota(jnp.int32, (NEW, 128), 1)
    stats = jnp.zeros((NEW, 128), jnp.float32)
    for head in range(HEADS):
        kv = head // group_size
        raw = proj_ref[:, head * HEAD_DIM : (head + 1) * HEAD_DIM].astype(jnp.float32)
        swapped = pltpu.roll(raw, HEAD_DIM // 2, 1)
        query = (raw * cosine + swapped * sine_signed).astype(jnp.bfloat16)
        keys = slot_ref[:, kv * HEAD_DIM : (kv + 1) * HEAD_DIM]
        values = slot_ref[:, key_width + kv * HEAD_DIM : key_width + (kv + 1) * HEAD_DIM]
        scores = lax.dot_general(
            query, keys, (((1,), (1,)), ((), ())), preferred_element_type=jnp.float32
        ) * (1.0 / math.sqrt(HEAD_DIM))
        scores = jnp.where(allowed, scores, -1e30)
        peak = jnp.max(scores, axis=1, keepdims=True)
        probs = jnp.exp(scores - peak)
        live = jnp.where(peak > -1e29, 1.0, 0.0)
        total = jnp.sum(probs, axis=1, keepdims=True) * live
        out_ref[:, head * HEAD_DIM : (head + 1) * HEAD_DIM] = (
            jnp.dot(probs.astype(jnp.bfloat16), values, preferred_element_type=jnp.float32) * live
        ).astype(out_ref.dtype)
        for slot, value in enumerate(split_three(peak) + split_three(total)):
            stats = jnp.where(lane == slot * HEADS + head, value, stats)
    out_ref[:, HEADS * HEAD_DIM :] = stats.astype(out_ref.dtype)


def local_attention(projected_all, cosine, sine_signed, slot_rows, positions, key_pos):
    width = HEADS * HEAD_DIM + 128
    return pl.pallas_call(
        attention_kernel,
        out_shape=jax.ShapeDtypeStruct((NEW, width), jnp.bfloat16),
        in_specs=[pl.BlockSpec(memory_space=pltpu.VMEM)] * 6,
        out_specs=pl.BlockSpec(memory_space=pltpu.VMEM),
        cost_estimate=pl.CostEstimate(
            flops=4 * NEW * slot_rows.shape[0] * HEAD_DIM * HEADS,
            transcendentals=NEW * slot_rows.shape[0] * HEADS,
            bytes_accessed=NEW * width * 2 + slot_rows.size * 2 + projected_all.size * 2,
        ),
    )(projected_all, cosine, sine_signed, slot_rows, positions[:, None], key_pos[None, :])


def combine_kernel(part_ref, out_ref):
    coded = part_ref[:, :, HEADS * HEAD_DIM :].astype(jnp.float32)
    lane_count = coded.shape[2]

    def shifted(piece):
        return pltpu.roll(coded, lane_count - piece * HEADS, 2)

    peak = (coded + shifted(1)) + shifted(2)
    total = (shifted(3) + shifted(4)) + shifted(5)
    factors = jnp.exp(peak - jnp.max(peak, axis=0, keepdims=True))
    denominators = jnp.sum(factors * total, axis=0)
    lane = lax.broadcasted_iota(jnp.int32, coded.shape, 2)
    for head in range(HEADS):
        factor = jnp.sum(jnp.where(lane == head, factors, 0.0), axis=2, keepdims=True)
        denominator = jnp.sum(jnp.where(lane[0] == head, denominators, 0.0), axis=1, keepdims=True)
        numerator = jnp.sum(
            part_ref[:, :, head * HEAD_DIM : (head + 1) * HEAD_DIM].astype(jnp.float32) * factor,
            axis=0,
        )
        out_ref[:, head * HEAD_DIM : (head + 1) * HEAD_DIM] = (
            numerator / denominator
        ).astype(out_ref.dtype)


def combine_attention(parts):
    sources, rows, width = parts.shape
    return pl.pallas_call(
        combine_kernel,
        out_shape=jax.ShapeDtypeStruct((rows, HEADS * HEAD_DIM), jnp.bfloat16),
        in_specs=[pl.BlockSpec(memory_space=pltpu.VMEM)],
        out_specs=pl.BlockSpec(memory_space=pltpu.VMEM),
        cost_estimate=pl.CostEstimate(
            flops=3 * parts.size, transcendentals=sources * rows * 128,
            bytes_accessed=parts.size * 2 + rows * HEADS * HEAD_DIM * 2,
        ),
    )(parts)


def gather_blocks(values, axis):
    count = lax.axis_size("blk")
    stacked = jnp.broadcast_to(values[None], (count,) + values.shape)
    received = lax.all_to_all(stacked, "blk", split_axis=0, concat_axis=axis + 1, tiled=True)
    return received.reshape(received.shape[1:])


def scatter_sum_blocks(values):
    count = lax.axis_size("blk")
    rows, width = values.shape
    pieces = values.reshape(rows, count, width // count).transpose(1, 0, 2)
    received = lax.all_to_all(
        pieces.astype(jnp.bfloat16), "blk", split_axis=0, concat_axis=0, tiled=True
    )
    return jnp.sum(received.astype(jnp.float32), axis=0)


def per_device(
    hidden,
    attn_gain,
    qkv_weight,
    out_weight,
    kv_pool,
    page_table,
    cache_lens,
    ffn_gain,
    route_ids,
    route_weights,
    shared_gate_up,
    shared_down,
    expert_gate_up,
    expert_down,
):
    blocks = lax.axis_size("blk")
    groups = lax.axis_size("exp")
    block_index = lax.axis_index("blk")
    model_width = hidden.shape[1] * blocks
    query_width = HEADS * HEAD_DIM
    key_width = KV_HEADS * HEAD_DIM
    group_size = HEADS // KV_HEADS
    own_rows = NEW // blocks
    full_rows = gather_blocks(hidden, 1)
    attn_in = normalize(full_rows, attn_gain)
    projected = jnp.dot(attn_in, qkv_weight, preferred_element_type=jnp.float32).astype(
        jnp.bfloat16
    )
    projected_all = gather_blocks(projected, 1)
    length = cache_lens[0]
    positions = length + jnp.arange(NEW, dtype=jnp.int32)
    fresh_keys = rotate(
        projected_all[:, query_width : query_width + key_width]
        .astype(jnp.float32)
        .reshape(NEW, KV_HEADS, HEAD_DIM),
        positions,
    ).astype(jnp.bfloat16)
    appended = jnp.concatenate(
        [fresh_keys.reshape(NEW, key_width), projected_all[:, query_width + key_width :]], axis=1
    )
    page_map = page_table[0]
    pool_pages = page_map.shape[0]
    page_index = jnp.arange(pool_pages, dtype=jnp.int32)
    logical = jnp.sum(
        jnp.where(page_map[None, :] == page_index[:, None], page_index[None, :], 0), axis=1
    )
    local_pages = kv_pool.shape[1]
    local_logical = lax.dynamic_slice_in_dim(logical, block_index * local_pages, local_pages)
    slot_offsets = jnp.arange(PAGE, dtype=jnp.int32)
    local_pos = local_logical[:, None] * PAGE + slot_offsets[None, :]
    offset = local_pos - length
    written = (offset >= 0) & (offset < NEW)
    picked = appended[jnp.clip(offset, 0, NEW - 1)]
    pool_out = jnp.where(written[:, :, None], picked, kv_pool[0])
    half_dim = HEAD_DIM // 2
    frequency = rope_base ** (-(jnp.arange(half_dim).astype(jnp.float32) * 2.0 / HEAD_DIM))
    angles = positions.astype(jnp.float32)[:, None] * frequency[None, :]
    cosine = jnp.cos(angles)
    sine_vals = jnp.sin(angles)
    cosine_full = jnp.concatenate([cosine, cosine], axis=1)
    sine_signed = jnp.concatenate([-sine_vals, sine_vals], axis=1)
    slot_rows = pool_out.reshape(local_pages * PAGE, 2 * key_width)
    payload = local_attention(
        projected_all, cosine_full, sine_signed, slot_rows, positions, local_pos.reshape(-1)
    ).reshape(blocks, own_rows, query_width + 128)
    gathered = lax.all_to_all(payload, "blk", split_axis=0, concat_axis=0, tiled=True)
    own_attention = combine_attention(gathered)
    attended = jnp.dot(
        gather_blocks(own_attention, 0),
        out_weight,
        preferred_element_type=jnp.float32,
    )
    mixed_cols = (hidden.astype(jnp.float32) + attended).astype(jnp.bfloat16)
    mixed_rows = gather_blocks(mixed_cols, 1)
    ffn_in = normalize(mixed_rows, ffn_gain)
    shared_cols = shared_gate_up.shape[2]
    gate_up = jnp.dot(
        ffn_in,
        shared_gate_up.reshape(model_width, 2 * shared_cols),
        preferred_element_type=jnp.float32,
    )
    shared_act = (jax.nn.silu(gate_up[:, :shared_cols]) * gate_up[:, shared_cols:]).astype(
        jnp.bfloat16
    )
    shared_term = jnp.dot(shared_act, shared_down, preferred_element_type=jnp.float32)
    row_experts = groups // SPLIT
    expert_count = row_experts * blocks
    capacity = NEW * TOPK * 4 // (expert_count * 3)
    row_expert_ids = block_index * row_experts + jnp.arange(row_experts, dtype=jnp.int32)
    route_hits = route_ids[:, :, None] == row_expert_ids[None, None, :]
    chosen = jnp.any(route_hits, axis=1)
    route_share = jnp.sum(jnp.where(route_hits, route_weights[:, :, None], 0.0), axis=1)
    slot_rank = jnp.cumsum(chosen.astype(jnp.int32), axis=0) - 1
    slot_ids = jnp.arange(capacity, dtype=jnp.int32)
    placed = chosen.T[:, None, :] & (slot_rank.T[:, None, :] == slot_ids[None, :, None])
    selector = placed.astype(jnp.bfloat16)
    outgoing = jnp.einsum(
        "ect,td->ecd", selector, ffn_in, preferred_element_type=jnp.float32
    ).astype(jnp.bfloat16)
    outgoing = jnp.repeat(outgoing, SPLIT, axis=0)
    received = lax.all_to_all(outgoing, "exp", split_axis=0, concat_axis=0, tiled=True)
    flat_rows = received.reshape(-1, model_width)
    expert_gu = jnp.dot(flat_rows, expert_gate_up[0], preferred_element_type=jnp.float32)
    activated = (jax.nn.silu(expert_gu[:, :FF_PART]) * expert_gu[:, FF_PART:]).astype(jnp.bfloat16)
    result = jnp.dot(activated, expert_down[0], preferred_element_type=jnp.float32).astype(
        jnp.bfloat16
    )
    returned = lax.all_to_all(
        result.reshape(received.shape), "exp", split_axis=0, concat_axis=0, tiled=True
    )
    summed = jnp.sum(
        returned.reshape(row_experts, SPLIT, capacity, model_width).astype(jnp.float32), axis=1
    )
    slot_weight = jnp.sum(placed.astype(jnp.float32) * route_share.T[:, None, :], axis=2)
    slot_values = summed * slot_weight[:, :, None]
    upper_part = slot_values.astype(jnp.bfloat16)
    lower_part = (slot_values - upper_part.astype(jnp.float32)).astype(jnp.bfloat16)
    routed = jnp.einsum(
        "ect,ecd->td", selector, upper_part, preferred_element_type=jnp.float32
    ) + jnp.einsum("ect,ecd->td", selector, lower_part, preferred_element_type=jnp.float32)
    layer_term = shared_term + routed
    summed_cols = scatter_sum_blocks(layer_term)
    hidden_out = (mixed_cols.astype(jnp.float32) + summed_cols).astype(jnp.bfloat16)
    return (hidden_out, pool_out[None])


def solution(mesh):
    placed = (
        P("exp", "blk"),
        P(),
        P(None, "blk"),
        P(None, "blk"),
        P("exp", "blk", None, None),
        P("exp", None),
        P("exp"),
        P(),
        P("exp", None),
        P("exp", None),
        P(None, None, "blk"),
        P("blk", None),
        P(("blk", "exp"), None, None),
        P(("blk", "exp"), None, None),
    )
    return jax.shard_map(
        per_device,
        mesh=mesh,
        in_specs=placed,
        out_specs=(P("exp", "blk"), P("exp", "blk", None, None)),
        check_vma=False,
    )
```

```python
import math

import jax
import jax.numpy as jnp
from jax import lax
from jax.experimental import pallas as pl
from jax.experimental.pallas import tpu as pltpu
from jax.sharding import PartitionSpec as P

HEADS = 20
KV_HEADS = 4
HEAD_DIM = 128
TOPK = 6
SPLIT = 4
PAGE = 128
NEW = 256
FF_PART = 384


rope_base = 500000.0
norm_eps = 1e-05


def normalize(inputs, gain_vec):
    values = inputs.astype(jnp.float32)
    inv_rms = lax.rsqrt(jnp.mean(values * values, axis=-1, keepdims=True) + norm_eps)
    return (values * inv_rms * gain_vec).astype(jnp.bfloat16)


def rotate(inputs, positions):
    half_dim = HEAD_DIM // 2
    frequency = rope_base ** (-(jnp.arange(half_dim).astype(jnp.float32) * 2.0 / HEAD_DIM))
    angles = positions.astype(jnp.float32)[:, None] * frequency[None, :]
    cosine = jnp.cos(angles)[:, None, :]
    sine_vals = jnp.sin(angles)[:, None, :]
    lower_half = inputs[..., :half_dim]
    upper_half = inputs[..., half_dim:]
    return jnp.concatenate(
        [
            lower_half * cosine - upper_half * sine_vals,
            upper_half * cosine + lower_half * sine_vals,
        ],
        axis=-1,
    )


def split_three(value):
    high = value.astype(jnp.bfloat16).astype(jnp.float32)
    rest = value - high
    middle = rest.astype(jnp.bfloat16).astype(jnp.float32)
    low = (rest - middle).astype(jnp.bfloat16).astype(jnp.float32)
    return [high, middle, low]


def attention_kernel(proj_ref, cos_ref, sin_ref, slot_ref, qpos_ref, kpos_ref, out_ref):
    key_width = KV_HEADS * HEAD_DIM
    group_size = HEADS // KV_HEADS
    allowed = kpos_ref[...] <= qpos_ref[...]
    cosine = cos_ref[...]
    sine_signed = sin_ref[...]
    lane = lax.broadcasted_iota(jnp.int32, (NEW, 128), 1)
    stats = jnp.zeros((NEW, 128), jnp.float32)
    for head in range(HEADS):
        kv = head // group_size
        raw = proj_ref[:, head * HEAD_DIM : (head + 1) * HEAD_DIM].astype(jnp.float32)
        swapped = pltpu.roll(raw, HEAD_DIM // 2, 1)
        query = (raw * cosine + swapped * sine_signed).astype(jnp.bfloat16)
        keys = slot_ref[:, kv * HEAD_DIM : (kv + 1) * HEAD_DIM]
        values = slot_ref[:, key_width + kv * HEAD_DIM : key_width + (kv + 1) * HEAD_DIM]
        scores = lax.dot_general(
            query, keys, (((1,), (1,)), ((), ())), preferred_element_type=jnp.float32
        ) * (1.0 / math.sqrt(HEAD_DIM))
        scores = jnp.where(allowed, scores, -1e30)
        peak = jnp.max(scores, axis=1, keepdims=True)
        probs = jnp.exp(scores - peak)
        live = jnp.where(peak > -1e29, 1.0, 0.0)
        total = jnp.sum(probs, axis=1, keepdims=True) * live
        out_ref[:, head * HEAD_DIM : (head + 1) * HEAD_DIM] = (
            jnp.dot(probs.astype(jnp.bfloat16), values, preferred_element_type=jnp.float32) * live
        ).astype(out_ref.dtype)
        for slot, value in enumerate(split_three(peak) + split_three(total)):
            stats = jnp.where(lane == slot * HEADS + head, value, stats)
    out_ref[:, HEADS * HEAD_DIM :] = stats.astype(out_ref.dtype)


def local_attention(projected_all, cosine, sine_signed, slot_rows, positions, key_pos):
    width = HEADS * HEAD_DIM + 128
    return pl.pallas_call(
        attention_kernel,
        out_shape=jax.ShapeDtypeStruct((NEW, width), jnp.bfloat16),
        in_specs=[pl.BlockSpec(memory_space=pltpu.VMEM)] * 6,
        out_specs=pl.BlockSpec(memory_space=pltpu.VMEM),
        cost_estimate=pl.CostEstimate(
            flops=4 * NEW * slot_rows.shape[0] * HEAD_DIM * HEADS,
            transcendentals=NEW * slot_rows.shape[0] * HEADS,
            bytes_accessed=NEW * width * 2 + slot_rows.size * 2 + projected_all.size * 2,
        ),
    )(projected_all, cosine, sine_signed, slot_rows, positions[:, None], key_pos[None, :])


def combine_kernel(part_ref, out_ref):
    coded = part_ref[:, :, HEADS * HEAD_DIM :].astype(jnp.float32)
    lane_count = coded.shape[2]

    def shifted(piece):
        return pltpu.roll(coded, lane_count - piece * HEADS, 2)

    peak = (coded + shifted(1)) + shifted(2)
    total = (shifted(3) + shifted(4)) + shifted(5)
    factors = jnp.exp(peak - jnp.max(peak, axis=0, keepdims=True))
    denominators = jnp.sum(factors * total, axis=0)
    lane = lax.broadcasted_iota(jnp.int32, coded.shape, 2)
    for head in range(HEADS):
        factor = jnp.sum(jnp.where(lane == head, factors, 0.0), axis=2, keepdims=True)
        denominator = jnp.sum(jnp.where(lane[0] == head, denominators, 0.0), axis=1, keepdims=True)
        numerator = jnp.sum(
            part_ref[:, :, head * HEAD_DIM : (head + 1) * HEAD_DIM].astype(jnp.float32) * factor,
            axis=0,
        )
        out_ref[:, head * HEAD_DIM : (head + 1) * HEAD_DIM] = (
            numerator / denominator
        ).astype(out_ref.dtype)


def combine_attention(parts):
    sources, rows, width = parts.shape
    return pl.pallas_call(
        combine_kernel,
        out_shape=jax.ShapeDtypeStruct((rows, HEADS * HEAD_DIM), jnp.bfloat16),
        in_specs=[pl.BlockSpec(memory_space=pltpu.VMEM)],
        out_specs=pl.BlockSpec(memory_space=pltpu.VMEM),
        cost_estimate=pl.CostEstimate(
            flops=3 * parts.size, transcendentals=sources * rows * 128,
            bytes_accessed=parts.size * 2 + rows * HEADS * HEAD_DIM * 2,
        ),
    )(parts)


def gather_blocks(values, axis):
    count = lax.axis_size("blk")
    stacked = jnp.broadcast_to(values[None], (count,) + values.shape)
    received = lax.all_to_all(stacked, "blk", split_axis=0, concat_axis=axis + 1, tiled=True)
    return received.reshape(received.shape[1:])


def scatter_sum_blocks(values):
    count = lax.axis_size("blk")
    rows, width = values.shape
    pieces = values.reshape(rows, count, width // count).transpose(1, 0, 2)
    received = lax.all_to_all(
        pieces.astype(jnp.bfloat16), "blk", split_axis=0, concat_axis=0, tiled=True
    )
    return jnp.sum(received.astype(jnp.float32), axis=0)


def per_device(
    hidden,
    attn_gain,
    qkv_weight,
    out_weight,
    kv_pool,
    page_table,
    cache_lens,
    ffn_gain,
    route_ids,
    route_weights,
    shared_gate_up,
    shared_down,
    expert_gate_up,
    expert_down,
):
    blocks = lax.axis_size("blk")
    groups = lax.axis_size("exp")
    block_index = lax.axis_index("blk")
    model_width = hidden.shape[1] * blocks
    query_width = HEADS * HEAD_DIM
    key_width = KV_HEADS * HEAD_DIM
    group_size = HEADS // KV_HEADS
    own_rows = NEW // blocks
    full_rows = gather_blocks(hidden, 1)
    attn_in = normalize(full_rows, attn_gain)
    projected = jnp.dot(attn_in, qkv_weight, preferred_element_type=jnp.float32).astype(
        jnp.bfloat16
    )
    projected_all = gather_blocks(projected, 1)
    length = cache_lens[0]
    positions = length + jnp.arange(NEW, dtype=jnp.int32)
    fresh_keys = rotate(
        projected_all[:, query_width : query_width + key_width]
        .astype(jnp.float32)
        .reshape(NEW, KV_HEADS, HEAD_DIM),
        positions,
    ).astype(jnp.bfloat16)
    appended = jnp.concatenate(
        [fresh_keys.reshape(NEW, key_width), projected_all[:, query_width + key_width :]], axis=1
    )
    page_map = page_table[0]
    pool_pages = page_map.shape[0]
    page_index = jnp.arange(pool_pages, dtype=jnp.int32)
    logical = jnp.sum(
        jnp.where(page_map[None, :] == page_index[:, None], page_index[None, :], 0), axis=1
    )
    local_pages = kv_pool.shape[1]
    local_logical = lax.dynamic_slice_in_dim(logical, block_index * local_pages, local_pages)
    slot_offsets = jnp.arange(PAGE, dtype=jnp.int32)
    local_pos = local_logical[:, None] * PAGE + slot_offsets[None, :]
    offset = local_pos - length
    written = (offset >= 0) & (offset < NEW)
    picked = appended[jnp.clip(offset, 0, NEW - 1)]
    pool_out = jnp.where(written[:, :, None], picked, kv_pool[0])
    half_dim = HEAD_DIM // 2
    frequency = rope_base ** (-(jnp.arange(half_dim).astype(jnp.float32) * 2.0 / HEAD_DIM))
    angles = positions.astype(jnp.float32)[:, None] * frequency[None, :]
    cosine = jnp.cos(angles)
    sine_vals = jnp.sin(angles)
    cosine_full = jnp.concatenate([cosine, cosine], axis=1)
    sine_signed = jnp.concatenate([-sine_vals, sine_vals], axis=1)
    slot_rows = pool_out.reshape(local_pages * PAGE, 2 * key_width)
    payload = local_attention(
        projected_all, cosine_full, sine_signed, slot_rows, positions, local_pos.reshape(-1)
    ).reshape(blocks, own_rows, query_width + 128)
    gathered = lax.all_to_all(payload, "blk", split_axis=0, concat_axis=0, tiled=True)
    own_attention = combine_attention(gathered)
    attended = jnp.dot(
        gather_blocks(own_attention, 0),
        out_weight,
        preferred_element_type=jnp.float32,
    )
    mixed_cols = (hidden.astype(jnp.float32) + attended).astype(jnp.bfloat16)
    mixed_rows = gather_blocks(mixed_cols, 1)
    ffn_in = normalize(mixed_rows, ffn_gain)
    shared_cols = shared_gate_up.shape[2]
    gate_up = jnp.dot(
        ffn_in,
        shared_gate_up.reshape(model_width, 2 * shared_cols),
        preferred_element_type=jnp.float32,
    )
    shared_act = (jax.nn.silu(gate_up[:, :shared_cols]) * gate_up[:, shared_cols:]).astype(
        jnp.bfloat16
    )
    shared_term = jnp.dot(shared_act, shared_down, preferred_element_type=jnp.float32)
    shared_sum = lax.psum_scatter(shared_term, "blk", scatter_dimension=1, tiled=True)
    row_experts = groups // SPLIT
    expert_count = row_experts * blocks
    capacity = NEW * TOPK * 4 // (expert_count * 3)
    row_expert_ids = block_index * row_experts + jnp.arange(row_experts, dtype=jnp.int32)
    route_hits = route_ids[:, :, None] == row_expert_ids[None, None, :]
    chosen = jnp.any(route_hits, axis=1)
    route_share = jnp.sum(jnp.where(route_hits, route_weights[:, :, None], 0.0), axis=1)
    slot_rank = jnp.cumsum(chosen.astype(jnp.int32), axis=0) - 1
    slot_ids = jnp.arange(capacity, dtype=jnp.int32)
    placed = chosen.T[:, None, :] & (slot_rank.T[:, None, :] == slot_ids[None, :, None])
    selector = placed.astype(jnp.bfloat16)
    outgoing = jnp.einsum(
        "ect,td->ecd", selector, ffn_in, preferred_element_type=jnp.float32
    ).astype(jnp.bfloat16)
    outgoing = jnp.repeat(outgoing, SPLIT, axis=0)
    received = lax.all_to_all(outgoing, "exp", split_axis=0, concat_axis=0, tiled=True)
    flat_rows = received.reshape(-1, model_width)
    expert_gu = jnp.dot(flat_rows, expert_gate_up[0], preferred_element_type=jnp.float32)
    activated = (jax.nn.silu(expert_gu[:, :FF_PART]) * expert_gu[:, FF_PART:]).astype(jnp.bfloat16)
    result = jnp.dot(activated, expert_down[0], preferred_element_type=jnp.float32).astype(
        jnp.bfloat16
    )
    column_width = model_width // blocks
    sent_back = (
        result.reshape(groups, capacity, blocks, column_width)
        .transpose(2, 0, 1, 3)
        .reshape(blocks * groups, capacity, column_width)
    )
    returned = lax.all_to_all(sent_back, ("blk", "exp"), split_axis=0, concat_axis=0, tiled=True)
    summed = jnp.sum(
        returned.reshape(expert_count, SPLIT, capacity, column_width).astype(jnp.float32), axis=1
    )
    every_expert = jnp.arange(expert_count, dtype=jnp.int32)
    all_hits = route_ids[:, :, None] == every_expert[None, None, :]
    all_chosen = jnp.any(all_hits, axis=1)
    all_share = jnp.sum(jnp.where(all_hits, route_weights[:, :, None], 0.0), axis=1)
    all_rank = jnp.cumsum(all_chosen.astype(jnp.int32), axis=0) - 1
    all_placed = all_chosen.T[:, None, :] & (all_rank.T[:, None, :] == slot_ids[None, :, None])
    all_selector = all_placed.astype(jnp.bfloat16)
    slot_weight = jnp.sum(all_placed.astype(jnp.float32) * all_share.T[:, None, :], axis=2)
    slot_values = summed * slot_weight[:, :, None]
    upper_part = slot_values.astype(jnp.bfloat16)
    lower_part = (slot_values - upper_part.astype(jnp.float32)).astype(jnp.bfloat16)
    routed_cols = jnp.einsum(
        "ect,ecd->td", all_selector, upper_part, preferred_element_type=jnp.float32
    ) + jnp.einsum("ect,ecd->td", all_selector, lower_part, preferred_element_type=jnp.float32)
    hidden_out = (mixed_cols.astype(jnp.float32) + shared_sum + routed_cols).astype(jnp.bfloat16)
    return (hidden_out, pool_out[None])


def solution(mesh):
    placed = (
        P("exp", "blk"),
        P(),
        P(None, "blk"),
        P(None, "blk"),
        P("exp", "blk", None, None),
        P("exp", None),
        P("exp"),
        P(),
        P("exp", None),
        P("exp", None),
        P(None, None, "blk"),
        P("blk", None),
        P(("blk", "exp"), None, None),
        P(("blk", "exp"), None, None),
    )
    return jax.shard_map(
        per_device,
        mesh=mesh,
        in_specs=placed,
        out_specs=(P("exp", "blk"), P("exp", "blk", None, None)),
        check_vma=False,
    )
```

```python
import math

import jax
import jax.numpy as jnp
from jax import lax
from jax.experimental import pallas as pl
from jax.experimental.pallas import tpu as pltpu
from jax.sharding import PartitionSpec as P

HEADS = 20
KV_HEADS = 4
HEAD_DIM = 128
TOPK = 6
SPLIT = 4
PAGE = 128
NEW = 256
FF_PART = 384


rope_base = 500000.0
norm_eps = 1e-05


def normalize(inputs, gain_vec):
    values = inputs.astype(jnp.float32)
    inv_rms = lax.rsqrt(jnp.mean(values * values, axis=-1, keepdims=True) + norm_eps)
    return (values * inv_rms * gain_vec).astype(jnp.bfloat16)


def rotate(inputs, positions):
    half_dim = HEAD_DIM // 2
    frequency = rope_base ** (-(jnp.arange(half_dim).astype(jnp.float32) * 2.0 / HEAD_DIM))
    angles = positions.astype(jnp.float32)[:, None] * frequency[None, :]
    cosine = jnp.cos(angles)[:, None, :]
    sine_vals = jnp.sin(angles)[:, None, :]
    lower_half = inputs[..., :half_dim]
    upper_half = inputs[..., half_dim:]
    return jnp.concatenate(
        [
            lower_half * cosine - upper_half * sine_vals,
            upper_half * cosine + lower_half * sine_vals,
        ],
        axis=-1,
    )


def split_three(value):
    high = value.astype(jnp.bfloat16).astype(jnp.float32)
    rest = value - high
    middle = rest.astype(jnp.bfloat16).astype(jnp.float32)
    low = (rest - middle).astype(jnp.bfloat16).astype(jnp.float32)
    return [high, middle, low]


def attention_kernel(proj_ref, cos_ref, sin_ref, slot_ref, qpos_ref, kpos_ref, out_ref):
    key_width = KV_HEADS * HEAD_DIM
    group_size = HEADS // KV_HEADS
    allowed = kpos_ref[...] <= qpos_ref[...]
    group_allowed = jnp.concatenate([allowed] * group_size, axis=0)
    cosine = cos_ref[...]
    sine_signed = sin_ref[...]
    lane = lax.broadcasted_iota(jnp.int32, (NEW, 128), 1)
    stats = jnp.zeros((NEW, 128), jnp.float32)
    for kv in range(KV_HEADS):
        rotated = []
        for member in range(group_size):
            head = kv * group_size + member
            raw = proj_ref[:, head * HEAD_DIM : (head + 1) * HEAD_DIM].astype(jnp.float32)
            swapped = pltpu.roll(raw, HEAD_DIM // 2, 1)
            rotated.append((raw * cosine + swapped * sine_signed).astype(jnp.bfloat16))
        query = jnp.concatenate(rotated, axis=0)
        keys = slot_ref[:, kv * HEAD_DIM : (kv + 1) * HEAD_DIM]
        values = slot_ref[:, key_width + kv * HEAD_DIM : key_width + (kv + 1) * HEAD_DIM]
        scores = lax.dot_general(
            query, keys, (((1,), (1,)), ((), ())), preferred_element_type=jnp.float32
        ) * (1.0 / math.sqrt(HEAD_DIM))
        scores = jnp.where(group_allowed, scores, -1e30)
        peak = jnp.max(scores, axis=1, keepdims=True)
        probs = jnp.exp(scores - peak)
        live = jnp.where(peak > -1e29, 1.0, 0.0)
        total = jnp.sum(probs, axis=1, keepdims=True) * live
        weighted = (
            jnp.dot(probs.astype(jnp.bfloat16), values, preferred_element_type=jnp.float32) * live
        )
        for member in range(group_size):
            head = kv * group_size + member
            rows = slice(member * NEW, (member + 1) * NEW)
            out_ref[:, head * HEAD_DIM : (head + 1) * HEAD_DIM] = weighted[rows].astype(
                out_ref.dtype
            )
            pieces = split_three(peak[rows]) + split_three(total[rows])
            for slot, value in enumerate(pieces):
                stats = jnp.where(lane == slot * HEADS + head, value, stats)
    out_ref[:, HEADS * HEAD_DIM :] = stats.astype(out_ref.dtype)


def local_attention(projected_all, cosine, sine_signed, slot_rows, positions, key_pos):
    width = HEADS * HEAD_DIM + 128
    return pl.pallas_call(
        attention_kernel,
        out_shape=jax.ShapeDtypeStruct((NEW, width), jnp.bfloat16),
        in_specs=[pl.BlockSpec(memory_space=pltpu.VMEM)] * 6,
        out_specs=pl.BlockSpec(memory_space=pltpu.VMEM),
        cost_estimate=pl.CostEstimate(
            flops=4 * NEW * slot_rows.shape[0] * HEAD_DIM * HEADS,
            transcendentals=NEW * slot_rows.shape[0] * HEADS,
            bytes_accessed=NEW * width * 2 + slot_rows.size * 2 + projected_all.size * 2,
        ),
    )(projected_all, cosine, sine_signed, slot_rows, positions[:, None], key_pos[None, :])


def combine_kernel(part_ref, out_ref):
    coded = part_ref[:, :, HEADS * HEAD_DIM :].astype(jnp.float32)
    lane_count = coded.shape[2]

    def shifted(piece):
        return pltpu.roll(coded, lane_count - piece * HEADS, 2)

    peak = (coded + shifted(1)) + shifted(2)
    total = (shifted(3) + shifted(4)) + shifted(5)
    factors = jnp.exp(peak - jnp.max(peak, axis=0, keepdims=True))
    denominators = jnp.sum(factors * total, axis=0)
    lane = lax.broadcasted_iota(jnp.int32, coded.shape, 2)
    for head in range(HEADS):
        factor = jnp.sum(jnp.where(lane == head, factors, 0.0), axis=2, keepdims=True)
        denominator = jnp.sum(jnp.where(lane[0] == head, denominators, 0.0), axis=1, keepdims=True)
        numerator = jnp.sum(
            part_ref[:, :, head * HEAD_DIM : (head + 1) * HEAD_DIM].astype(jnp.float32) * factor,
            axis=0,
        )
        out_ref[:, head * HEAD_DIM : (head + 1) * HEAD_DIM] = (
            numerator / denominator
        ).astype(out_ref.dtype)


def combine_attention(parts):
    sources, rows, width = parts.shape
    return pl.pallas_call(
        combine_kernel,
        out_shape=jax.ShapeDtypeStruct((rows, HEADS * HEAD_DIM), jnp.bfloat16),
        in_specs=[pl.BlockSpec(memory_space=pltpu.VMEM)],
        out_specs=pl.BlockSpec(memory_space=pltpu.VMEM),
        cost_estimate=pl.CostEstimate(
            flops=3 * parts.size, transcendentals=sources * rows * 128,
            bytes_accessed=parts.size * 2 + rows * HEADS * HEAD_DIM * 2,
        ),
    )(parts)


def gather_blocks(values, axis):
    count = lax.axis_size("blk")
    stacked = jnp.broadcast_to(values[None], (count,) + values.shape)
    received = lax.all_to_all(stacked, "blk", split_axis=0, concat_axis=axis + 1, tiled=True)
    return received.reshape(received.shape[1:])


def scatter_sum_blocks(values):
    count = lax.axis_size("blk")
    rows, width = values.shape
    pieces = values.reshape(rows, count, width // count).transpose(1, 0, 2)
    received = lax.all_to_all(
        pieces.astype(jnp.bfloat16), "blk", split_axis=0, concat_axis=0, tiled=True
    )
    return jnp.sum(received.astype(jnp.float32), axis=0)


def per_device(
    hidden,
    attn_gain,
    qkv_weight,
    out_weight,
    kv_pool,
    page_table,
    cache_lens,
    ffn_gain,
    route_ids,
    route_weights,
    shared_gate_up,
    shared_down,
    expert_gate_up,
    expert_down,
):
    blocks = lax.axis_size("blk")
    groups = lax.axis_size("exp")
    block_index = lax.axis_index("blk")
    model_width = hidden.shape[1] * blocks
    query_width = HEADS * HEAD_DIM
    key_width = KV_HEADS * HEAD_DIM
    group_size = HEADS // KV_HEADS
    own_rows = NEW // blocks
    full_rows = gather_blocks(hidden, 1)
    attn_in = normalize(full_rows, attn_gain)
    projected = jnp.dot(attn_in, qkv_weight, preferred_element_type=jnp.float32).astype(
        jnp.bfloat16
    )
    projected_all = gather_blocks(projected, 1)
    length = cache_lens[0]
    positions = length + jnp.arange(NEW, dtype=jnp.int32)
    fresh_keys = rotate(
        projected_all[:, query_width : query_width + key_width]
        .astype(jnp.float32)
        .reshape(NEW, KV_HEADS, HEAD_DIM),
        positions,
    ).astype(jnp.bfloat16)
    appended = jnp.concatenate(
        [fresh_keys.reshape(NEW, key_width), projected_all[:, query_width + key_width :]], axis=1
    )
    page_map = page_table[0]
    pool_pages = page_map.shape[0]
    page_index = jnp.arange(pool_pages, dtype=jnp.int32)
    logical = jnp.sum(
        jnp.where(page_map[None, :] == page_index[:, None], page_index[None, :], 0), axis=1
    )
    local_pages = kv_pool.shape[1]
    local_logical = lax.dynamic_slice_in_dim(logical, block_index * local_pages, local_pages)
    slot_offsets = jnp.arange(PAGE, dtype=jnp.int32)
    local_pos = local_logical[:, None] * PAGE + slot_offsets[None, :]
    offset = local_pos - length
    written = (offset >= 0) & (offset < NEW)
    picked = appended[jnp.clip(offset, 0, NEW - 1)]
    pool_out = jnp.where(written[:, :, None], picked, kv_pool[0])
    half_dim = HEAD_DIM // 2
    frequency = rope_base ** (-(jnp.arange(half_dim).astype(jnp.float32) * 2.0 / HEAD_DIM))
    angles = positions.astype(jnp.float32)[:, None] * frequency[None, :]
    cosine = jnp.cos(angles)
    sine_vals = jnp.sin(angles)
    cosine_full = jnp.concatenate([cosine, cosine], axis=1)
    sine_signed = jnp.concatenate([-sine_vals, sine_vals], axis=1)
    slot_rows = pool_out.reshape(local_pages * PAGE, 2 * key_width)
    payload = local_attention(
        projected_all, cosine_full, sine_signed, slot_rows, positions, local_pos.reshape(-1)
    ).reshape(blocks, own_rows, query_width + 128)
    gathered = lax.all_to_all(payload, "blk", split_axis=0, concat_axis=0, tiled=True)
    own_attention = combine_attention(gathered)
    attended = jnp.dot(
        gather_blocks(own_attention, 0),
        out_weight,
        preferred_element_type=jnp.float32,
    )
    mixed_cols = (hidden.astype(jnp.float32) + attended).astype(jnp.bfloat16)
    mixed_rows = gather_blocks(mixed_cols, 1)
    ffn_in = normalize(mixed_rows, ffn_gain)
    shared_cols = shared_gate_up.shape[2]
    gate_up = jnp.dot(
        ffn_in,
        shared_gate_up.reshape(model_width, 2 * shared_cols),
        preferred_element_type=jnp.float32,
    )
    shared_act = (jax.nn.silu(gate_up[:, :shared_cols]) * gate_up[:, shared_cols:]).astype(
        jnp.bfloat16
    )
    shared_term = jnp.dot(shared_act, shared_down, preferred_element_type=jnp.float32)
    row_experts = groups // SPLIT
    expert_count = row_experts * blocks
    capacity = NEW * TOPK * 4 // (expert_count * 3)
    row_expert_ids = block_index * row_experts + jnp.arange(row_experts, dtype=jnp.int32)
    route_hits = route_ids[:, :, None] == row_expert_ids[None, None, :]
    chosen = jnp.any(route_hits, axis=1)
    route_share = jnp.sum(jnp.where(route_hits, route_weights[:, :, None], 0.0), axis=1)
    slot_rank = jnp.cumsum(chosen.astype(jnp.int32), axis=0) - 1
    slot_ids = jnp.arange(capacity, dtype=jnp.int32)
    placed = chosen.T[:, None, :] & (slot_rank.T[:, None, :] == slot_ids[None, :, None])
    selector = placed.astype(jnp.bfloat16)
    outgoing = jnp.einsum(
        "ect,td->ecd", selector, ffn_in, preferred_element_type=jnp.float32
    ).astype(jnp.bfloat16)
    outgoing = jnp.repeat(outgoing, SPLIT, axis=0)
    received = lax.all_to_all(outgoing, "exp", split_axis=0, concat_axis=0, tiled=True)
    flat_rows = received.reshape(-1, model_width)
    expert_gu = jnp.dot(flat_rows, expert_gate_up[0], preferred_element_type=jnp.float32)
    activated = (jax.nn.silu(expert_gu[:, :FF_PART]) * expert_gu[:, FF_PART:]).astype(jnp.bfloat16)
    result = jnp.dot(activated, expert_down[0], preferred_element_type=jnp.float32).astype(
        jnp.bfloat16
    )
    returned = lax.all_to_all(
        result.reshape(received.shape), "exp", split_axis=0, concat_axis=0, tiled=True
    )
    summed = jnp.sum(
        returned.reshape(row_experts, SPLIT, capacity, model_width).astype(jnp.float32), axis=1
    )
    slot_weight = jnp.sum(placed.astype(jnp.float32) * route_share.T[:, None, :], axis=2)
    slot_values = summed * slot_weight[:, :, None]
    upper_part = slot_values.astype(jnp.bfloat16)
    lower_part = (slot_values - upper_part.astype(jnp.float32)).astype(jnp.bfloat16)
    routed = jnp.einsum(
        "ect,ecd->td", selector, upper_part, preferred_element_type=jnp.float32
    ) + jnp.einsum("ect,ecd->td", selector, lower_part, preferred_element_type=jnp.float32)
    layer_term = shared_term + routed
    summed_cols = scatter_sum_blocks(layer_term)
    hidden_out = (mixed_cols.astype(jnp.float32) + summed_cols).astype(jnp.bfloat16)
    return (hidden_out, pool_out[None])


def solution(mesh):
    placed = (
        P("exp", "blk"),
        P(),
        P(None, "blk"),
        P(None, "blk"),
        P("exp", "blk", None, None),
        P("exp", None),
        P("exp"),
        P(),
        P("exp", None),
        P("exp", None),
        P(None, None, "blk"),
        P("blk", None),
        P(("blk", "exp"), None, None),
        P(("blk", "exp"), None, None),
    )
    return jax.shard_map(
        per_device,
        mesh=mesh,
        in_specs=placed,
        out_specs=(P("exp", "blk"), P("exp", "blk", None, None)),
        check_vma=False,
    )
```

```python
import math

import jax
import jax.numpy as jnp
from jax import lax
from jax.experimental import pallas as pl
from jax.experimental.pallas import tpu as pltpu
from jax.sharding import PartitionSpec as P

HEADS = 20
KV_HEADS = 4
HEAD_DIM = 128
TOPK = 6
SPLIT = 4
PAGE = 128
NEW = 256
FF_PART = 384


rope_base = 500000.0
norm_eps = 1e-05


def normalize(inputs, gain_vec):
    values = inputs.astype(jnp.float32)
    inv_rms = lax.rsqrt(jnp.mean(values * values, axis=-1, keepdims=True) + norm_eps)
    return (values * inv_rms * gain_vec).astype(jnp.bfloat16)


def rotate(inputs, positions):
    half_dim = HEAD_DIM // 2
    frequency = rope_base ** (-(jnp.arange(half_dim).astype(jnp.float32) * 2.0 / HEAD_DIM))
    angles = positions.astype(jnp.float32)[:, None] * frequency[None, :]
    cosine = jnp.cos(angles)[:, None, :]
    sine_vals = jnp.sin(angles)[:, None, :]
    lower_half = inputs[..., :half_dim]
    upper_half = inputs[..., half_dim:]
    return jnp.concatenate(
        [
            lower_half * cosine - upper_half * sine_vals,
            upper_half * cosine + lower_half * sine_vals,
        ],
        axis=-1,
    )


def split_three(value):
    high = value.astype(jnp.bfloat16).astype(jnp.float32)
    rest = value - high
    middle = rest.astype(jnp.bfloat16).astype(jnp.float32)
    low = (rest - middle).astype(jnp.bfloat16).astype(jnp.float32)
    return [high, middle, low]


def attention_kernel(proj_ref, cos_ref, sin_ref, slot_ref, qpos_ref, kpos_ref, out_ref):
    key_width = KV_HEADS * HEAD_DIM
    group_size = HEADS // KV_HEADS
    allowed = kpos_ref[...] <= qpos_ref[...]
    group_allowed = jnp.concatenate([allowed] * group_size, axis=0)
    cosine = cos_ref[...]
    sine_signed = sin_ref[...]
    lane = lax.broadcasted_iota(jnp.int32, (NEW, 128), 1)
    stats = jnp.zeros((NEW, 128), jnp.float32)
    for kv in range(KV_HEADS):
        rotated = []
        for member in range(group_size):
            head = kv * group_size + member
            raw = proj_ref[:, head * HEAD_DIM : (head + 1) * HEAD_DIM].astype(jnp.float32)
            swapped = pltpu.roll(raw, HEAD_DIM // 2, 1)
            rotated.append((raw * cosine + swapped * sine_signed).astype(jnp.bfloat16))
        query = jnp.concatenate(rotated, axis=0)
        keys = slot_ref[:, kv * HEAD_DIM : (kv + 1) * HEAD_DIM]
        values = slot_ref[:, key_width + kv * HEAD_DIM : key_width + (kv + 1) * HEAD_DIM]
        scores = lax.dot_general(
            query, keys, (((1,), (1,)), ((), ())), preferred_element_type=jnp.float32
        ) * (1.0 / math.sqrt(HEAD_DIM))
        scores = jnp.where(group_allowed, scores, -1e30)
        peak = jnp.max(scores, axis=1, keepdims=True)
        probs = jnp.exp(scores - peak)
        live = jnp.where(peak > -1e29, 1.0, 0.0)
        total = jnp.sum(probs, axis=1, keepdims=True) * live
        weighted = (
            jnp.dot(probs.astype(jnp.bfloat16), values, preferred_element_type=jnp.float32) * live
        )
        for member in range(group_size):
            head = kv * group_size + member
            rows = slice(member * NEW, (member + 1) * NEW)
            out_ref[:, head * HEAD_DIM : (head + 1) * HEAD_DIM] = weighted[rows].astype(
                out_ref.dtype
            )
            pieces = split_three(peak[rows]) + split_three(total[rows])
            for slot, value in enumerate(pieces):
                stats = jnp.where(lane == slot * HEADS + head, value, stats)
    out_ref[:, HEADS * HEAD_DIM :] = stats.astype(out_ref.dtype)


def local_attention(projected_all, cosine, sine_signed, slot_rows, positions, key_pos):
    width = HEADS * HEAD_DIM + 128
    return pl.pallas_call(
        attention_kernel,
        out_shape=jax.ShapeDtypeStruct((NEW, width), jnp.bfloat16),
        in_specs=[pl.BlockSpec(memory_space=pltpu.VMEM)] * 6,
        out_specs=pl.BlockSpec(memory_space=pltpu.VMEM),
        cost_estimate=pl.CostEstimate(
            flops=4 * NEW * slot_rows.shape[0] * HEAD_DIM * HEADS,
            transcendentals=NEW * slot_rows.shape[0] * HEADS,
            bytes_accessed=NEW * width * 2 + slot_rows.size * 2 + projected_all.size * 2,
        ),
    )(projected_all, cosine, sine_signed, slot_rows, positions[:, None], key_pos[None, :])


def combine_kernel(part_ref, out_ref):
    coded = part_ref[:, :, HEADS * HEAD_DIM :].astype(jnp.float32)
    lane_count = coded.shape[2]

    def shifted(piece):
        return pltpu.roll(coded, lane_count - piece * HEADS, 2)

    peak = (coded + shifted(1)) + shifted(2)
    total = (shifted(3) + shifted(4)) + shifted(5)
    factors = jnp.exp(peak - jnp.max(peak, axis=0, keepdims=True))
    denominators = jnp.sum(factors * total, axis=0)
    lane = lax.broadcasted_iota(jnp.int32, coded.shape, 2)
    for head in range(HEADS):
        factor = jnp.sum(jnp.where(lane == head, factors, 0.0), axis=2, keepdims=True)
        denominator = jnp.sum(jnp.where(lane[0] == head, denominators, 0.0), axis=1, keepdims=True)
        numerator = jnp.sum(
            part_ref[:, :, head * HEAD_DIM : (head + 1) * HEAD_DIM].astype(jnp.float32) * factor,
            axis=0,
        )
        out_ref[:, head * HEAD_DIM : (head + 1) * HEAD_DIM] = (
            numerator / denominator
        ).astype(out_ref.dtype)


def combine_attention(parts):
    sources, rows, width = parts.shape
    return pl.pallas_call(
        combine_kernel,
        out_shape=jax.ShapeDtypeStruct((rows, HEADS * HEAD_DIM), jnp.bfloat16),
        in_specs=[pl.BlockSpec(memory_space=pltpu.VMEM)],
        out_specs=pl.BlockSpec(memory_space=pltpu.VMEM),
        cost_estimate=pl.CostEstimate(
            flops=3 * parts.size, transcendentals=sources * rows * 128,
            bytes_accessed=parts.size * 2 + rows * HEADS * HEAD_DIM * 2,
        ),
    )(parts)


def gather_blocks(values, axis):
    count = lax.axis_size("blk")
    stacked = jnp.broadcast_to(values[None], (count,) + values.shape)
    received = lax.all_to_all(stacked, "blk", split_axis=0, concat_axis=axis + 1, tiled=True)
    return received.reshape(received.shape[1:])


def scatter_sum_blocks(values):
    count = lax.axis_size("blk")
    rows, width = values.shape
    pieces = values.reshape(rows, count, width // count)
    received = lax.all_to_all(
        pieces.astype(jnp.bfloat16), "blk", split_axis=1, concat_axis=1, tiled=True
    )
    return jnp.sum(received.astype(jnp.float32), axis=1)


def per_device(
    hidden,
    attn_gain,
    qkv_weight,
    out_weight,
    kv_pool,
    page_table,
    cache_lens,
    ffn_gain,
    route_ids,
    route_weights,
    shared_gate_up,
    shared_down,
    expert_gate_up,
    expert_down,
):
    blocks = lax.axis_size("blk")
    groups = lax.axis_size("exp")
    block_index = lax.axis_index("blk")
    model_width = hidden.shape[1] * blocks
    query_width = HEADS * HEAD_DIM
    key_width = KV_HEADS * HEAD_DIM
    group_size = HEADS // KV_HEADS
    own_rows = NEW // blocks
    full_rows = gather_blocks(hidden, 1)
    attn_in = normalize(full_rows, attn_gain)
    projected = jnp.dot(attn_in, qkv_weight, preferred_element_type=jnp.float32).astype(
        jnp.bfloat16
    )
    projected_all = gather_blocks(projected, 1)
    length = cache_lens[0]
    positions = length + jnp.arange(NEW, dtype=jnp.int32)
    fresh_keys = rotate(
        projected_all[:, query_width : query_width + key_width]
        .astype(jnp.float32)
        .reshape(NEW, KV_HEADS, HEAD_DIM),
        positions,
    ).astype(jnp.bfloat16)
    appended = jnp.concatenate(
        [fresh_keys.reshape(NEW, key_width), projected_all[:, query_width + key_width :]], axis=1
    )
    page_map = page_table[0]
    pool_pages = page_map.shape[0]
    page_index = jnp.arange(pool_pages, dtype=jnp.int32)
    logical = jnp.sum(
        jnp.where(page_map[None, :] == page_index[:, None], page_index[None, :], 0), axis=1
    )
    local_pages = kv_pool.shape[1]
    local_logical = lax.dynamic_slice_in_dim(logical, block_index * local_pages, local_pages)
    slot_offsets = jnp.arange(PAGE, dtype=jnp.int32)
    local_pos = local_logical[:, None] * PAGE + slot_offsets[None, :]
    offset = local_pos - length
    written = (offset >= 0) & (offset < NEW)
    padding = jnp.zeros((PAGE, 2 * key_width), appended.dtype)
    padded = jnp.concatenate([padding, appended, padding], axis=0)
    starts = jnp.clip(local_logical * PAGE - length + PAGE, 0, NEW + PAGE)
    picked = jnp.stack(
        [
            lax.dynamic_slice_in_dim(padded, starts[page], PAGE, 0)
            for page in range(local_pages)
        ]
    )
    pool_out = jnp.where(written[:, :, None], picked, kv_pool[0])
    half_dim = HEAD_DIM // 2
    frequency = rope_base ** (-(jnp.arange(half_dim).astype(jnp.float32) * 2.0 / HEAD_DIM))
    angles = positions.astype(jnp.float32)[:, None] * frequency[None, :]
    cosine = jnp.cos(angles)
    sine_vals = jnp.sin(angles)
    cosine_full = jnp.concatenate([cosine, cosine], axis=1)
    sine_signed = jnp.concatenate([-sine_vals, sine_vals], axis=1)
    slot_rows = pool_out.reshape(local_pages * PAGE, 2 * key_width)
    payload = local_attention(
        projected_all, cosine_full, sine_signed, slot_rows, positions, local_pos.reshape(-1)
    ).reshape(blocks, own_rows, query_width + 128)
    gathered = lax.all_to_all(payload, "blk", split_axis=0, concat_axis=0, tiled=True)
    own_attention = combine_attention(gathered)
    attended = jnp.dot(
        gather_blocks(own_attention, 0),
        out_weight,
        preferred_element_type=jnp.float32,
    )
    mixed_cols = (hidden.astype(jnp.float32) + attended).astype(jnp.bfloat16)
    mixed_rows = gather_blocks(mixed_cols, 1)
    ffn_in = normalize(mixed_rows, ffn_gain)
    shared_cols = shared_gate_up.shape[2]
    gate_up = jnp.dot(
        ffn_in,
        shared_gate_up.reshape(model_width, 2 * shared_cols),
        preferred_element_type=jnp.float32,
    )
    shared_act = (jax.nn.silu(gate_up[:, :shared_cols]) * gate_up[:, shared_cols:]).astype(
        jnp.bfloat16
    )
    shared_term = jnp.dot(shared_act, shared_down, preferred_element_type=jnp.float32)
    row_experts = groups // SPLIT
    expert_count = row_experts * blocks
    capacity = NEW * TOPK * 4 // (expert_count * 3)
    row_expert_ids = block_index * row_experts + jnp.arange(row_experts, dtype=jnp.int32)
    route_hits = route_ids[:, :, None] == row_expert_ids[None, None, :]
    chosen = jnp.any(route_hits, axis=1)
    route_share = jnp.sum(jnp.where(route_hits, route_weights[:, :, None], 0.0), axis=1)
    slot_rank = jnp.cumsum(chosen.astype(jnp.int32), axis=0) - 1
    slot_ids = jnp.arange(capacity, dtype=jnp.int32)
    placed = chosen.T[:, None, :] & (slot_rank.T[:, None, :] == slot_ids[None, :, None])
    selector = placed.astype(jnp.bfloat16)
    outgoing = jnp.einsum(
        "ect,td->ecd", selector, ffn_in, preferred_element_type=jnp.float32
    ).astype(jnp.bfloat16)
    outgoing = jnp.repeat(outgoing, SPLIT, axis=0)
    received = lax.all_to_all(outgoing, "exp", split_axis=0, concat_axis=0, tiled=True)
    flat_rows = received.reshape(-1, model_width)
    expert_gu = jnp.dot(flat_rows, expert_gate_up[0], preferred_element_type=jnp.float32)
    activated = (jax.nn.silu(expert_gu[:, :FF_PART]) * expert_gu[:, FF_PART:]).astype(jnp.bfloat16)
    result = jnp.dot(activated, expert_down[0], preferred_element_type=jnp.float32).astype(
        jnp.bfloat16
    )
    returned = lax.all_to_all(
        result.reshape(received.shape), "exp", split_axis=0, concat_axis=0, tiled=True
    )
    summed = jnp.sum(
        returned.reshape(row_experts, SPLIT, capacity, model_width).astype(jnp.float32), axis=1
    )
    slot_weight = jnp.sum(placed.astype(jnp.float32) * route_share.T[:, None, :], axis=2)
    slot_values = summed * slot_weight[:, :, None]
    upper_part = slot_values.astype(jnp.bfloat16)
    lower_part = (slot_values - upper_part.astype(jnp.float32)).astype(jnp.bfloat16)
    routed = jnp.einsum(
        "ect,ecd->td", selector, upper_part, preferred_element_type=jnp.float32
    ) + jnp.einsum("ect,ecd->td", selector, lower_part, preferred_element_type=jnp.float32)
    layer_term = shared_term + routed
    summed_cols = scatter_sum_blocks(layer_term)
    hidden_out = (mixed_cols.astype(jnp.float32) + summed_cols).astype(jnp.bfloat16)
    return (hidden_out, pool_out[None])


def solution(mesh):
    placed = (
        P("exp", "blk"),
        P(),
        P(None, "blk"),
        P(None, "blk"),
        P("exp", "blk", None, None),
        P("exp", None),
        P("exp"),
        P(),
        P("exp", None),
        P("exp", None),
        P(None, None, "blk"),
        P("blk", None),
        P(("blk", "exp"), None, None),
        P(("blk", "exp"), None, None),
    )
    return jax.shard_map(
        per_device,
        mesh=mesh,
        in_specs=placed,
        out_specs=(P("exp", "blk"), P("exp", "blk", None, None)),
        check_vma=False,
    )
```

```python
import math

import jax
import jax.numpy as jnp
from jax import lax
from jax.experimental import pallas as pl
from jax.experimental.pallas import tpu as pltpu
from jax.sharding import PartitionSpec as P

HEADS = 20
KV_HEADS = 4
HEAD_DIM = 128
TOPK = 6
SPLIT = 4
PAGE = 128
NEW = 256
FF_PART = 384


rope_base = 500000.0
norm_eps = 1e-05


def normalize(inputs, gain_vec):
    values = inputs.astype(jnp.float32)
    inv_rms = lax.rsqrt(jnp.mean(values * values, axis=-1, keepdims=True) + norm_eps)
    return (values * inv_rms * gain_vec).astype(jnp.bfloat16)


def rotate(inputs, positions):
    half_dim = HEAD_DIM // 2
    frequency = rope_base ** (-(jnp.arange(half_dim).astype(jnp.float32) * 2.0 / HEAD_DIM))
    angles = positions.astype(jnp.float32)[:, None] * frequency[None, :]
    cosine = jnp.cos(angles)[:, None, :]
    sine_vals = jnp.sin(angles)[:, None, :]
    lower_half = inputs[..., :half_dim]
    upper_half = inputs[..., half_dim:]
    return jnp.concatenate(
        [
            lower_half * cosine - upper_half * sine_vals,
            upper_half * cosine + lower_half * sine_vals,
        ],
        axis=-1,
    )


def split_three(value):
    high = value.astype(jnp.bfloat16).astype(jnp.float32)
    rest = value - high
    middle = rest.astype(jnp.bfloat16).astype(jnp.float32)
    low = (rest - middle).astype(jnp.bfloat16).astype(jnp.float32)
    return [high, middle, low]


def attention_kernel(proj_ref, cos_ref, sin_ref, slot_ref, qpos_ref, kpos_ref, out_ref):
    key_width = KV_HEADS * HEAD_DIM
    group_size = HEADS // KV_HEADS
    allowed = kpos_ref[...] <= qpos_ref[...]
    group_allowed = jnp.concatenate([allowed] * group_size, axis=0)
    cosine = cos_ref[...]
    sine_signed = sin_ref[...]
    lane = lax.broadcasted_iota(jnp.int32, (NEW, 128), 1)
    stats = jnp.zeros((NEW, 128), jnp.float32)
    for kv in range(KV_HEADS):
        rotated = []
        for member in range(group_size):
            head = kv * group_size + member
            raw = proj_ref[:, head * HEAD_DIM : (head + 1) * HEAD_DIM].astype(jnp.float32)
            swapped = pltpu.roll(raw, HEAD_DIM // 2, 1)
            rotated.append((raw * cosine + swapped * sine_signed).astype(jnp.bfloat16))
        query = jnp.concatenate(rotated, axis=0)
        keys = slot_ref[:, kv * HEAD_DIM : (kv + 1) * HEAD_DIM]
        values = slot_ref[:, key_width + kv * HEAD_DIM : key_width + (kv + 1) * HEAD_DIM]
        scores = lax.dot_general(
            query, keys, (((1,), (1,)), ((), ())), preferred_element_type=jnp.float32
        ) * (1.0 / math.sqrt(HEAD_DIM))
        scores = jnp.where(group_allowed, scores, -1e30)
        peak = jnp.max(scores, axis=1, keepdims=True)
        probs = jnp.exp(scores - peak)
        live = jnp.where(peak > -1e29, 1.0, 0.0)
        total = jnp.sum(probs, axis=1, keepdims=True) * live
        weighted = (
            jnp.dot(probs.astype(jnp.bfloat16), values, preferred_element_type=jnp.float32) * live
        )
        for member in range(group_size):
            head = kv * group_size + member
            rows = slice(member * NEW, (member + 1) * NEW)
            out_ref[:, head * HEAD_DIM : (head + 1) * HEAD_DIM] = weighted[rows].astype(
                out_ref.dtype
            )
            pieces = split_three(peak[rows]) + split_three(total[rows])
            for slot, value in enumerate(pieces):
                stats = jnp.where(lane == slot * HEADS + head, value, stats)
    out_ref[:, HEADS * HEAD_DIM :] = stats.astype(out_ref.dtype)


def local_attention(projected_all, cosine, sine_signed, slot_rows, positions, key_pos):
    width = HEADS * HEAD_DIM + 128
    return pl.pallas_call(
        attention_kernel,
        out_shape=jax.ShapeDtypeStruct((NEW, width), jnp.bfloat16),
        in_specs=[pl.BlockSpec(memory_space=pltpu.VMEM)] * 6,
        out_specs=pl.BlockSpec(memory_space=pltpu.VMEM),
        cost_estimate=pl.CostEstimate(
            flops=4 * NEW * slot_rows.shape[0] * HEAD_DIM * HEADS,
            transcendentals=NEW * slot_rows.shape[0] * HEADS,
            bytes_accessed=NEW * width * 2 + slot_rows.size * 2 + projected_all.size * 2,
        ),
    )(projected_all, cosine, sine_signed, slot_rows, positions[:, None], key_pos[None, :])


def combine_kernel(part_ref, out_ref):
    coded = part_ref[:, :, HEADS * HEAD_DIM :].astype(jnp.float32)
    lane_count = coded.shape[2]

    def shifted(piece):
        return pltpu.roll(coded, lane_count - piece * HEADS, 2)

    peak = (coded + shifted(1)) + shifted(2)
    total = (shifted(3) + shifted(4)) + shifted(5)
    factors = jnp.exp(peak - jnp.max(peak, axis=0, keepdims=True))
    denominators = jnp.sum(factors * total, axis=0)
    lane = lax.broadcasted_iota(jnp.int32, coded.shape, 2)
    for head in range(HEADS):
        factor = jnp.sum(jnp.where(lane == head, factors, 0.0), axis=2, keepdims=True)
        denominator = jnp.sum(jnp.where(lane[0] == head, denominators, 0.0), axis=1, keepdims=True)
        numerator = jnp.sum(
            part_ref[:, :, head * HEAD_DIM : (head + 1) * HEAD_DIM].astype(jnp.float32) * factor,
            axis=0,
        )
        out_ref[:, head * HEAD_DIM : (head + 1) * HEAD_DIM] = (
            numerator / denominator
        ).astype(out_ref.dtype)


def combine_attention(parts):
    sources, rows, width = parts.shape
    return pl.pallas_call(
        combine_kernel,
        out_shape=jax.ShapeDtypeStruct((rows, HEADS * HEAD_DIM), jnp.bfloat16),
        in_specs=[pl.BlockSpec(memory_space=pltpu.VMEM)],
        out_specs=pl.BlockSpec(memory_space=pltpu.VMEM),
        cost_estimate=pl.CostEstimate(
            flops=3 * parts.size, transcendentals=sources * rows * 128,
            bytes_accessed=parts.size * 2 + rows * HEADS * HEAD_DIM * 2,
        ),
    )(parts)


def gather_blocks(values, axis):
    count = lax.axis_size("blk")
    stacked = jnp.broadcast_to(values[None], (count,) + values.shape)
    received = lax.all_to_all(stacked, "blk", split_axis=0, concat_axis=axis + 1, tiled=True)
    return received.reshape(received.shape[1:])


def scatter_sum_blocks(values):
    count = lax.axis_size("blk")
    rows, width = values.shape
    pieces = values.reshape(rows, count, width // count).transpose(1, 0, 2)
    received = lax.all_to_all(
        pieces.astype(jnp.bfloat16), "blk", split_axis=0, concat_axis=0, tiled=True
    )
    return jnp.sum(received.astype(jnp.float32), axis=0)


def per_device(
    hidden,
    attn_gain,
    qkv_weight,
    out_weight,
    kv_pool,
    page_table,
    cache_lens,
    ffn_gain,
    route_ids,
    route_weights,
    shared_gate_up,
    shared_down,
    expert_gate_up,
    expert_down,
):
    blocks = lax.axis_size("blk")
    groups = lax.axis_size("exp")
    block_index = lax.axis_index("blk")
    model_width = hidden.shape[1] * blocks
    query_width = HEADS * HEAD_DIM
    key_width = KV_HEADS * HEAD_DIM
    group_size = HEADS // KV_HEADS
    own_rows = NEW // blocks
    full_rows = gather_blocks(hidden, 1)
    attn_in = normalize(full_rows, attn_gain)
    projected = jnp.dot(attn_in, qkv_weight, preferred_element_type=jnp.float32).astype(
        jnp.bfloat16
    )
    projected_all = gather_blocks(projected, 1)
    length = cache_lens[0]
    positions = length + jnp.arange(NEW, dtype=jnp.int32)
    fresh_keys = rotate(
        projected_all[:, query_width : query_width + key_width]
        .astype(jnp.float32)
        .reshape(NEW, KV_HEADS, HEAD_DIM),
        positions,
    ).astype(jnp.bfloat16)
    appended = jnp.concatenate(
        [fresh_keys.reshape(NEW, key_width), projected_all[:, query_width + key_width :]], axis=1
    )
    page_map = page_table[0]
    pool_pages = page_map.shape[0]
    page_index = jnp.arange(pool_pages, dtype=jnp.int32)
    logical = jnp.sum(
        jnp.where(page_map[None, :] == page_index[:, None], page_index[None, :], 0), axis=1
    )
    local_pages = kv_pool.shape[1]
    local_logical = lax.dynamic_slice_in_dim(logical, block_index * local_pages, local_pages)
    slot_offsets = jnp.arange(PAGE, dtype=jnp.int32)
    local_pos = local_logical[:, None] * PAGE + slot_offsets[None, :]
    offset = local_pos - length
    written = (offset >= 0) & (offset < NEW)
    picked = appended[jnp.clip(offset, 0, NEW - 1)]
    pool_out = jnp.where(written[:, :, None], picked, kv_pool[0])
    half_dim = HEAD_DIM // 2
    frequency = rope_base ** (-(jnp.arange(half_dim).astype(jnp.float32) * 2.0 / HEAD_DIM))
    angles = positions.astype(jnp.float32)[:, None] * frequency[None, :]
    cosine = jnp.cos(angles)
    sine_vals = jnp.sin(angles)
    cosine_full = jnp.concatenate([cosine, cosine], axis=1)
    sine_signed = jnp.concatenate([-sine_vals, sine_vals], axis=1)
    slot_rows = pool_out.reshape(local_pages * PAGE, 2 * key_width)
    payload = local_attention(
        projected_all, cosine_full, sine_signed, slot_rows, positions, local_pos.reshape(-1)
    ).reshape(blocks, own_rows, query_width + 128)
    gathered = lax.all_to_all(payload, "blk", split_axis=0, concat_axis=0, tiled=True)
    own_attention = combine_attention(gathered)
    attended = jnp.dot(
        gather_blocks(own_attention, 0),
        out_weight,
        preferred_element_type=jnp.float32,
    )
    mixed_cols = (hidden.astype(jnp.float32) + attended).astype(jnp.bfloat16)
    mixed_rows = gather_blocks(mixed_cols, 1)
    ffn_in = normalize(mixed_rows, ffn_gain)
    shared_cols = shared_gate_up.shape[2]
    gate_up = jnp.dot(
        ffn_in,
        shared_gate_up.reshape(model_width, 2 * shared_cols),
        preferred_element_type=jnp.float32,
    )
    shared_act = (jax.nn.silu(gate_up[:, :shared_cols]) * gate_up[:, shared_cols:]).astype(
        jnp.bfloat16
    )
    shared_term = jnp.dot(shared_act, shared_down, preferred_element_type=jnp.float32)
    row_experts = groups // SPLIT
    expert_count = row_experts * blocks
    capacity = NEW * TOPK * 4 // (expert_count * 3)
    row_expert_ids = block_index * row_experts + jnp.arange(row_experts, dtype=jnp.int32)
    route_hits = route_ids[:, :, None] == row_expert_ids[None, None, :]
    chosen = jnp.any(route_hits, axis=1)
    route_share = jnp.sum(jnp.where(route_hits, route_weights[:, :, None], 0.0), axis=1)
    slot_rank = jnp.cumsum(chosen.astype(jnp.int32), axis=0) - 1
    slot_ids = jnp.arange(capacity, dtype=jnp.int32)
    placed = chosen.T[:, None, :] & (slot_rank.T[:, None, :] == slot_ids[None, :, None])
    selector = placed.astype(jnp.bfloat16)
    outgoing = jnp.einsum(
        "ect,td->ecd", selector, ffn_in, preferred_element_type=jnp.float32
    ).astype(jnp.bfloat16)
    outgoing = jnp.repeat(outgoing, SPLIT, axis=0)
    received = lax.all_to_all(outgoing, "exp", split_axis=0, concat_axis=0, tiled=True)
    slot_weight = jnp.sum(placed.astype(jnp.float32) * route_share.T[:, None, :], axis=2)
    received, slot_weight = lax.optimization_barrier((received, slot_weight))
    flat_rows = received.reshape(-1, model_width)
    expert_gu = jnp.dot(flat_rows, expert_gate_up[0], preferred_element_type=jnp.float32)
    activated = (jax.nn.silu(expert_gu[:, :FF_PART]) * expert_gu[:, FF_PART:]).astype(jnp.bfloat16)
    result = jnp.dot(activated, expert_down[0], preferred_element_type=jnp.float32).astype(
        jnp.bfloat16
    )
    returned = lax.all_to_all(
        result.reshape(received.shape), "exp", split_axis=0, concat_axis=0, tiled=True
    )
    summed = jnp.sum(
        returned.reshape(row_experts, SPLIT, capacity, model_width).astype(jnp.float32), axis=1
    )
    slot_values = summed * slot_weight[:, :, None]
    upper_part = slot_values.astype(jnp.bfloat16)
    lower_part = (slot_values - upper_part.astype(jnp.float32)).astype(jnp.bfloat16)
    routed = jnp.einsum(
        "ect,ecd->td", selector, upper_part, preferred_element_type=jnp.float32
    ) + jnp.einsum("ect,ecd->td", selector, lower_part, preferred_element_type=jnp.float32)
    layer_term = shared_term + routed
    summed_cols = scatter_sum_blocks(layer_term)
    hidden_out = (mixed_cols.astype(jnp.float32) + summed_cols).astype(jnp.bfloat16)
    return (hidden_out, pool_out[None])


def solution(mesh):
    placed = (
        P("exp", "blk"),
        P(),
        P(None, "blk"),
        P(None, "blk"),
        P("exp", "blk", None, None),
        P("exp", None),
        P("exp"),
        P(),
        P("exp", None),
        P("exp", None),
        P(None, None, "blk"),
        P("blk", None),
        P(("blk", "exp"), None, None),
        P(("blk", "exp"), None, None),
    )
    return jax.shard_map(
        per_device,
        mesh=mesh,
        in_specs=placed,
        out_specs=(P("exp", "blk"), P("exp", "blk", None, None)),
        check_vma=False,
    )
```

```python
import math

import jax
import jax.numpy as jnp
from jax import lax
from jax.experimental import pallas as pl
from jax.experimental.pallas import tpu as pltpu
from jax.sharding import PartitionSpec as P

HEADS = 20
KV_HEADS = 4
HEAD_DIM = 128
TOPK = 6
SPLIT = 4
PAGE = 128
NEW = 256
FF_PART = 384


rope_base = 500000.0
norm_eps = 1e-05


def normalize(inputs, gain_vec):
    values = inputs.astype(jnp.float32)
    inv_rms = lax.rsqrt(jnp.mean(values * values, axis=-1, keepdims=True) + norm_eps)
    return (values * inv_rms * gain_vec).astype(jnp.bfloat16)


def rotate(inputs, positions):
    half_dim = HEAD_DIM // 2
    frequency = rope_base ** (-(jnp.arange(half_dim).astype(jnp.float32) * 2.0 / HEAD_DIM))
    angles = positions.astype(jnp.float32)[:, None] * frequency[None, :]
    cosine = jnp.cos(angles)[:, None, :]
    sine_vals = jnp.sin(angles)[:, None, :]
    lower_half = inputs[..., :half_dim]
    upper_half = inputs[..., half_dim:]
    return jnp.concatenate(
        [
            lower_half * cosine - upper_half * sine_vals,
            upper_half * cosine + lower_half * sine_vals,
        ],
        axis=-1,
    )


def split_three(value):
    high = value.astype(jnp.bfloat16).astype(jnp.float32)
    rest = value - high
    middle = rest.astype(jnp.bfloat16).astype(jnp.float32)
    low = (rest - middle).astype(jnp.bfloat16).astype(jnp.float32)
    return [high, middle, low]


def attention_kernel(
    proj_ref, cos_ref, sin_ref, cache_ref, fresh_ref, offset_ref, qpos_ref, kpos_ref, out_ref, slot_ref
):
    offsets = offset_ref[...]
    columns = lax.broadcasted_iota(jnp.int32, (offsets.shape[0], NEW), 1)
    chooser = jnp.where(offsets == columns, 1.0, 0.0).astype(jnp.bfloat16)
    picked = jnp.dot(chooser, fresh_ref[...], preferred_element_type=jnp.float32)
    written = (offsets >= 0) & (offsets < NEW)
    slot_ref[...] = jnp.where(written, picked.astype(slot_ref.dtype), cache_ref[...])
    key_width = KV_HEADS * HEAD_DIM
    group_size = HEADS // KV_HEADS
    allowed = kpos_ref[...] <= qpos_ref[...]
    group_allowed = jnp.concatenate([allowed] * group_size, axis=0)
    cosine = cos_ref[...]
    sine_signed = sin_ref[...]
    lane = lax.broadcasted_iota(jnp.int32, (NEW, 128), 1)
    stats = jnp.zeros((NEW, 128), jnp.float32)
    for kv in range(KV_HEADS):
        rotated = []
        for member in range(group_size):
            head = kv * group_size + member
            raw = proj_ref[:, head * HEAD_DIM : (head + 1) * HEAD_DIM].astype(jnp.float32)
            swapped = pltpu.roll(raw, HEAD_DIM // 2, 1)
            rotated.append((raw * cosine + swapped * sine_signed).astype(jnp.bfloat16))
        query = jnp.concatenate(rotated, axis=0)
        keys = slot_ref[:, kv * HEAD_DIM : (kv + 1) * HEAD_DIM]
        values = slot_ref[:, key_width + kv * HEAD_DIM : key_width + (kv + 1) * HEAD_DIM]
        scores = lax.dot_general(
            query, keys, (((1,), (1,)), ((), ())), preferred_element_type=jnp.float32
        ) * (1.0 / math.sqrt(HEAD_DIM))
        scores = jnp.where(group_allowed, scores, -1e30)
        peak = jnp.max(scores, axis=1, keepdims=True)
        probs = jnp.exp(scores - peak)
        live = jnp.where(peak > -1e29, 1.0, 0.0)
        total = jnp.sum(probs, axis=1, keepdims=True) * live
        weighted = (
            jnp.dot(probs.astype(jnp.bfloat16), values, preferred_element_type=jnp.float32) * live
        )
        for member in range(group_size):
            head = kv * group_size + member
            rows = slice(member * NEW, (member + 1) * NEW)
            out_ref[:, head * HEAD_DIM : (head + 1) * HEAD_DIM] = weighted[rows].astype(
                out_ref.dtype
            )
            pieces = split_three(peak[rows]) + split_three(total[rows])
            for slot, value in enumerate(pieces):
                stats = jnp.where(lane == slot * HEADS + head, value, stats)
    out_ref[:, HEADS * HEAD_DIM :] = stats.astype(out_ref.dtype)


def local_attention(projected_all, cosine, sine_signed, cache_rows, fresh, offsets, positions, key_pos):
    width = HEADS * HEAD_DIM + 128
    return pl.pallas_call(
        attention_kernel,
        out_shape=(
            jax.ShapeDtypeStruct((NEW, width), jnp.bfloat16),
            jax.ShapeDtypeStruct(cache_rows.shape, cache_rows.dtype),
        ),
        in_specs=[pl.BlockSpec(memory_space=pltpu.VMEM)] * 8,
        out_specs=(pl.BlockSpec(memory_space=pltpu.VMEM), pl.BlockSpec(memory_space=pltpu.VMEM)),
        cost_estimate=pl.CostEstimate(
            flops=4 * NEW * cache_rows.shape[0] * HEAD_DIM * HEADS,
            transcendentals=NEW * cache_rows.shape[0] * HEADS,
            bytes_accessed=NEW * width * 2 + cache_rows.size * 4 + projected_all.size * 2,
        ),
    )(
        projected_all,
        cosine,
        sine_signed,
        cache_rows,
        fresh,
        offsets[:, None],
        positions[:, None],
        key_pos[None, :],
    )


def combine_kernel(part_ref, out_ref):
    coded = part_ref[:, :, HEADS * HEAD_DIM :].astype(jnp.float32)
    lane_count = coded.shape[2]

    def shifted(piece):
        return pltpu.roll(coded, lane_count - piece * HEADS, 2)

    peak = (coded + shifted(1)) + shifted(2)
    total = (shifted(3) + shifted(4)) + shifted(5)
    factors = jnp.exp(peak - jnp.max(peak, axis=0, keepdims=True))
    denominators = jnp.sum(factors * total, axis=0)
    lane = lax.broadcasted_iota(jnp.int32, coded.shape, 2)
    for head in range(HEADS):
        factor = jnp.sum(jnp.where(lane == head, factors, 0.0), axis=2, keepdims=True)
        denominator = jnp.sum(jnp.where(lane[0] == head, denominators, 0.0), axis=1, keepdims=True)
        numerator = jnp.sum(
            part_ref[:, :, head * HEAD_DIM : (head + 1) * HEAD_DIM].astype(jnp.float32) * factor,
            axis=0,
        )
        out_ref[:, head * HEAD_DIM : (head + 1) * HEAD_DIM] = (
            numerator / denominator
        ).astype(out_ref.dtype)


def combine_attention(parts):
    sources, rows, width = parts.shape
    return pl.pallas_call(
        combine_kernel,
        out_shape=jax.ShapeDtypeStruct((rows, HEADS * HEAD_DIM), jnp.bfloat16),
        in_specs=[pl.BlockSpec(memory_space=pltpu.VMEM)],
        out_specs=pl.BlockSpec(memory_space=pltpu.VMEM),
        cost_estimate=pl.CostEstimate(
            flops=3 * parts.size, transcendentals=sources * rows * 128,
            bytes_accessed=parts.size * 2 + rows * HEADS * HEAD_DIM * 2,
        ),
    )(parts)


def gather_blocks(values, axis):
    count = lax.axis_size("blk")
    stacked = jnp.broadcast_to(values[None], (count,) + values.shape)
    received = lax.all_to_all(stacked, "blk", split_axis=0, concat_axis=axis + 1, tiled=True)
    return received.reshape(received.shape[1:])


def scatter_sum_blocks(values):
    count = lax.axis_size("blk")
    rows, width = values.shape
    pieces = values.reshape(rows, count, width // count).transpose(1, 0, 2)
    received = lax.all_to_all(
        pieces.astype(jnp.bfloat16), "blk", split_axis=0, concat_axis=0, tiled=True
    )
    return jnp.sum(received.astype(jnp.float32), axis=0)


def per_device(
    hidden,
    attn_gain,
    qkv_weight,
    out_weight,
    kv_pool,
    page_table,
    cache_lens,
    ffn_gain,
    route_ids,
    route_weights,
    shared_gate_up,
    shared_down,
    expert_gate_up,
    expert_down,
):
    blocks = lax.axis_size("blk")
    groups = lax.axis_size("exp")
    block_index = lax.axis_index("blk")
    model_width = hidden.shape[1] * blocks
    query_width = HEADS * HEAD_DIM
    key_width = KV_HEADS * HEAD_DIM
    group_size = HEADS // KV_HEADS
    own_rows = NEW // blocks
    full_rows = gather_blocks(hidden, 1)
    attn_in = normalize(full_rows, attn_gain)
    projected = jnp.dot(attn_in, qkv_weight, preferred_element_type=jnp.float32).astype(
        jnp.bfloat16
    )
    projected_all = gather_blocks(projected, 1)
    length = cache_lens[0]
    positions = length + jnp.arange(NEW, dtype=jnp.int32)
    fresh_keys = rotate(
        projected_all[:, query_width : query_width + key_width]
        .astype(jnp.float32)
        .reshape(NEW, KV_HEADS, HEAD_DIM),
        positions,
    ).astype(jnp.bfloat16)
    appended = jnp.concatenate(
        [fresh_keys.reshape(NEW, key_width), projected_all[:, query_width + key_width :]], axis=1
    )
    page_map = page_table[0]
    pool_pages = page_map.shape[0]
    page_index = jnp.arange(pool_pages, dtype=jnp.int32)
    logical = jnp.sum(
        jnp.where(page_map[None, :] == page_index[:, None], page_index[None, :], 0), axis=1
    )
    local_pages = kv_pool.shape[1]
    local_logical = lax.dynamic_slice_in_dim(logical, block_index * local_pages, local_pages)
    slot_offsets = jnp.arange(PAGE, dtype=jnp.int32)
    local_pos = local_logical[:, None] * PAGE + slot_offsets[None, :]
    offset = local_pos - length
    written = (offset >= 0) & (offset < NEW)
    half_dim = HEAD_DIM // 2
    frequency = rope_base ** (-(jnp.arange(half_dim).astype(jnp.float32) * 2.0 / HEAD_DIM))
    angles = positions.astype(jnp.float32)[:, None] * frequency[None, :]
    cosine = jnp.cos(angles)
    sine_vals = jnp.sin(angles)
    cosine_full = jnp.concatenate([cosine, cosine], axis=1)
    sine_signed = jnp.concatenate([-sine_vals, sine_vals], axis=1)
    payload, slot_rows = local_attention(
        projected_all,
        cosine_full,
        sine_signed,
        kv_pool[0].reshape(local_pages * PAGE, 2 * key_width),
        appended,
        offset.reshape(-1),
        positions,
        local_pos.reshape(-1),
    )
    pool_out = slot_rows.reshape(local_pages, PAGE, 2 * key_width)
    payload = payload.reshape(blocks, own_rows, query_width + 128)
    gathered = lax.all_to_all(payload, "blk", split_axis=0, concat_axis=0, tiled=True)
    own_attention = combine_attention(gathered)
    attended = jnp.dot(
        gather_blocks(own_attention, 0),
        out_weight,
        preferred_element_type=jnp.float32,
    )
    mixed_cols = (hidden.astype(jnp.float32) + attended).astype(jnp.bfloat16)
    mixed_rows = gather_blocks(mixed_cols, 1)
    ffn_in = normalize(mixed_rows, ffn_gain)
    shared_cols = shared_gate_up.shape[2]
    gate_up = jnp.dot(
        ffn_in,
        shared_gate_up.reshape(model_width, 2 * shared_cols),
        preferred_element_type=jnp.float32,
    )
    shared_act = (jax.nn.silu(gate_up[:, :shared_cols]) * gate_up[:, shared_cols:]).astype(
        jnp.bfloat16
    )
    shared_term = jnp.dot(shared_act, shared_down, preferred_element_type=jnp.float32)
    row_experts = groups // SPLIT
    expert_count = row_experts * blocks
    capacity = NEW * TOPK * 4 // (expert_count * 3)
    row_expert_ids = block_index * row_experts + jnp.arange(row_experts, dtype=jnp.int32)
    route_hits = route_ids[:, :, None] == row_expert_ids[None, None, :]
    chosen = jnp.any(route_hits, axis=1)
    route_share = jnp.sum(jnp.where(route_hits, route_weights[:, :, None], 0.0), axis=1)
    slot_rank = jnp.cumsum(chosen.astype(jnp.int32), axis=0) - 1
    slot_ids = jnp.arange(capacity, dtype=jnp.int32)
    placed = chosen.T[:, None, :] & (slot_rank.T[:, None, :] == slot_ids[None, :, None])
    selector = placed.astype(jnp.bfloat16)
    outgoing = jnp.einsum(
        "ect,td->ecd", selector, ffn_in, preferred_element_type=jnp.float32
    ).astype(jnp.bfloat16)
    outgoing = jnp.repeat(outgoing, SPLIT, axis=0)
    received = lax.all_to_all(outgoing, "exp", split_axis=0, concat_axis=0, tiled=True)
    flat_rows = received.reshape(-1, model_width)
    expert_gu = jnp.dot(flat_rows, expert_gate_up[0], preferred_element_type=jnp.float32)
    activated = (jax.nn.silu(expert_gu[:, :FF_PART]) * expert_gu[:, FF_PART:]).astype(jnp.bfloat16)
    result = jnp.dot(activated, expert_down[0], preferred_element_type=jnp.float32).astype(
        jnp.bfloat16
    )
    returned = lax.all_to_all(
        result.reshape(received.shape), "exp", split_axis=0, concat_axis=0, tiled=True
    )
    summed = jnp.sum(
        returned.reshape(row_experts, SPLIT, capacity, model_width).astype(jnp.float32), axis=1
    )
    slot_weight = jnp.sum(placed.astype(jnp.float32) * route_share.T[:, None, :], axis=2)
    slot_values = summed * slot_weight[:, :, None]
    upper_part = slot_values.astype(jnp.bfloat16)
    lower_part = (slot_values - upper_part.astype(jnp.float32)).astype(jnp.bfloat16)
    routed = jnp.einsum(
        "ect,ecd->td", selector, upper_part, preferred_element_type=jnp.float32
    ) + jnp.einsum("ect,ecd->td", selector, lower_part, preferred_element_type=jnp.float32)
    layer_term = shared_term + routed
    summed_cols = scatter_sum_blocks(layer_term)
    hidden_out = (mixed_cols.astype(jnp.float32) + summed_cols).astype(jnp.bfloat16)
    return (hidden_out, pool_out[None])


def solution(mesh):
    placed = (
        P("exp", "blk"),
        P(),
        P(None, "blk"),
        P(None, "blk"),
        P("exp", "blk", None, None),
        P("exp", None),
        P("exp"),
        P(),
        P("exp", None),
        P("exp", None),
        P(None, None, "blk"),
        P("blk", None),
        P(("blk", "exp"), None, None),
        P(("blk", "exp"), None, None),
    )
    return jax.shard_map(
        per_device,
        mesh=mesh,
        in_specs=placed,
        out_specs=(P("exp", "blk"), P("exp", "blk", None, None)),
        check_vma=False,
    )
```

```python
import math

import jax
import jax.numpy as jnp
from jax import lax
from jax.experimental import pallas as pl
from jax.experimental.pallas import tpu as pltpu
from jax.sharding import PartitionSpec as P

HEADS = 20
KV_HEADS = 4
HEAD_DIM = 128
TOPK = 6
SPLIT = 4
PAGE = 128
NEW = 256
FF_PART = 384


rope_base = 500000.0
norm_eps = 1e-05


def normalize(inputs, gain_vec):
    values = inputs.astype(jnp.float32)
    inv_rms = lax.rsqrt(jnp.mean(values * values, axis=-1, keepdims=True) + norm_eps)
    return (values * inv_rms * gain_vec).astype(jnp.bfloat16)


def rotate(inputs, positions):
    half_dim = HEAD_DIM // 2
    frequency = rope_base ** (-(jnp.arange(half_dim).astype(jnp.float32) * 2.0 / HEAD_DIM))
    angles = positions.astype(jnp.float32)[:, None] * frequency[None, :]
    cosine = jnp.cos(angles)[:, None, :]
    sine_vals = jnp.sin(angles)[:, None, :]
    lower_half = inputs[..., :half_dim]
    upper_half = inputs[..., half_dim:]
    return jnp.concatenate(
        [
            lower_half * cosine - upper_half * sine_vals,
            upper_half * cosine + lower_half * sine_vals,
        ],
        axis=-1,
    )


def split_three(value):
    high = value.astype(jnp.bfloat16).astype(jnp.float32)
    rest = value - high
    middle = rest.astype(jnp.bfloat16).astype(jnp.float32)
    low = (rest - middle).astype(jnp.bfloat16).astype(jnp.float32)
    return [high, middle, low]


def query_columns(proj_ref, head):
    width = proj_ref.shape[2]
    first = head * HEAD_DIM
    last = first + HEAD_DIM
    pieces = []
    while first < last:
        source = first // width
        stop = min(last, (source + 1) * width)
        pieces.append(proj_ref[source, :, first - source * width : stop - source * width])
        first = stop
    return pieces[0] if len(pieces) == 1 else jnp.concatenate(pieces, axis=1)


def attention_kernel(
    proj_ref, cos_ref, sin_ref, cache_ref, fresh_ref, offset_ref, qpos_ref, kpos_ref, out_ref, slot_ref
):
    offsets = offset_ref[...]
    columns = lax.broadcasted_iota(jnp.int32, (offsets.shape[0], NEW), 1)
    chooser = jnp.where(offsets == columns, 1.0, 0.0).astype(jnp.bfloat16)
    picked = jnp.dot(chooser, fresh_ref[...], preferred_element_type=jnp.float32)
    written = (offsets >= 0) & (offsets < NEW)
    slot_ref[...] = jnp.where(written, picked.astype(slot_ref.dtype), cache_ref[...])
    key_width = KV_HEADS * HEAD_DIM
    group_size = HEADS // KV_HEADS
    allowed = kpos_ref[...] <= qpos_ref[...]
    group_allowed = jnp.concatenate([allowed] * group_size, axis=0)
    cosine = cos_ref[...]
    sine_signed = sin_ref[...]
    lane = lax.broadcasted_iota(jnp.int32, (NEW, 128), 1)
    stats = jnp.zeros((NEW, 128), jnp.float32)
    for kv in range(KV_HEADS):
        rotated = []
        for member in range(group_size):
            head = kv * group_size + member
            raw = query_columns(proj_ref, head).astype(jnp.float32)
            swapped = pltpu.roll(raw, HEAD_DIM // 2, 1)
            rotated.append((raw * cosine + swapped * sine_signed).astype(jnp.bfloat16))
        query = jnp.concatenate(rotated, axis=0)
        keys = slot_ref[:, kv * HEAD_DIM : (kv + 1) * HEAD_DIM]
        values = slot_ref[:, key_width + kv * HEAD_DIM : key_width + (kv + 1) * HEAD_DIM]
        scores = lax.dot_general(
            query, keys, (((1,), (1,)), ((), ())), preferred_element_type=jnp.float32
        ) * (1.0 / math.sqrt(HEAD_DIM))
        scores = jnp.where(group_allowed, scores, -1e30)
        peak = jnp.max(scores, axis=1, keepdims=True)
        probs = jnp.exp(scores - peak)
        live = jnp.where(peak > -1e29, 1.0, 0.0)
        total = jnp.sum(probs, axis=1, keepdims=True) * live
        weighted = (
            jnp.dot(probs.astype(jnp.bfloat16), values, preferred_element_type=jnp.float32) * live
        )
        for member in range(group_size):
            head = kv * group_size + member
            rows = slice(member * NEW, (member + 1) * NEW)
            out_ref[:, head * HEAD_DIM : (head + 1) * HEAD_DIM] = weighted[rows].astype(
                out_ref.dtype
            )
            pieces = split_three(peak[rows]) + split_three(total[rows])
            for slot, value in enumerate(pieces):
                stats = jnp.where(lane == slot * HEADS + head, value, stats)
    out_ref[:, HEADS * HEAD_DIM :] = stats.astype(out_ref.dtype)


def local_attention(projected_all, cosine, sine_signed, cache_rows, fresh, offsets, positions, key_pos):
    width = HEADS * HEAD_DIM + 128
    return pl.pallas_call(
        attention_kernel,
        out_shape=(
            jax.ShapeDtypeStruct((NEW, width), jnp.bfloat16),
            jax.ShapeDtypeStruct(cache_rows.shape, cache_rows.dtype),
        ),
        in_specs=[pl.BlockSpec(memory_space=pltpu.VMEM)] * 8,
        out_specs=(pl.BlockSpec(memory_space=pltpu.VMEM), pl.BlockSpec(memory_space=pltpu.VMEM)),
        cost_estimate=pl.CostEstimate(
            flops=4 * NEW * cache_rows.shape[0] * HEAD_DIM * HEADS,
            transcendentals=NEW * cache_rows.shape[0] * HEADS,
            bytes_accessed=NEW * width * 2 + cache_rows.size * 4 + projected_all.size * 2,
        ),
    )(
        projected_all,
        cosine,
        sine_signed,
        cache_rows,
        fresh,
        offsets[:, None],
        positions[:, None],
        key_pos[None, :],
    )


def combine_kernel(part_ref, out_ref):
    coded = part_ref[:, :, HEADS * HEAD_DIM :].astype(jnp.float32)
    lane_count = coded.shape[2]

    def shifted(piece):
        return pltpu.roll(coded, lane_count - piece * HEADS, 2)

    peak = (coded + shifted(1)) + shifted(2)
    total = (shifted(3) + shifted(4)) + shifted(5)
    factors = jnp.exp(peak - jnp.max(peak, axis=0, keepdims=True))
    denominators = jnp.sum(factors * total, axis=0)
    lane = lax.broadcasted_iota(jnp.int32, coded.shape, 2)
    for head in range(HEADS):
        factor = jnp.sum(jnp.where(lane == head, factors, 0.0), axis=2, keepdims=True)
        denominator = jnp.sum(jnp.where(lane[0] == head, denominators, 0.0), axis=1, keepdims=True)
        numerator = jnp.sum(
            part_ref[:, :, head * HEAD_DIM : (head + 1) * HEAD_DIM].astype(jnp.float32) * factor,
            axis=0,
        )
        out_ref[:, head * HEAD_DIM : (head + 1) * HEAD_DIM] = (
            numerator / denominator
        ).astype(out_ref.dtype)


def combine_attention(parts):
    sources, rows, width = parts.shape
    return pl.pallas_call(
        combine_kernel,
        out_shape=jax.ShapeDtypeStruct((rows, HEADS * HEAD_DIM), jnp.bfloat16),
        in_specs=[pl.BlockSpec(memory_space=pltpu.VMEM)],
        out_specs=pl.BlockSpec(memory_space=pltpu.VMEM),
        cost_estimate=pl.CostEstimate(
            flops=3 * parts.size, transcendentals=sources * rows * 128,
            bytes_accessed=parts.size * 2 + rows * HEADS * HEAD_DIM * 2,
        ),
    )(parts)


def gather_blocks(values, axis):
    count = lax.axis_size("blk")
    stacked = jnp.broadcast_to(values[None], (count,) + values.shape)
    received = lax.all_to_all(stacked, "blk", split_axis=0, concat_axis=axis + 1, tiled=True)
    return received.reshape(received.shape[1:])


def scatter_sum_blocks(values):
    count = lax.axis_size("blk")
    rows, width = values.shape
    pieces = values.reshape(rows, count, width // count).transpose(1, 0, 2)
    received = lax.all_to_all(
        pieces.astype(jnp.bfloat16), "blk", split_axis=0, concat_axis=0, tiled=True
    )
    return jnp.sum(received.astype(jnp.float32), axis=0)


def per_device(
    hidden,
    attn_gain,
    qkv_weight,
    out_weight,
    kv_pool,
    page_table,
    cache_lens,
    ffn_gain,
    route_ids,
    route_weights,
    shared_gate_up,
    shared_down,
    expert_gate_up,
    expert_down,
):
    blocks = lax.axis_size("blk")
    groups = lax.axis_size("exp")
    block_index = lax.axis_index("blk")
    model_width = hidden.shape[1] * blocks
    query_width = HEADS * HEAD_DIM
    key_width = KV_HEADS * HEAD_DIM
    group_size = HEADS // KV_HEADS
    own_rows = NEW // blocks
    full_rows = gather_blocks(hidden, 1)
    attn_in = normalize(full_rows, attn_gain)
    projected = jnp.dot(attn_in, qkv_weight, preferred_element_type=jnp.float32).astype(
        jnp.bfloat16
    )
    projected_blocks = lax.all_to_all(
        jnp.broadcast_to(projected[None], (blocks,) + projected.shape),
        "blk", split_axis=0, concat_axis=0, tiled=True,
    )
    projected_all = projected_blocks.transpose(1, 0, 2).reshape(NEW, -1)
    length = cache_lens[0]
    positions = length + jnp.arange(NEW, dtype=jnp.int32)
    fresh_keys = rotate(
        projected_all[:, query_width : query_width + key_width]
        .astype(jnp.float32)
        .reshape(NEW, KV_HEADS, HEAD_DIM),
        positions,
    ).astype(jnp.bfloat16)
    appended = jnp.concatenate(
        [fresh_keys.reshape(NEW, key_width), projected_all[:, query_width + key_width :]], axis=1
    )
    page_map = page_table[0]
    pool_pages = page_map.shape[0]
    page_index = jnp.arange(pool_pages, dtype=jnp.int32)
    logical = jnp.sum(
        jnp.where(page_map[None, :] == page_index[:, None], page_index[None, :], 0), axis=1
    )
    local_pages = kv_pool.shape[1]
    local_logical = lax.dynamic_slice_in_dim(logical, block_index * local_pages, local_pages)
    slot_offsets = jnp.arange(PAGE, dtype=jnp.int32)
    local_pos = local_logical[:, None] * PAGE + slot_offsets[None, :]
    offset = local_pos - length
    written = (offset >= 0) & (offset < NEW)
    half_dim = HEAD_DIM // 2
    frequency = rope_base ** (-(jnp.arange(half_dim).astype(jnp.float32) * 2.0 / HEAD_DIM))
    angles = positions.astype(jnp.float32)[:, None] * frequency[None, :]
    cosine = jnp.cos(angles)
    sine_vals = jnp.sin(angles)
    cosine_full = jnp.concatenate([cosine, cosine], axis=1)
    sine_signed = jnp.concatenate([-sine_vals, sine_vals], axis=1)
    payload, slot_rows = local_attention(
        projected_blocks,
        cosine_full,
        sine_signed,
        kv_pool[0].reshape(local_pages * PAGE, 2 * key_width),
        appended,
        offset.reshape(-1),
        positions,
        local_pos.reshape(-1),
    )
    pool_out = slot_rows.reshape(local_pages, PAGE, 2 * key_width)
    payload = payload.reshape(blocks, own_rows, query_width + 128)
    gathered = lax.all_to_all(payload, "blk", split_axis=0, concat_axis=0, tiled=True)
    own_attention = combine_attention(gathered)
    attended = jnp.dot(
        gather_blocks(own_attention, 0),
        out_weight,
        preferred_element_type=jnp.float32,
    )
    mixed_cols = (hidden.astype(jnp.float32) + attended).astype(jnp.bfloat16)
    mixed_rows = gather_blocks(mixed_cols, 1)
    ffn_in = normalize(mixed_rows, ffn_gain)
    shared_cols = shared_gate_up.shape[2]
    gate_up = jnp.dot(
        ffn_in,
        shared_gate_up.reshape(model_width, 2 * shared_cols),
        preferred_element_type=jnp.float32,
    )
    shared_act = (jax.nn.silu(gate_up[:, :shared_cols]) * gate_up[:, shared_cols:]).astype(
        jnp.bfloat16
    )
    shared_term = jnp.dot(shared_act, shared_down, preferred_element_type=jnp.float32)
    row_experts = groups // SPLIT
    expert_count = row_experts * blocks
    capacity = NEW * TOPK * 4 // (expert_count * 3)
    row_expert_ids = block_index * row_experts + jnp.arange(row_experts, dtype=jnp.int32)
    route_hits = route_ids[:, :, None] == row_expert_ids[None, None, :]
    chosen = jnp.any(route_hits, axis=1)
    route_share = jnp.sum(jnp.where(route_hits, route_weights[:, :, None], 0.0), axis=1)
    slot_rank = jnp.cumsum(chosen.astype(jnp.int32), axis=0) - 1
    slot_ids = jnp.arange(capacity, dtype=jnp.int32)
    placed = chosen.T[:, None, :] & (slot_rank.T[:, None, :] == slot_ids[None, :, None])
    selector = placed.astype(jnp.bfloat16)
    outgoing = jnp.einsum(
        "ect,td->ecd", selector, ffn_in, preferred_element_type=jnp.float32
    ).astype(jnp.bfloat16)
    outgoing = jnp.repeat(outgoing, SPLIT, axis=0)
    received = lax.all_to_all(outgoing, "exp", split_axis=0, concat_axis=0, tiled=True)
    flat_rows = received.reshape(-1, model_width)
    expert_gu = jnp.dot(flat_rows, expert_gate_up[0], preferred_element_type=jnp.float32)
    activated = (jax.nn.silu(expert_gu[:, :FF_PART]) * expert_gu[:, FF_PART:]).astype(jnp.bfloat16)
    result = jnp.dot(activated, expert_down[0], preferred_element_type=jnp.float32).astype(
        jnp.bfloat16
    )
    returned = lax.all_to_all(
        result.reshape(received.shape), "exp", split_axis=0, concat_axis=0, tiled=True
    )
    summed = jnp.sum(
        returned.reshape(row_experts, SPLIT, capacity, model_width).astype(jnp.float32), axis=1
    )
    slot_weight = jnp.sum(placed.astype(jnp.float32) * route_share.T[:, None, :], axis=2)
    slot_values = summed * slot_weight[:, :, None]
    upper_part = slot_values.astype(jnp.bfloat16)
    lower_part = (slot_values - upper_part.astype(jnp.float32)).astype(jnp.bfloat16)
    routed = jnp.einsum(
        "ect,ecd->td", selector, upper_part, preferred_element_type=jnp.float32
    ) + jnp.einsum("ect,ecd->td", selector, lower_part, preferred_element_type=jnp.float32)
    layer_term = shared_term + routed
    summed_cols = scatter_sum_blocks(layer_term)
    hidden_out = (mixed_cols.astype(jnp.float32) + summed_cols).astype(jnp.bfloat16)
    return (hidden_out, pool_out[None])


def solution(mesh):
    placed = (
        P("exp", "blk"),
        P(),
        P(None, "blk"),
        P(None, "blk"),
        P("exp", "blk", None, None),
        P("exp", None),
        P("exp"),
        P(),
        P("exp", None),
        P("exp", None),
        P(None, None, "blk"),
        P("blk", None),
        P(("blk", "exp"), None, None),
        P(("blk", "exp"), None, None),
    )
    return jax.shard_map(
        per_device,
        mesh=mesh,
        in_specs=placed,
        out_specs=(P("exp", "blk"), P("exp", "blk", None, None)),
        check_vma=False,
    )
```

```python
import math

import jax
import jax.numpy as jnp
from jax import lax
from jax.experimental import pallas as pl
from jax.experimental.pallas import tpu as pltpu
from jax.sharding import PartitionSpec as P

HEADS = 20
KV_HEADS = 4
HEAD_DIM = 128
TOPK = 6
SPLIT = 4
PAGE = 128
NEW = 256
FF_PART = 384


rope_base = 500000.0
norm_eps = 1e-05


def normalize(inputs, gain_vec):
    values = inputs.astype(jnp.float32)
    inv_rms = lax.rsqrt(jnp.mean(values * values, axis=-1, keepdims=True) + norm_eps)
    return (values * inv_rms * gain_vec).astype(jnp.bfloat16)


def rotate(inputs, positions):
    half_dim = HEAD_DIM // 2
    frequency = rope_base ** (-(jnp.arange(half_dim).astype(jnp.float32) * 2.0 / HEAD_DIM))
    angles = positions.astype(jnp.float32)[:, None] * frequency[None, :]
    cosine = jnp.cos(angles)[:, None, :]
    sine_vals = jnp.sin(angles)[:, None, :]
    lower_half = inputs[..., :half_dim]
    upper_half = inputs[..., half_dim:]
    return jnp.concatenate(
        [
            lower_half * cosine - upper_half * sine_vals,
            upper_half * cosine + lower_half * sine_vals,
        ],
        axis=-1,
    )


def split_three(value):
    high = value.astype(jnp.bfloat16).astype(jnp.float32)
    rest = value - high
    middle = rest.astype(jnp.bfloat16).astype(jnp.float32)
    low = (rest - middle).astype(jnp.bfloat16).astype(jnp.float32)
    return [high, middle, low]


def attention_kernel(
    proj_ref, cos_ref, sin_ref, cache_ref, fresh_ref, offset_ref, qpos_ref, kpos_ref, out_ref, slot_ref
):
    offsets = offset_ref[...]
    columns = lax.broadcasted_iota(jnp.int32, (offsets.shape[0], NEW), 1)
    chooser = jnp.where(offsets == columns, 1.0, 0.0).astype(jnp.bfloat16)
    picked = jnp.dot(chooser, fresh_ref[...], preferred_element_type=jnp.float32)
    written = (offsets >= 0) & (offsets < NEW)
    slot_ref[...] = jnp.where(written, picked.astype(slot_ref.dtype), cache_ref[...])
    key_width = KV_HEADS * HEAD_DIM
    group_size = HEADS // KV_HEADS
    allowed = kpos_ref[...] <= qpos_ref[...]
    group_allowed = jnp.concatenate([allowed] * group_size, axis=0)
    cosine = cos_ref[...]
    sine_signed = sin_ref[...]
    lane = lax.broadcasted_iota(jnp.int32, (NEW, 128), 1)
    stats = jnp.zeros((NEW, 128), jnp.float32)
    for kv in range(KV_HEADS):
        rotated = []
        for member in range(group_size):
            head = kv * group_size + member
            raw = proj_ref[:, head * HEAD_DIM : (head + 1) * HEAD_DIM].astype(jnp.float32)
            swapped = pltpu.roll(raw, HEAD_DIM // 2, 1)
            rotated.append((raw * cosine + swapped * sine_signed).astype(jnp.bfloat16))
        query = jnp.concatenate(rotated, axis=0)
        keys = slot_ref[:, kv * HEAD_DIM : (kv + 1) * HEAD_DIM]
        values = slot_ref[:, key_width + kv * HEAD_DIM : key_width + (kv + 1) * HEAD_DIM]
        scores = lax.dot_general(
            query, keys, (((1,), (1,)), ((), ())), preferred_element_type=jnp.float32
        ) * (1.0 / math.sqrt(HEAD_DIM))
        scores = jnp.where(group_allowed, scores, -1e30)
        peak = jnp.max(scores, axis=1, keepdims=True)
        probs = jnp.exp(scores - peak)
        live = jnp.where(peak > -1e29, 1.0, 0.0)
        total = jnp.sum(probs, axis=1, keepdims=True) * live
        weighted = (
            jnp.dot(probs.astype(jnp.bfloat16), values, preferred_element_type=jnp.float32) * live
        )
        for member in range(group_size):
            head = kv * group_size + member
            rows = slice(member * NEW, (member + 1) * NEW)
            out_ref[:, head * HEAD_DIM : (head + 1) * HEAD_DIM] = weighted[rows].astype(
                out_ref.dtype
            )
            pieces = split_three(peak[rows]) + split_three(total[rows])
            for slot, value in enumerate(pieces):
                stats = jnp.where(lane == slot * HEADS + head, value, stats)
    out_ref[:, HEADS * HEAD_DIM :] = stats.astype(out_ref.dtype)


def local_attention(projected_all, cosine, sine_signed, cache_rows, fresh, offsets, positions, key_pos):
    width = HEADS * HEAD_DIM + 128
    return pl.pallas_call(
        attention_kernel,
        out_shape=(
            jax.ShapeDtypeStruct((NEW, width), jnp.bfloat16),
            jax.ShapeDtypeStruct(cache_rows.shape, cache_rows.dtype),
        ),
        in_specs=[pl.BlockSpec(memory_space=pltpu.VMEM)] * 8,
        out_specs=(pl.BlockSpec(memory_space=pltpu.VMEM), pl.BlockSpec(memory_space=pltpu.VMEM)),
        cost_estimate=pl.CostEstimate(
            flops=4 * NEW * cache_rows.shape[0] * HEAD_DIM * HEADS,
            transcendentals=NEW * cache_rows.shape[0] * HEADS,
            bytes_accessed=NEW * width * 2 + cache_rows.size * 4 + projected_all.size * 2,
        ),
    )(
        projected_all,
        cosine,
        sine_signed,
        cache_rows,
        fresh,
        offsets[:, None],
        positions[:, None],
        key_pos[None, :],
    )


def combine_kernel(part_ref, out_ref):
    coded = part_ref[:, :, HEADS * HEAD_DIM :].astype(jnp.float32)
    lane_count = coded.shape[2]

    def shifted(piece):
        return pltpu.roll(coded, lane_count - piece * HEADS, 2)

    peak = (coded + shifted(1)) + shifted(2)
    total = (shifted(3) + shifted(4)) + shifted(5)
    factors = jnp.exp(peak - jnp.max(peak, axis=0, keepdims=True))
    denominators = jnp.sum(factors * total, axis=0)
    lane = lax.broadcasted_iota(jnp.int32, coded.shape, 2)
    for head in range(HEADS):
        factor = jnp.sum(jnp.where(lane == head, factors, 0.0), axis=2, keepdims=True)
        denominator = jnp.sum(jnp.where(lane[0] == head, denominators, 0.0), axis=1, keepdims=True)
        numerator = jnp.sum(
            part_ref[:, :, head * HEAD_DIM : (head + 1) * HEAD_DIM].astype(jnp.float32) * factor,
            axis=0,
        )
        result = (numerator / denominator).astype(out_ref.dtype)
        out_ref[:, :, head * HEAD_DIM : (head + 1) * HEAD_DIM] = jnp.broadcast_to(
            result[None], (out_ref.shape[0],) + result.shape
        )


def combine_attention(parts):
    sources, rows, width = parts.shape
    return pl.pallas_call(
        combine_kernel,
        out_shape=jax.ShapeDtypeStruct((sources, rows, HEADS * HEAD_DIM), jnp.bfloat16),
        in_specs=[pl.BlockSpec(memory_space=pltpu.VMEM)],
        out_specs=pl.BlockSpec(memory_space=pltpu.VMEM),
        cost_estimate=pl.CostEstimate(
            flops=3 * parts.size, transcendentals=sources * rows * 128,
            bytes_accessed=parts.size * 2 + sources * rows * HEADS * HEAD_DIM * 2,
        ),
    )(parts)


def gather_blocks(values, axis):
    count = lax.axis_size("blk")
    stacked = jnp.broadcast_to(values[None], (count,) + values.shape)
    received = lax.all_to_all(stacked, "blk", split_axis=0, concat_axis=axis + 1, tiled=True)
    return received.reshape(received.shape[1:])


def scatter_sum_blocks(values):
    count = lax.axis_size("blk")
    rows, width = values.shape
    pieces = values.reshape(rows, count, width // count).transpose(1, 0, 2)
    received = lax.all_to_all(
        pieces.astype(jnp.bfloat16), "blk", split_axis=0, concat_axis=0, tiled=True
    )
    return jnp.sum(received.astype(jnp.float32), axis=0)


def per_device(
    hidden,
    attn_gain,
    qkv_weight,
    out_weight,
    kv_pool,
    page_table,
    cache_lens,
    ffn_gain,
    route_ids,
    route_weights,
    shared_gate_up,
    shared_down,
    expert_gate_up,
    expert_down,
):
    blocks = lax.axis_size("blk")
    groups = lax.axis_size("exp")
    block_index = lax.axis_index("blk")
    model_width = hidden.shape[1] * blocks
    query_width = HEADS * HEAD_DIM
    key_width = KV_HEADS * HEAD_DIM
    group_size = HEADS // KV_HEADS
    own_rows = NEW // blocks
    full_rows = gather_blocks(hidden, 1)
    attn_in = normalize(full_rows, attn_gain)
    projected = jnp.dot(attn_in, qkv_weight, preferred_element_type=jnp.float32).astype(
        jnp.bfloat16
    )
    projected_all = gather_blocks(projected, 1)
    length = cache_lens[0]
    positions = length + jnp.arange(NEW, dtype=jnp.int32)
    fresh_keys = rotate(
        projected_all[:, query_width : query_width + key_width]
        .astype(jnp.float32)
        .reshape(NEW, KV_HEADS, HEAD_DIM),
        positions,
    ).astype(jnp.bfloat16)
    appended = jnp.concatenate(
        [fresh_keys.reshape(NEW, key_width), projected_all[:, query_width + key_width :]], axis=1
    )
    page_map = page_table[0]
    pool_pages = page_map.shape[0]
    page_index = jnp.arange(pool_pages, dtype=jnp.int32)
    logical = jnp.sum(
        jnp.where(page_map[None, :] == page_index[:, None], page_index[None, :], 0), axis=1
    )
    local_pages = kv_pool.shape[1]
    local_logical = lax.dynamic_slice_in_dim(logical, block_index * local_pages, local_pages)
    slot_offsets = jnp.arange(PAGE, dtype=jnp.int32)
    local_pos = local_logical[:, None] * PAGE + slot_offsets[None, :]
    offset = local_pos - length
    written = (offset >= 0) & (offset < NEW)
    half_dim = HEAD_DIM // 2
    frequency = rope_base ** (-(jnp.arange(half_dim).astype(jnp.float32) * 2.0 / HEAD_DIM))
    angles = positions.astype(jnp.float32)[:, None] * frequency[None, :]
    cosine = jnp.cos(angles)
    sine_vals = jnp.sin(angles)
    cosine_full = jnp.concatenate([cosine, cosine], axis=1)
    sine_signed = jnp.concatenate([-sine_vals, sine_vals], axis=1)
    payload, slot_rows = local_attention(
        projected_all,
        cosine_full,
        sine_signed,
        kv_pool[0].reshape(local_pages * PAGE, 2 * key_width),
        appended,
        offset.reshape(-1),
        positions,
        local_pos.reshape(-1),
    )
    pool_out = slot_rows.reshape(local_pages, PAGE, 2 * key_width)
    payload = payload.reshape(blocks, own_rows, query_width + 128)
    gathered = lax.all_to_all(payload, "blk", split_axis=0, concat_axis=0, tiled=True)
    own_attention = combine_attention(gathered)
    attended = jnp.dot(
        lax.all_to_all(own_attention, "blk", split_axis=0, concat_axis=0, tiled=True).reshape(NEW, query_width),
        out_weight,
        preferred_element_type=jnp.float32,
    )
    mixed_cols = (hidden.astype(jnp.float32) + attended).astype(jnp.bfloat16)
    mixed_rows = gather_blocks(mixed_cols, 1)
    ffn_in = normalize(mixed_rows, ffn_gain)
    shared_cols = shared_gate_up.shape[2]
    gate_up = jnp.dot(
        ffn_in,
        shared_gate_up.reshape(model_width, 2 * shared_cols),
        preferred_element_type=jnp.float32,
    )
    shared_act = (jax.nn.silu(gate_up[:, :shared_cols]) * gate_up[:, shared_cols:]).astype(
        jnp.bfloat16
    )
    shared_term = jnp.dot(shared_act, shared_down, preferred_element_type=jnp.float32)
    row_experts = groups // SPLIT
    expert_count = row_experts * blocks
    capacity = NEW * TOPK * 4 // (expert_count * 3)
    row_expert_ids = block_index * row_experts + jnp.arange(row_experts, dtype=jnp.int32)
    route_hits = route_ids[:, :, None] == row_expert_ids[None, None, :]
    chosen = jnp.any(route_hits, axis=1)
    route_share = jnp.sum(jnp.where(route_hits, route_weights[:, :, None], 0.0), axis=1)
    slot_rank = jnp.cumsum(chosen.astype(jnp.int32), axis=0) - 1
    slot_ids = jnp.arange(capacity, dtype=jnp.int32)
    placed = chosen.T[:, None, :] & (slot_rank.T[:, None, :] == slot_ids[None, :, None])
    selector = placed.astype(jnp.bfloat16)
    outgoing = jnp.einsum(
        "ect,td->ecd", selector, ffn_in, preferred_element_type=jnp.float32
    ).astype(jnp.bfloat16)
    outgoing = jnp.repeat(outgoing, SPLIT, axis=0)
    received = lax.all_to_all(outgoing, "exp", split_axis=0, concat_axis=0, tiled=True)
    flat_rows = received.reshape(-1, model_width)
    expert_gu = jnp.dot(flat_rows, expert_gate_up[0], preferred_element_type=jnp.float32)
    activated = (jax.nn.silu(expert_gu[:, :FF_PART]) * expert_gu[:, FF_PART:]).astype(jnp.bfloat16)
    result = jnp.dot(activated, expert_down[0], preferred_element_type=jnp.float32).astype(
        jnp.bfloat16
    )
    returned = lax.all_to_all(
        result.reshape(received.shape), "exp", split_axis=0, concat_axis=0, tiled=True
    )
    summed = jnp.sum(
        returned.reshape(row_experts, SPLIT, capacity, model_width).astype(jnp.float32), axis=1
    )
    slot_weight = jnp.sum(placed.astype(jnp.float32) * route_share.T[:, None, :], axis=2)
    slot_values = summed * slot_weight[:, :, None]
    upper_part = slot_values.astype(jnp.bfloat16)
    lower_part = (slot_values - upper_part.astype(jnp.float32)).astype(jnp.bfloat16)
    routed = jnp.einsum(
        "ect,ecd->td", selector, upper_part, preferred_element_type=jnp.float32
    ) + jnp.einsum("ect,ecd->td", selector, lower_part, preferred_element_type=jnp.float32)
    layer_term = shared_term + routed
    summed_cols = scatter_sum_blocks(layer_term)
    hidden_out = (mixed_cols.astype(jnp.float32) + summed_cols).astype(jnp.bfloat16)
    return (hidden_out, pool_out[None])


def solution(mesh):
    placed = (
        P("exp", "blk"),
        P(),
        P(None, "blk"),
        P(None, "blk"),
        P("exp", "blk", None, None),
        P("exp", None),
        P("exp"),
        P(),
        P("exp", None),
        P("exp", None),
        P(None, None, "blk"),
        P("blk", None),
        P(("blk", "exp"), None, None),
        P(("blk", "exp"), None, None),
    )
    return jax.shard_map(
        per_device,
        mesh=mesh,
        in_specs=placed,
        out_specs=(P("exp", "blk"), P("exp", "blk", None, None)),
        check_vma=False,
    )
```

```python
import math

import jax
import jax.numpy as jnp
from jax import lax
from jax.experimental import pallas as pl
from jax.experimental.pallas import tpu as pltpu
from jax.sharding import PartitionSpec as P

HEADS = 20
KV_HEADS = 4
HEAD_DIM = 128
TOPK = 6
SPLIT = 4
PAGE = 128
NEW = 256
FF_PART = 384


rope_base = 500000.0
norm_eps = 1e-05


def normalize(inputs, gain_vec):
    values = inputs.astype(jnp.float32)
    inv_rms = lax.rsqrt(jnp.mean(values * values, axis=-1, keepdims=True) + norm_eps)
    return (values * inv_rms * gain_vec).astype(jnp.bfloat16)


def rotate(inputs, positions):
    half_dim = HEAD_DIM // 2
    frequency = rope_base ** (-(jnp.arange(half_dim).astype(jnp.float32) * 2.0 / HEAD_DIM))
    angles = positions.astype(jnp.float32)[:, None] * frequency[None, :]
    cosine = jnp.cos(angles)[:, None, :]
    sine_vals = jnp.sin(angles)[:, None, :]
    lower_half = inputs[..., :half_dim]
    upper_half = inputs[..., half_dim:]
    return jnp.concatenate(
        [
            lower_half * cosine - upper_half * sine_vals,
            upper_half * cosine + lower_half * sine_vals,
        ],
        axis=-1,
    )


def split_three(value):
    high = value.astype(jnp.bfloat16).astype(jnp.float32)
    rest = value - high
    middle = rest.astype(jnp.bfloat16).astype(jnp.float32)
    low = (rest - middle).astype(jnp.bfloat16).astype(jnp.float32)
    return [high, middle, low]


def attention_kernel(
    proj_ref, cos_ref, sin_ref, cache_ref, fresh_ref, offset_ref, qpos_ref, kpos_ref, out_ref, slot_ref
):
    offsets = offset_ref[...]
    columns = lax.broadcasted_iota(jnp.int32, (offsets.shape[0], NEW), 1)
    chooser = jnp.where(offsets == columns, 1.0, 0.0).astype(jnp.bfloat16)
    picked = jnp.dot(chooser, fresh_ref[...], preferred_element_type=jnp.float32)
    written = (offsets >= 0) & (offsets < NEW)
    slot_ref[...] = jnp.where(written, picked.astype(slot_ref.dtype), cache_ref[...])
    key_width = KV_HEADS * HEAD_DIM
    group_size = HEADS // KV_HEADS
    allowed = kpos_ref[...] <= qpos_ref[...]
    group_allowed = jnp.concatenate([allowed] * group_size, axis=0)
    cosine = cos_ref[...]
    sine_signed = sin_ref[...]
    lane = lax.broadcasted_iota(jnp.int32, (NEW, 128), 1)
    stats = jnp.zeros((NEW, 128), jnp.float32)
    for kv in range(KV_HEADS):
        rotated = []
        for member in range(group_size):
            head = kv * group_size + member
            raw = proj_ref[:, head * HEAD_DIM : (head + 1) * HEAD_DIM].astype(jnp.float32)
            swapped = pltpu.roll(raw, HEAD_DIM // 2, 1)
            rotated.append((raw * cosine + swapped * sine_signed).astype(jnp.bfloat16))
        query = jnp.concatenate(rotated, axis=0)
        keys = slot_ref[:, kv * HEAD_DIM : (kv + 1) * HEAD_DIM]
        values = slot_ref[:, key_width + kv * HEAD_DIM : key_width + (kv + 1) * HEAD_DIM]
        scores = lax.dot_general(
            query, keys, (((1,), (1,)), ((), ())), preferred_element_type=jnp.float32
        ) * (1.0 / math.sqrt(HEAD_DIM))
        scores = jnp.where(group_allowed, scores, -1e30)
        peak = jnp.max(scores, axis=1, keepdims=True)
        probs = jnp.exp(scores - peak)
        live = jnp.where(peak > -1e29, 1.0, 0.0)
        total = jnp.sum(probs, axis=1, keepdims=True) * live
        weighted = (
            jnp.dot(probs.astype(jnp.bfloat16), values, preferred_element_type=jnp.float32) * live
        )
        for member in range(group_size):
            head = kv * group_size + member
            rows = slice(member * NEW, (member + 1) * NEW)
            out_ref[:, head * HEAD_DIM : (head + 1) * HEAD_DIM] = weighted[rows].astype(
                out_ref.dtype
            )
            pieces = split_three(peak[rows]) + split_three(total[rows])
            for slot, value in enumerate(pieces):
                stats = jnp.where(lane == slot * HEADS + head, value, stats)
    out_ref[:, HEADS * HEAD_DIM :] = stats.astype(out_ref.dtype)


def local_attention(projected_all, cosine, sine_signed, cache_rows, fresh, offsets, positions, key_pos):
    width = HEADS * HEAD_DIM + 128
    return pl.pallas_call(
        attention_kernel,
        out_shape=(
            jax.ShapeDtypeStruct((NEW, width), jnp.bfloat16),
            jax.ShapeDtypeStruct(cache_rows.shape, cache_rows.dtype),
        ),
        in_specs=[pl.BlockSpec(memory_space=pltpu.VMEM)] * 8,
        out_specs=(pl.BlockSpec(memory_space=pltpu.VMEM), pl.BlockSpec(memory_space=pltpu.VMEM)),
        cost_estimate=pl.CostEstimate(
            flops=4 * NEW * cache_rows.shape[0] * HEAD_DIM * HEADS,
            transcendentals=NEW * cache_rows.shape[0] * HEADS,
            bytes_accessed=NEW * width * 2 + cache_rows.size * 4 + projected_all.size * 2,
        ),
    )(
        projected_all,
        cosine,
        sine_signed,
        cache_rows,
        fresh,
        offsets[:, None],
        positions[:, None],
        key_pos[None, :],
    )


def combine_kernel(part_ref, out_ref):
    coded = part_ref[:, :, HEADS * HEAD_DIM :].astype(jnp.float32)
    lane_count = coded.shape[2]

    def shifted(piece):
        return pltpu.roll(coded, lane_count - piece * HEADS, 2)

    peak = (coded + shifted(1)) + shifted(2)
    total = (shifted(3) + shifted(4)) + shifted(5)
    factors = jnp.exp(peak - jnp.max(peak, axis=0, keepdims=True))
    denominators = jnp.sum(factors * total, axis=0)
    lane = lax.broadcasted_iota(jnp.int32, coded.shape, 2)
    for head in range(HEADS):
        factor = jnp.sum(jnp.where(lane == head, factors, 0.0), axis=2, keepdims=True)
        denominator = jnp.sum(jnp.where(lane[0] == head, denominators, 0.0), axis=1, keepdims=True)
        numerator = jnp.sum(
            part_ref[:, :, head * HEAD_DIM : (head + 1) * HEAD_DIM].astype(jnp.float32) * factor,
            axis=0,
        )
        result = (numerator / denominator).astype(out_ref.dtype)
        out_ref[:, :, head * HEAD_DIM : (head + 1) * HEAD_DIM] = jnp.broadcast_to(
            result[None], (out_ref.shape[0],) + result.shape
        )


def combine_attention(parts):
    sources, rows, width = parts.shape
    return pl.pallas_call(
        combine_kernel,
        out_shape=jax.ShapeDtypeStruct((sources, rows, HEADS * HEAD_DIM), jnp.bfloat16),
        in_specs=[pl.BlockSpec(memory_space=pltpu.VMEM)],
        out_specs=pl.BlockSpec(memory_space=pltpu.VMEM),
        cost_estimate=pl.CostEstimate(
            flops=3 * parts.size, transcendentals=sources * rows * 128,
            bytes_accessed=parts.size * 2 + sources * rows * HEADS * HEAD_DIM * 2,
        ),
    )(parts)


def gather_blocks(values, axis):
    count = lax.axis_size("blk")
    stacked = jnp.broadcast_to(values[None], (count,) + values.shape)
    received = lax.all_to_all(stacked, "blk", split_axis=0, concat_axis=axis + 1, tiled=True)
    return received.reshape(received.shape[1:])


def scatter_sum_blocks(values):
    count = lax.axis_size("blk")
    rows, width = values.shape
    pieces = values.reshape(rows, count, width // count).transpose(1, 0, 2)
    received = lax.all_to_all(
        pieces.astype(jnp.bfloat16), "blk", split_axis=0, concat_axis=0, tiled=True
    )
    return jnp.sum(received.astype(jnp.float32), axis=0)


def per_device(
    hidden,
    attn_gain,
    qkv_weight,
    out_weight,
    kv_pool,
    page_table,
    cache_lens,
    ffn_gain,
    route_ids,
    route_weights,
    shared_gate_up,
    shared_down,
    expert_gate_up,
    expert_down,
):
    blocks = lax.axis_size("blk")
    groups = lax.axis_size("exp")
    block_index = lax.axis_index("blk")
    model_width = hidden.shape[1] * blocks
    query_width = HEADS * HEAD_DIM
    key_width = KV_HEADS * HEAD_DIM
    group_size = HEADS // KV_HEADS
    own_rows = NEW // blocks
    full_rows = gather_blocks(hidden, 1)
    attn_in = normalize(full_rows, attn_gain)
    projected = jnp.dot(attn_in, qkv_weight, preferred_element_type=jnp.float32).astype(
        jnp.bfloat16
    )
    projected_all = gather_blocks(projected, 1)
    length = cache_lens[0]
    positions = length + jnp.arange(NEW, dtype=jnp.int32)
    fresh_keys = rotate(
        projected_all[:, query_width : query_width + key_width]
        .astype(jnp.float32)
        .reshape(NEW, KV_HEADS, HEAD_DIM),
        positions,
    ).astype(jnp.bfloat16)
    appended = jnp.concatenate(
        [fresh_keys.reshape(NEW, key_width), projected_all[:, query_width + key_width :]], axis=1
    )
    page_map = page_table[0]
    pool_pages = page_map.shape[0]
    page_index = jnp.arange(pool_pages, dtype=jnp.int32)
    logical = jnp.sum(
        jnp.where(page_map[None, :] == page_index[:, None], page_index[None, :], 0), axis=1
    )
    local_pages = kv_pool.shape[1]
    local_logical = lax.dynamic_slice_in_dim(logical, block_index * local_pages, local_pages)
    slot_offsets = jnp.arange(PAGE, dtype=jnp.int32)
    local_pos = local_logical[:, None] * PAGE + slot_offsets[None, :]
    offset = local_pos - length
    written = (offset >= 0) & (offset < NEW)
    half_dim = HEAD_DIM // 2
    frequency = rope_base ** (-(jnp.arange(half_dim).astype(jnp.float32) * 2.0 / HEAD_DIM))
    angles = positions.astype(jnp.float32)[:, None] * frequency[None, :]
    cosine = jnp.cos(angles)
    sine_vals = jnp.sin(angles)
    cosine_full = jnp.concatenate([cosine, cosine], axis=1)
    sine_signed = jnp.concatenate([-sine_vals, sine_vals], axis=1)
    payload, slot_rows = local_attention(
        projected_all,
        cosine_full,
        sine_signed,
        kv_pool[0].reshape(local_pages * PAGE, 2 * key_width),
        appended,
        offset.reshape(-1),
        positions,
        local_pos.reshape(-1),
    )
    pool_out = slot_rows.reshape(local_pages, PAGE, 2 * key_width)
    payload = payload.reshape(blocks, own_rows, query_width + 128)
    gathered = lax.all_to_all(payload, "blk", split_axis=0, concat_axis=0, tiled=True)
    own_attention = combine_attention(gathered)
    attended = jnp.dot(
        lax.all_to_all(own_attention, "blk", split_axis=0, concat_axis=0, tiled=True).reshape(NEW, query_width),
        out_weight,
        preferred_element_type=jnp.float32,
    )
    mixed_cols = (hidden.astype(jnp.float32) + attended).astype(jnp.bfloat16)
    mixed_rows = gather_blocks(mixed_cols, 1)
    ffn_in = normalize(mixed_rows, ffn_gain)
    shared_cols = shared_gate_up.shape[2]
    gate_up = jnp.dot(
        ffn_in,
        shared_gate_up.reshape(model_width, 2 * shared_cols),
        preferred_element_type=jnp.float32,
    )
    shared_act = (jax.nn.silu(gate_up[:, :shared_cols]) * gate_up[:, shared_cols:]).astype(
        jnp.bfloat16
    )
    shared_term = jnp.dot(shared_act, shared_down, preferred_element_type=jnp.float32)
    row_experts = groups // SPLIT
    expert_count = row_experts * blocks
    capacity = NEW * TOPK * 4 // (expert_count * 3)
    row_expert_ids = block_index * row_experts + jnp.arange(row_experts, dtype=jnp.int32)
    route_hits = route_ids[:, :, None] == row_expert_ids[None, None, :]
    chosen = jnp.any(route_hits, axis=1)
    route_share = jnp.sum(jnp.where(route_hits, route_weights[:, :, None], 0.0), axis=1)
    slot_rank = jnp.cumsum(chosen.astype(jnp.int32), axis=0) - 1
    slot_ids = jnp.arange(capacity, dtype=jnp.int32)
    placed = chosen.T[:, None, :] & (slot_rank.T[:, None, :] == slot_ids[None, :, None])
    selector = placed.astype(jnp.bfloat16)
    outgoing = jnp.einsum(
        "ect,td->ecd", selector, ffn_in, preferred_element_type=jnp.float32
    ).astype(jnp.bfloat16)
    outgoing = jnp.repeat(outgoing, SPLIT, axis=0)
    received = lax.all_to_all(outgoing, "exp", split_axis=0, concat_axis=0, tiled=True)
    flat_rows = received.reshape(-1, model_width)
    expert_gu = jnp.dot(flat_rows, expert_gate_up[0], preferred_element_type=jnp.float32)
    activated = (jax.nn.silu(expert_gu[:, :FF_PART]) * expert_gu[:, FF_PART:]).astype(jnp.bfloat16)
    result = jnp.dot(activated, expert_down[0], preferred_element_type=jnp.float32).astype(
        jnp.bfloat16
    )
    returned = lax.all_to_all(
        result.reshape(received.shape), "exp", split_axis=0, concat_axis=0, tiled=True
    )
    summed = jnp.sum(
        returned.reshape(row_experts, SPLIT, capacity, model_width).astype(jnp.float32), axis=1
    )
    slot_weight = jnp.sum(placed.astype(jnp.float32) * route_share.T[:, None, :], axis=2)
    slot_values = summed * slot_weight[:, :, None]
    upper_part = slot_values.astype(jnp.bfloat16)
    lower_part = (slot_values - upper_part.astype(jnp.float32)).astype(jnp.bfloat16)
    routed = jnp.einsum(
        "ect,ecd->td",
        jnp.concatenate([selector, selector], axis=1),
        jnp.concatenate([upper_part, lower_part], axis=1),
        preferred_element_type=jnp.float32,
    )
    layer_term = shared_term + routed
    summed_cols = scatter_sum_blocks(layer_term)
    hidden_out = (mixed_cols.astype(jnp.float32) + summed_cols).astype(jnp.bfloat16)
    return (hidden_out, pool_out[None])


def solution(mesh):
    placed = (
        P("exp", "blk"),
        P(),
        P(None, "blk"),
        P(None, "blk"),
        P("exp", "blk", None, None),
        P("exp", None),
        P("exp"),
        P(),
        P("exp", None),
        P("exp", None),
        P(None, None, "blk"),
        P("blk", None),
        P(("blk", "exp"), None, None),
        P(("blk", "exp"), None, None),
    )
    return jax.shard_map(
        per_device,
        mesh=mesh,
        in_specs=placed,
        out_specs=(P("exp", "blk"), P("exp", "blk", None, None)),
        check_vma=False,
    )
```
